32 devices in a mesh: member: 1, lat: 32 (over z, y, x, core).
Axes of the slice: x: 2, y: 2, z: 4, core: 2. Of those that a mesh axis runs over, the one named last changes fastest.
Arguments:
- spectral: bfloat16 [512, 512, 256], P(('member', 'lat')), may hold values from -6 to 6
- lat_basis: bfloat16 [512, 512, 192], P('lat'), may hold values from -0.0078125 to 0.0078125
- block_order: int32 [128], replicated, may hold values from 0 to 127, each once
- in_weight: bfloat16 [128, 1024], replicated, may hold values from -0.5 to 0.5
- in_bias: float32 [1024], replicated, may hold values from -3 to 3
- out_weight: bfloat16 [1024, 128], replicated, may hold values from -0.1875 to 0.1875
- col_gain: float32 [128], replicated, may hold values from 0.5 to 2
- damping: float32 [128], replicated, may hold values from 0.2 to 2
Outputs:
- tendency: float32 [512, 512, 256], P(('member', 'lat'))
The draws below stay inside these ranges and needn't reach their ends.
Inputs may be any that keep to these rules, and one draw needn't show every extreme that they name: `block_order`: each wavenumber block appears exactly once.
All inputs are finite; a program needn't handle non-finite values.
Results may differ from the reference program's by a relative error of at most 0.004.
The reference program's roundings to bfloat16 on the way count: a program that leaves them out, or rounds other values in their place, can miss the bound.
Values may be sent and summed in bfloat16 or wider, within the bound.
No kernel may reach another device: no remote copies, remote signals or barrier semaphores. Data moves between devices by JAX's collectives and lax.ppermute only.
A program may use at most 128 MiB of HBM per device.

```python
import math
import jax
import jax.numpy as jnp
from jax import lax

NM = 512
NN = 512
NLAT = 384
NLON = 1536
CHAN = 128
HID = 1024
MB = 4
NBLK = 128
HALF = 192


def block_levels(key, shape, cuts, low, top_value):
    def one(axis_at, blocks):
        steps = jax.random.uniform(jax.random.fold_in(jax.random.fold_in(key, 6), axis_at), (blocks,), jnp.float32, low / len(cuts), top_value / len(cuts))
        return jnp.repeat(jnp.exp(steps), shape[axis_at] // blocks).reshape((-1,) + (1,) * (len(shape) - axis_at - 1))

    factor_of = one(*cuts[0])
    for cut in cuts[1:]:
        factor_of = factor_of * one(*cut)
    return factor_of


def centred(rng, shape, deviation, reach, cuts=(), kind=jnp.bfloat16):
    level = block_levels(rng, shape, cuts, -0.22, 0.18) if cuts else 1.0
    values = jax.random.normal(rng, shape, jnp.float32) * deviation * level
    return jnp.minimum(jnp.maximum(values, -reach), reach).astype(kind)


def setup_inputs(seed: int = 0, part: int = 0) -> dict:
    seeds = jax.random.split(jax.random.key(seed), 9)
    part_splits = jax.random.split(jax.random.fold_in(seeds[8], part), 9)
    spectral = centred(part_splits[0], (NM, NN, 2 * CHAN), 1.0, 6.0, ((0, 32),))
    lat_basis = centred(seeds[1], (NM, NN, HALF), (2 * NN * NM) ** -0.5, 0.0078125, ((0, 32),))
    block_order = jax.random.permutation(seeds[2], NBLK).astype(jnp.int32)
    in_weight = centred(seeds[3], (CHAN, HID), CHAN ** -0.5, 0.5)
    in_bias = centred(seeds[4], (HID,), 0.5, 3.0, (), jnp.float32)
    out_weight = centred(seeds[5], (HID, CHAN), HID ** -0.5, 0.1875)
    col_gain = jnp.clip(jnp.exp(jax.random.uniform(seeds[6], (CHAN,), jnp.float32, math.log(0.5), math.log(2.0))), 0.5, 2.0)
    damping = jnp.clip(jnp.exp(jax.random.uniform(seeds[7], (CHAN,), jnp.float32, math.log(0.2), math.log(2.0))), 0.2, 2.0)
    return dict(spectral=spectral, lat_basis=lat_basis, block_order=block_order, in_weight=in_weight, in_bias=in_bias, out_weight=out_weight, col_gain=col_gain, damping=damping)


def wavenumbers(block_order, slot_count):
    slot_ids = jnp.arange(slot_count, dtype=jnp.int32)
    blocks = block_order.shape[0]
    matches = (slot_ids // MB)[:, None] == jnp.arange(blocks, dtype=jnp.int32)[None, :]
    chosen = lax.optimization_barrier(jnp.sum(jnp.where(matches, block_order[None, :], 0), axis=1)).astype(jnp.int32)
    return chosen * MB + slot_ids % MB

def lon_table(wave_all):
    longitude = jnp.arange(NLON, dtype=jnp.int32)
    phase_index = wave_all[:, None] * longitude[None, :] % NLON
    angles = phase_index.astype(jnp.float32) * (2.0 * math.pi / NLON)
    return jnp.concatenate([jnp.cos(angles), jnp.sin(angles)], axis=0).astype(jnp.bfloat16)

def lat_weights(first_lat, lat_count):
    latitude = (first_lat + jnp.arange(lat_count, dtype=jnp.int32)).astype(jnp.float32)
    return jnp.cos(math.pi * ((latitude + 0.5) / NLAT - 0.5))

def reference(spectral, lat_basis, block_order, in_weight, in_bias, out_weight, col_gain, damping):
    wave_all = wavenumbers(block_order, NM)
    degree = jnp.arange(NN, dtype=jnp.int32)
    inside = degree[None, :] >= wave_all[:, None]
    parity = jnp.where((degree[None, :] + wave_all[:, None]) % 2 == 0, 1.0, -1.0).astype(jnp.float32)
    masked = jnp.where(inside[:, :, None], spectral, jnp.zeros_like(spectral))
    flipped = jnp.where(parity[:, :, None] > 0, masked, -masked)
    basis_wide = lat_basis.astype(jnp.float32)
    north_half = jnp.einsum('rnj,rnc->jrc', basis_wide, masked.astype(jnp.float32))
    south_half = jnp.einsum('rnj,rnc->jrc', basis_wide, flipped.astype(jnp.float32))
    fourier = jnp.concatenate([north_half, south_half[::-1]], axis=0).astype(jnp.bfloat16)
    wave_table = lon_table(wave_all)
    signed = jnp.concatenate([fourier[:, :, :CHAN], -fourier[:, :, CHAN:]], axis=1)
    grid_field = jnp.einsum('jrk,rl->jkl', signed.astype(jnp.float32), wave_table.astype(jnp.float32)).astype(jnp.bfloat16)
    weight_all = lat_weights(0, NLAT)
    grid_wide = grid_field.astype(jnp.float32)
    sum_squares = lax.optimization_barrier(jnp.sum(weight_all[:, None, None] * grid_wide * grid_wide, axis=(0, 2)))
    variance = sum_squares / (NLON * jnp.sum(weight_all))
    col_scale = col_gain * lax.rsqrt(variance + 1e-05)
    inv_root = 1.0 / math.sqrt(NLON)

    def column(row_grid):
        normed = (row_grid.astype(jnp.float32) * col_scale[:, None]).astype(jnp.bfloat16)
        hidden = jax.nn.gelu(jnp.dot(in_weight.T, normed, preferred_element_type=jnp.float32) + in_bias[:, None]).astype(jnp.bfloat16)
        column_out = jnp.dot(out_weight.T, hidden, preferred_element_type=jnp.float32).astype(jnp.bfloat16)
        back_proj = jnp.dot(wave_table, column_out.T, preferred_element_type=jnp.float32)
        return (jnp.concatenate([back_proj[:NM], -back_proj[NM:]], axis=1) * inv_root).astype(jnp.bfloat16)
    coeffs = lax.map(column, grid_field)
    weighted = (weight_all[:, None, None] * coeffs.astype(jnp.float32)).astype(jnp.bfloat16)
    north_part = weighted[:HALF].astype(jnp.float32)
    south_part = weighted[HALF:][::-1].astype(jnp.float32)
    east_sum = jnp.einsum('rnj,jrc->rnc', basis_wide, north_part)
    west_sum = jnp.einsum('rnj,jrc->rnc', basis_wide, south_part)
    factor = 2.0 * math.sqrt(NN * NM / NLAT)
    legendre = factor * (east_sum + parity[:, :, None] * west_sum)
    damp_all = jnp.concatenate([damping, damping])
    wave_factor = (degree * (degree + 1)).astype(jnp.float32) / (NN * NN)
    damped = legendre - damp_all[None, None, :] * wave_factor[None, :, None] * spectral.astype(jnp.float32)
    return jnp.where(inside[:, :, None], damped, jnp.zeros_like(damped))
```

```python
import functools
import math

import jax
import jax.numpy as jnp
from jax import lax
from jax.experimental import pallas as pl
from jax.experimental.pallas import tpu as pltpu
from jax.sharding import PartitionSpec as P

NN = 512
NLON = 1536
MB = 4
LON_TILE = 512


def wavenumbers(block_order, slot_count):
    slot_ids = jnp.arange(slot_count, dtype=jnp.int32)
    blocks = block_order.shape[0]
    matches = (slot_ids // MB)[:, None] == jnp.arange(blocks, dtype=jnp.int32)[None, :]
    chosen = jnp.sum(jnp.where(matches, block_order[None, :], 0), axis=1)
    return chosen * MB + slot_ids % MB


def lon_table(wave_all):
    longitude = jnp.arange(NLON, dtype=jnp.int32)
    phase_index = wave_all[:, None] * longitude[None, :] % NLON
    angles = phase_index.astype(jnp.float32) * (2.0 * math.pi / NLON)
    return jnp.concatenate([jnp.cos(angles), jnp.sin(angles)], axis=0).astype(jnp.bfloat16)


def lat_weights_of(latitude_index, lat_total):
    latitude = latitude_index.astype(jnp.float32)
    return jnp.cos(math.pi * ((latitude + 0.5) / lat_total - 0.5))


def column_kernel(weight_ref, grid_ref, scale_ref, in_t_ref, bias_ref, out_t_ref, table_ref, o_ref):
    j = pl.program_id(0)
    chan = grid_ref.shape[1]
    waves = table_ref.shape[0] // 2
    scale = scale_ref[...]
    acc = jnp.zeros((2 * waves, chan), jnp.float32)
    for c in range(NLON // LON_TILE):
        lo = c * LON_TILE
        g = grid_ref[0, :, lo:lo + LON_TILE].astype(jnp.float32)
        normed = (g * scale).astype(jnp.bfloat16)
        pre = jnp.dot(in_t_ref[...], normed, preferred_element_type=jnp.float32) + bias_ref[...]
        hidden = jax.nn.gelu(pre).astype(jnp.bfloat16)
        col = jnp.dot(out_t_ref[...], hidden, preferred_element_type=jnp.float32).astype(
            jnp.bfloat16
        )
        acc = acc + lax.dot_general(
            table_ref[:, lo:lo + LON_TILE],
            col,
            (((1,), (1,)), ((), ())),
            preferred_element_type=jnp.float32,
        )
    inv_root = 1.0 / math.sqrt(NLON)
    w = weight_ref[j]
    cos_part = (acc[:waves] * inv_root).astype(jnp.bfloat16).astype(jnp.float32)
    sin_part = ((-acc[waves:]) * inv_root).astype(jnp.bfloat16).astype(jnp.float32)
    o_ref[0, :, :chan] = (w * cos_part).astype(jnp.bfloat16)
    o_ref[0, :, chan:] = (w * sin_part).astype(jnp.bfloat16)


def column_network(lat_w, grid_field, col_scale, in_weight, in_bias, out_weight, wave_table):
    lat_local, chan, nlon = grid_field.shape
    hid = in_weight.shape[1]
    two_waves = wave_table.shape[0]
    full = lambda shape: pl.BlockSpec(shape, lambda j: (0,) * len(shape))
    return pl.pallas_call(
        column_kernel,
        grid=(lat_local,),
        in_specs=[
            pl.BlockSpec(memory_space=pltpu.SMEM),
            pl.BlockSpec((1, chan, nlon), lambda j: (j, 0, 0)),
            full((chan, 1)),
            full((hid, chan)),
            full((hid, 1)),
            full((chan, hid)),
            full((two_waves, nlon)),
        ],
        out_specs=pl.BlockSpec((1, two_waves // 2, 2 * chan), lambda j: (j, 0, 0)),
        out_shape=jax.ShapeDtypeStruct((lat_local, two_waves // 2, 2 * chan), jnp.bfloat16),
        compiler_params=pltpu.CompilerParams(vmem_limit_bytes=48 * 1024 * 1024),
    )(
        lat_w,
        grid_field,
        col_scale[:, None],
        in_weight.T,
        in_bias[:, None],
        out_weight.T,
        wave_table,
    )


def on_device(spectral, lat_basis, block_order, in_weight, in_bias, out_weight, col_gain, damping):
    devices = lax.axis_size("lat")
    my_index = lax.axis_index("lat")
    row_count = spectral.shape[0]
    degrees = spectral.shape[1]
    chan_width = spectral.shape[2]
    chan_count = chan_width // 2
    half_lat = lat_basis.shape[2]
    lat_total = 2 * half_lat
    lat_local = lat_total // devices
    wave_total = row_count * devices
    wave_all = wavenumbers(block_order, wave_total)
    wave_own = lax.dynamic_slice_in_dim(wave_all, my_index * row_count, row_count)
    degree = jnp.arange(degrees, dtype=jnp.int32)
    inside = degree[None, :] >= wave_own[:, None]
    parity = jnp.where((degree[None, :] + wave_own[:, None]) % 2 == 0, 1.0, -1.0).astype(
        jnp.float32
    )
    masked = jnp.where(inside[:, :, None], spectral, jnp.zeros_like(spectral))
    flipped = jnp.where(parity[:, :, None] > 0, masked, -masked)
    both = jnp.stack([masked, flipped], axis=0)
    fourier = jnp.einsum(
        "rnj,srnc->sjrc", lat_basis, both, preferred_element_type=jnp.float32
    ).astype(jnp.bfloat16)
    outbound = fourier.reshape(devices, lat_local, row_count, chan_width)
    wave_table = lon_table(wave_all)
    rows_in = lax.all_to_all(outbound, "lat", split_axis=0, concat_axis=2, tiled=True)[0]
    signed = jnp.concatenate([rows_in[:, :, :chan_count], -rows_in[:, :, chan_count:]], axis=1)
    grid_field = jnp.einsum(
        "jrk,rl->jkl", signed, wave_table, preferred_element_type=jnp.float32
    ).astype(jnp.bfloat16)
    row_ids = my_index * lat_local + jnp.arange(lat_local, dtype=jnp.int32)
    lat_ids = jnp.where(row_ids < half_lat, row_ids, lat_total + half_lat - 1 - row_ids)
    weight_own = lat_weights_of(lat_ids, lat_total)
    grid_wide = grid_field.astype(jnp.float32)
    partial_value = jnp.sum(weight_own[:, None, None] * grid_wide * grid_wide, axis=(0, 2))
    global_sum = lax.psum(partial_value, "lat")
    weight_all = lat_weights_of(jnp.arange(lat_total, dtype=jnp.int32), lat_total)
    variance = global_sum / (NLON * jnp.sum(weight_all))
    col_scale = col_gain * lax.rsqrt(variance + 1e-05)
    weighted_local = column_network(
        weight_own, grid_field, col_scale, in_weight, in_bias, out_weight, wave_table
    )
    returning = weighted_local.reshape(lat_local, devices, row_count, chan_width)
    weighted = lax.all_to_all(returning, "lat", split_axis=1, concat_axis=0, tiled=True)[:, 0]
    weighted = weighted.reshape(2, half_lat, row_count, chan_width)
    factor = 2.0 * math.sqrt(degrees * wave_total / lat_total)
    sums = jnp.einsum("rnj,sjrc->srnc", lat_basis, weighted, preferred_element_type=jnp.float32)
    legendre = factor * (sums[0] + parity[:, :, None] * sums[1])
    damp_all = jnp.concatenate([damping, damping])
    wave_factor = (degree * (degree + 1)).astype(jnp.float32) / (NN * NN)
    damped = legendre - damp_all[None, None, :] * wave_factor[None, :, None] * spectral.astype(
        jnp.float32
    )
    return jnp.where(inside[:, :, None], damped, jnp.zeros_like(damped))


def solution(mesh):
    in_specs = (
        P(("member", "lat"), None, None),
        P("lat", None, None),
        P(),
        P(),
        P(),
        P(),
        P(),
        P(),
    )
    out_specs = P(("member", "lat"), None, None)
    return jax.shard_map(
        on_device, mesh=mesh, in_specs=in_specs, out_specs=out_specs, check_vma=False
    )
```

```python
import functools
import math

import jax
import jax.numpy as jnp
from jax import lax
from jax.experimental import pallas as pl
from jax.experimental.pallas import tpu as pltpu
from jax.sharding import PartitionSpec as P

NN = 512
NLON = 1536
MB = 4
LON_TILE = 512


def wavenumbers(block_order, slot_count):
    slot_ids = jnp.arange(slot_count, dtype=jnp.int32)
    blocks = block_order.shape[0]
    matches = (slot_ids // MB)[:, None] == jnp.arange(blocks, dtype=jnp.int32)[None, :]
    chosen = jnp.sum(jnp.where(matches, block_order[None, :], 0), axis=1)
    return chosen * MB + slot_ids % MB


def lon_table(wave_all):
    longitude = jnp.arange(NLON, dtype=jnp.int32)
    phase_index = wave_all[:, None] * longitude[None, :] % NLON
    angles = phase_index.astype(jnp.float32) * (2.0 * math.pi / NLON)
    return jnp.concatenate([jnp.cos(angles), jnp.sin(angles)], axis=0).astype(jnp.bfloat16)


def lat_weights_of(latitude_index, lat_total):
    latitude = latitude_index.astype(jnp.float32)
    return jnp.cos(math.pi * ((latitude + 0.5) / lat_total - 0.5))


def column_kernel(weight_ref, grid_ref, scale_ref, in_t_ref, bias_ref, out_t_ref, table_ref, o_ref):
    j = pl.program_id(0)
    chan = grid_ref.shape[1]
    waves = table_ref.shape[0] // 2
    scale = scale_ref[...]
    acc = jnp.zeros((2 * waves, chan), jnp.float32)
    for c in range(NLON // LON_TILE):
        lo = c * LON_TILE
        g = grid_ref[0, :, lo:lo + LON_TILE].astype(jnp.float32)
        normed = (g * scale).astype(jnp.bfloat16)
        pre = jnp.dot(in_t_ref[...], normed, preferred_element_type=jnp.float32) + bias_ref[...]
        hidden = jax.nn.gelu(pre).astype(jnp.bfloat16)
        col = jnp.dot(out_t_ref[...], hidden, preferred_element_type=jnp.float32).astype(
            jnp.bfloat16
        )
        acc = acc + lax.dot_general(
            table_ref[:, lo:lo + LON_TILE],
            col,
            (((1,), (1,)), ((), ())),
            preferred_element_type=jnp.float32,
        )
    inv_root = 1.0 / math.sqrt(NLON)
    w = weight_ref[j]
    cos_part = (acc[:waves] * inv_root).astype(jnp.bfloat16).astype(jnp.float32)
    sin_part = ((-acc[waves:]) * inv_root).astype(jnp.bfloat16).astype(jnp.float32)
    o_ref[0, :, :chan] = (w * cos_part).astype(jnp.bfloat16)
    o_ref[0, :, chan:] = (w * sin_part).astype(jnp.bfloat16)


def column_network(lat_w, grid_field, col_scale, in_weight, in_bias, out_weight, wave_table):
    lat_local, chan, nlon = grid_field.shape
    hid = in_weight.shape[1]
    two_waves = wave_table.shape[0]
    full = lambda shape: pl.BlockSpec(shape, lambda j: (0,) * len(shape))
    return pl.pallas_call(
        column_kernel,
        grid=(lat_local,),
        in_specs=[
            pl.BlockSpec(memory_space=pltpu.SMEM),
            pl.BlockSpec((1, chan, nlon), lambda j: (j, 0, 0)),
            full((chan, 1)),
            full((hid, chan)),
            full((hid, 1)),
            full((chan, hid)),
            full((two_waves, nlon)),
        ],
        out_specs=pl.BlockSpec((1, two_waves // 2, 2 * chan), lambda j: (j, 0, 0)),
        out_shape=jax.ShapeDtypeStruct((lat_local, two_waves // 2, 2 * chan), jnp.bfloat16),
        compiler_params=pltpu.CompilerParams(vmem_limit_bytes=48 * 1024 * 1024),
    )(
        lat_w,
        grid_field,
        col_scale[:, None],
        in_weight.T,
        in_bias[:, None],
        out_weight.T,
        wave_table,
    )


def inverse_kernel(wave_ref, basis_ref, w_ref, spec_ref, damp_ref, o_ref, *, factor):
    r = pl.program_id(0)
    m = wave_ref[r]
    basis = basis_ref[0]
    east = jnp.dot(basis, w_ref[0, 0], preferred_element_type=jnp.float32)
    west = jnp.dot(basis, w_ref[0, 1], preferred_element_type=jnp.float32)
    degrees = basis.shape[0]
    n = lax.broadcasted_iota(jnp.int32, (degrees, 1), 0)
    parity = jnp.where((n + m) % 2 == 0, 1.0, -1.0).astype(jnp.float32)
    legendre = factor * (east + parity * west)
    wave_factor = (n * (n + 1)).astype(jnp.float32) / (NN * NN)
    damped = legendre - damp_ref[...] * wave_factor * spec_ref[0].astype(jnp.float32)
    o_ref[0] = jnp.where(n >= m, damped, 0.0)


def inverse_legendre(wave_own, lat_basis, weighted, spectral, damp_all, factor):
    rows, degrees, half_lat = lat_basis.shape
    width = spectral.shape[2]
    return pl.pallas_call(
        functools.partial(inverse_kernel, factor=factor),
        grid=(rows,),
        in_specs=[
            pl.BlockSpec(memory_space=pltpu.SMEM),
            pl.BlockSpec((1, degrees, half_lat), lambda r: (r, 0, 0)),
            pl.BlockSpec((1, 2, half_lat, width), lambda r: (r, 0, 0, 0)),
            pl.BlockSpec((1, degrees, width), lambda r: (r, 0, 0)),
            pl.BlockSpec((1, width), lambda r: (0, 0)),
        ],
        out_specs=pl.BlockSpec((1, degrees, width), lambda r: (r, 0, 0)),
        out_shape=jax.ShapeDtypeStruct((rows, degrees, width), jnp.float32),
    )(wave_own, lat_basis, weighted, spectral, damp_all[None, :])


def on_device(spectral, lat_basis, block_order, in_weight, in_bias, out_weight, col_gain, damping):
    devices = lax.axis_size("lat")
    my_index = lax.axis_index("lat")
    row_count = spectral.shape[0]
    degrees = spectral.shape[1]
    chan_width = spectral.shape[2]
    chan_count = chan_width // 2
    half_lat = lat_basis.shape[2]
    lat_total = 2 * half_lat
    lat_local = lat_total // devices
    wave_total = row_count * devices
    wave_all = wavenumbers(block_order, wave_total)
    wave_own = lax.dynamic_slice_in_dim(wave_all, my_index * row_count, row_count)
    degree = jnp.arange(degrees, dtype=jnp.int32)
    inside = degree[None, :] >= wave_own[:, None]
    parity = jnp.where((degree[None, :] + wave_own[:, None]) % 2 == 0, 1.0, -1.0).astype(
        jnp.float32
    )
    masked = jnp.where(inside[:, :, None], spectral, jnp.zeros_like(spectral))
    flipped = jnp.where(parity[:, :, None] > 0, masked, -masked)
    both = jnp.stack([masked, flipped], axis=0)
    fourier = jnp.einsum(
        "rnj,srnc->sjrc", lat_basis, both, preferred_element_type=jnp.float32
    ).astype(jnp.bfloat16)
    outbound = fourier.reshape(devices, lat_local, row_count, chan_width)
    wave_table = lon_table(wave_all)
    rows_in = lax.all_to_all(outbound, "lat", split_axis=0, concat_axis=2, tiled=True)[0]
    signed = jnp.concatenate([rows_in[:, :, :chan_count], -rows_in[:, :, chan_count:]], axis=1)
    grid_field = jnp.einsum(
        "jrk,rl->jkl", signed, wave_table, preferred_element_type=jnp.float32
    ).astype(jnp.bfloat16)
    row_ids = my_index * lat_local + jnp.arange(lat_local, dtype=jnp.int32)
    lat_ids = jnp.where(row_ids < half_lat, row_ids, lat_total + half_lat - 1 - row_ids)
    weight_own = lat_weights_of(lat_ids, lat_total)
    grid_wide = grid_field.astype(jnp.float32)
    partial_value = jnp.sum(weight_own[:, None, None] * grid_wide * grid_wide, axis=(0, 2))
    gathered = lax.all_to_all(
        jnp.broadcast_to(partial_value[None], (devices, chan_count)), "lat", 0, 0, tiled=True
    )
    global_sum = jnp.sum(gathered, axis=0)
    weight_all = lat_weights_of(jnp.arange(lat_total, dtype=jnp.int32), lat_total)
    variance = global_sum / (NLON * jnp.sum(weight_all))
    col_scale = col_gain * lax.rsqrt(variance + 1e-05)
    weighted_local = column_network(
        weight_own, grid_field, col_scale, in_weight, in_bias, out_weight, wave_table
    )
    returning = weighted_local.reshape(lat_local, devices, row_count, chan_width)
    weighted = lax.all_to_all(returning, "lat", split_axis=1, concat_axis=0, tiled=True)[:, 0]
    weighted = weighted.reshape(2, half_lat, row_count, chan_width).transpose(2, 0, 1, 3)
    factor = 2.0 * math.sqrt(degrees * wave_total / lat_total)
    damp_all = jnp.concatenate([damping, damping])
    return inverse_legendre(wave_own, lat_basis, weighted, spectral, damp_all, factor)


def solution(mesh):
    in_specs = (
        P(("member", "lat"), None, None),
        P("lat", None, None),
        P(),
        P(),
        P(),
        P(),
        P(),
        P(),
    )
    out_specs = P(("member", "lat"), None, None)
    return jax.shard_map(
        on_device, mesh=mesh, in_specs=in_specs, out_specs=out_specs, check_vma=False
    )
```

```python
import functools
import math

import jax
import jax.numpy as jnp
from jax import lax
from jax.experimental import pallas as pl
from jax.experimental.pallas import tpu as pltpu
from jax.sharding import PartitionSpec as P

NN = 512
NLON = 1536
MB = 4
LON_TILE = 512


def wavenumbers(block_order, slot_count):
    slot_ids = jnp.arange(slot_count, dtype=jnp.int32)
    blocks = block_order.shape[0]
    matches = (slot_ids // MB)[:, None] == jnp.arange(blocks, dtype=jnp.int32)[None, :]
    chosen = jnp.sum(jnp.where(matches, block_order[None, :], 0), axis=1)
    return chosen * MB + slot_ids % MB


def lon_table(wave_all):
    longitude = jnp.arange(NLON, dtype=jnp.int32)
    phase_index = wave_all[:, None] * longitude[None, :] % NLON
    angles = phase_index.astype(jnp.float32) * (2.0 * math.pi / NLON)
    return jnp.concatenate([jnp.cos(angles), jnp.sin(angles)], axis=0).astype(jnp.bfloat16)


def lat_weights_of(latitude_index, lat_total):
    latitude = latitude_index.astype(jnp.float32)
    return jnp.cos(math.pi * ((latitude + 0.5) / lat_total - 0.5))


def column_kernel(weight_ref, grid_ref, scale_ref, in_t_ref, bias_ref, out_t_ref, table_ref, o_ref):
    j = pl.program_id(0)
    chan = grid_ref.shape[1]
    waves = table_ref.shape[0] // 2
    scale = scale_ref[...]
    acc = jnp.zeros((2 * waves, chan), jnp.float32)
    for c in range(NLON // LON_TILE):
        lo = c * LON_TILE
        g = grid_ref[0, :, lo:lo + LON_TILE].astype(jnp.float32)
        normed = (g * scale).astype(jnp.bfloat16)
        pre = jnp.dot(in_t_ref[...], normed, preferred_element_type=jnp.float32) + bias_ref[...]
        hidden = jax.nn.gelu(pre).astype(jnp.bfloat16)
        col = jnp.dot(out_t_ref[...], hidden, preferred_element_type=jnp.float32).astype(
            jnp.bfloat16
        )
        acc = acc + lax.dot_general(
            table_ref[:, lo:lo + LON_TILE],
            col,
            (((1,), (1,)), ((), ())),
            preferred_element_type=jnp.float32,
        )
    inv_root = 1.0 / math.sqrt(NLON)
    w = weight_ref[j]
    cos_part = (acc[:waves] * inv_root).astype(jnp.bfloat16).astype(jnp.float32)
    sin_part = ((-acc[waves:]) * inv_root).astype(jnp.bfloat16).astype(jnp.float32)
    o_ref[0, :, :chan] = (w * cos_part).astype(jnp.bfloat16)
    o_ref[0, :, chan:] = (w * sin_part).astype(jnp.bfloat16)


def column_network(lat_w, grid_field, col_scale, in_weight, in_bias, out_weight, wave_table):
    lat_local, chan, nlon = grid_field.shape
    hid = in_weight.shape[1]
    two_waves = wave_table.shape[0]
    full = lambda shape: pl.BlockSpec(shape, lambda j: (0,) * len(shape))
    return pl.pallas_call(
        column_kernel,
        grid=(lat_local,),
        in_specs=[
            pl.BlockSpec(memory_space=pltpu.SMEM),
            pl.BlockSpec((1, chan, nlon), lambda j: (j, 0, 0)),
            full((chan, 1)),
            full((hid, chan)),
            full((hid, 1)),
            full((chan, hid)),
            full((two_waves, nlon)),
        ],
        out_specs=pl.BlockSpec((1, two_waves // 2, 2 * chan), lambda j: (j, 0, 0)),
        out_shape=jax.ShapeDtypeStruct((lat_local, two_waves // 2, 2 * chan), jnp.bfloat16),
        compiler_params=pltpu.CompilerParams(vmem_limit_bytes=48 * 1024 * 1024),
        cost_estimate=pl.CostEstimate(
            flops=2 * lat_local * nlon * (2 * hid * chan + two_waves * chan),
            transcendentals=lat_local * nlon * hid,
            bytes_accessed=two_waves * nlon * 2 + lat_local * (chan * nlon * 2 + two_waves * chan * 2),
        ),
    )(
        lat_w,
        grid_field,
        col_scale[:, None],
        in_weight.T,
        in_bias[:, None],
        out_weight.T,
        wave_table,
    )


def east_kernel(basis_ref, w_ref, o_ref):
    o_ref[0] = jnp.dot(basis_ref[0], w_ref[0], preferred_element_type=jnp.float32)


def east_sum(lat_basis, north):
    rows, degrees, half_lat = lat_basis.shape
    width = north.shape[2]
    return pl.pallas_call(
        east_kernel,
        grid=(rows,),
        in_specs=[
            pl.BlockSpec((1, degrees, half_lat), lambda r: (r, 0, 0)),
            pl.BlockSpec((1, half_lat, width), lambda r: (r, 0, 0)),
        ],
        out_specs=pl.BlockSpec((1, degrees, width), lambda r: (r, 0, 0)),
        out_shape=jax.ShapeDtypeStruct((rows, degrees, width), jnp.float32),
        cost_estimate=pl.CostEstimate(
            flops=2 * rows * degrees * half_lat * width,
            transcendentals=0,
            bytes_accessed=rows * (degrees * half_lat * 2 + half_lat * width * 2 + degrees * width * 4),
        ),
    )(lat_basis, north)


def inverse_kernel(wave_ref, basis_ref, w_ref, east_ref, spec_ref, damp_ref, o_ref, *, factor):
    r = pl.program_id(0)
    m = wave_ref[r]
    basis = basis_ref[0]
    west = jnp.dot(basis, w_ref[0], preferred_element_type=jnp.float32)
    degrees = basis.shape[0]
    n = lax.broadcasted_iota(jnp.int32, (degrees, 1), 0)
    parity = jnp.where((n + m) % 2 == 0, 1.0, -1.0).astype(jnp.float32)
    legendre = factor * (east_ref[0] + parity * west)
    wave_factor = (n * (n + 1)).astype(jnp.float32) / (NN * NN)
    damped = legendre - damp_ref[...] * wave_factor * spec_ref[0].astype(jnp.float32)
    o_ref[0] = jnp.where(n >= m, damped, 0.0)


def inverse_legendre(wave_own, lat_basis, south, east, spectral, damp_all, factor):
    rows, degrees, half_lat = lat_basis.shape
    width = spectral.shape[2]
    return pl.pallas_call(
        functools.partial(inverse_kernel, factor=factor),
        grid=(rows,),
        in_specs=[
            pl.BlockSpec(memory_space=pltpu.SMEM),
            pl.BlockSpec((1, degrees, half_lat), lambda r: (r, 0, 0)),
            pl.BlockSpec((1, half_lat, width), lambda r: (r, 0, 0)),
            pl.BlockSpec((1, degrees, width), lambda r: (r, 0, 0)),
            pl.BlockSpec((1, degrees, width), lambda r: (r, 0, 0)),
            pl.BlockSpec((1, width), lambda r: (0, 0)),
        ],
        out_specs=pl.BlockSpec((1, degrees, width), lambda r: (r, 0, 0)),
        out_shape=jax.ShapeDtypeStruct((rows, degrees, width), jnp.float32),
        cost_estimate=pl.CostEstimate(
            flops=2 * rows * degrees * half_lat * width,
            transcendentals=0,
            bytes_accessed=rows * (degrees * half_lat * 2 + half_lat * width * 2 + degrees * width * 10),
        ),
    )(wave_own, lat_basis, south, east, spectral, damp_all[None, :])


def on_device(spectral, lat_basis, block_order, in_weight, in_bias, out_weight, col_gain, damping):
    devices = lax.axis_size("lat")
    my_index = lax.axis_index("lat")
    row_count = spectral.shape[0]
    degrees = spectral.shape[1]
    chan_width = spectral.shape[2]
    chan_count = chan_width // 2
    half_lat = lat_basis.shape[2]
    lat_total = 2 * half_lat
    half_local = half_lat // devices
    wave_total = row_count * devices
    wave_all = wavenumbers(block_order, wave_total)
    wave_own = lax.dynamic_slice_in_dim(wave_all, my_index * row_count, row_count)
    degree = jnp.arange(degrees, dtype=jnp.int32)
    inside = degree[None, :] >= wave_own[:, None]
    parity = jnp.where((degree[None, :] + wave_own[:, None]) % 2 == 0, 1.0, -1.0).astype(
        jnp.float32
    )
    masked = jnp.where(inside[:, :, None], spectral, jnp.zeros_like(spectral))
    flipped = jnp.where(parity[:, :, None] > 0, masked, -masked)
    wave_table = lon_table(wave_all)

    def to_grid(values):
        fourier = jnp.einsum(
            "rnj,rnc->jrc", lat_basis, values, preferred_element_type=jnp.float32
        ).astype(jnp.bfloat16)
        outbound = fourier.reshape(devices, half_local, row_count, chan_width)
        rows_in = lax.all_to_all(outbound, "lat", split_axis=0, concat_axis=2, tiled=True)[0]
        signed = jnp.concatenate(
            [rows_in[:, :, :chan_count], -rows_in[:, :, chan_count:]], axis=1
        )
        return jnp.einsum(
            "jrk,rl->jkl", signed, wave_table, preferred_element_type=jnp.float32
        ).astype(jnp.bfloat16)

    grid_north = to_grid(masked)
    grid_south = to_grid(flipped)
    j_ids = my_index * half_local + jnp.arange(half_local, dtype=jnp.int32)
    weight_north = lat_weights_of(j_ids, lat_total)
    weight_south = lat_weights_of(lat_total - 1 - j_ids, lat_total)

    def sum_squares(grid_field, weight):
        grid_wide = grid_field.astype(jnp.float32)
        return jnp.sum(weight[:, None, None] * grid_wide * grid_wide, axis=(0, 2))

    partial_value = sum_squares(grid_north, weight_north) + sum_squares(grid_south, weight_south)
    gathered = lax.all_to_all(
        jnp.broadcast_to(partial_value[None], (devices, chan_count)), "lat", 0, 0, tiled=True
    )
    global_sum = jnp.sum(gathered, axis=0)
    weight_all = lat_weights_of(jnp.arange(lat_total, dtype=jnp.int32), lat_total)
    variance = global_sum / (NLON * jnp.sum(weight_all))
    col_scale = col_gain * lax.rsqrt(variance + 1e-05)

    def to_spectral(grid_field, weight):
        weighted_local = column_network(
            weight, grid_field, col_scale, in_weight, in_bias, out_weight, wave_table
        )
        returning = weighted_local.reshape(half_local, devices, row_count, chan_width)
        weighted = lax.all_to_all(returning, "lat", split_axis=1, concat_axis=0, tiled=True)
        return weighted.reshape(half_lat, row_count, chan_width).transpose(1, 0, 2)

    north = to_spectral(grid_north, weight_north)
    south = to_spectral(grid_south, weight_south)
    east = east_sum(lat_basis, north)
    factor = 2.0 * math.sqrt(degrees * wave_total / lat_total)
    damp_all = jnp.concatenate([damping, damping])
    return inverse_legendre(wave_own, lat_basis, south, east, spectral, damp_all, factor)


def solution(mesh):
    in_specs = (
        P(("member", "lat"), None, None),
        P("lat", None, None),
        P(),
        P(),
        P(),
        P(),
        P(),
        P(),
    )
    out_specs = P(("member", "lat"), None, None)
    return jax.shard_map(
        on_device, mesh=mesh, in_specs=in_specs, out_specs=out_specs, check_vma=False
    )
```

```python
import functools
import math

import jax
import jax.numpy as jnp
from jax import lax
from jax.experimental import pallas as pl
from jax.experimental.pallas import tpu as pltpu
from jax.sharding import PartitionSpec as P

NN = 512
NLON = 1536
MB = 4
LON_TILE = 512


def wavenumbers(block_order, slot_count):
    slot_ids = jnp.arange(slot_count, dtype=jnp.int32)
    blocks = block_order.shape[0]
    matches = (slot_ids // MB)[:, None] == jnp.arange(blocks, dtype=jnp.int32)[None, :]
    chosen = jnp.sum(jnp.where(matches, block_order[None, :], 0), axis=1)
    return chosen * MB + slot_ids % MB


def lon_table(wave_all):
    longitude = jnp.arange(NLON, dtype=jnp.int32)
    phase_index = wave_all[:, None] * longitude[None, :] % NLON
    angles = phase_index.astype(jnp.float32) * (2.0 * math.pi / NLON)
    return jnp.concatenate([jnp.cos(angles), jnp.sin(angles)], axis=0).astype(jnp.bfloat16)


def lat_weights_of(latitude_index, lat_total):
    latitude = latitude_index.astype(jnp.float32)
    return jnp.cos(math.pi * ((latitude + 0.5) / lat_total - 0.5))


def column_kernel(weight_ref, grid_ref, scale_ref, in_t_ref, bias_ref, out_t_ref, table_ref, o_ref):
    j = pl.program_id(0)
    chan = grid_ref.shape[1]
    waves = table_ref.shape[0] // 2
    scale = scale_ref[...]
    acc = jnp.zeros((2 * waves, chan), jnp.float32)
    for c in range(NLON // LON_TILE):
        lo = c * LON_TILE
        g = grid_ref[0, :, lo:lo + LON_TILE].astype(jnp.float32)
        normed = (g * scale).astype(jnp.bfloat16)
        pre = jnp.dot(in_t_ref[...], normed, preferred_element_type=jnp.float32) + bias_ref[...]
        hidden = jax.nn.gelu(pre).astype(jnp.bfloat16)
        col = jnp.dot(out_t_ref[...], hidden, preferred_element_type=jnp.float32).astype(
            jnp.bfloat16
        )
        acc = acc + lax.dot_general(
            table_ref[:, lo:lo + LON_TILE],
            col,
            (((1,), (1,)), ((), ())),
            preferred_element_type=jnp.float32,
        )
    inv_root = 1.0 / math.sqrt(NLON)
    w = weight_ref[j]
    cos_part = (acc[:waves] * inv_root).astype(jnp.bfloat16).astype(jnp.float32)
    sin_part = ((-acc[waves:]) * inv_root).astype(jnp.bfloat16).astype(jnp.float32)
    o_ref[0, :, :chan] = (w * cos_part).astype(jnp.bfloat16)
    o_ref[0, :, chan:] = (w * sin_part).astype(jnp.bfloat16)


def column_network(lat_w, grid_field, col_scale, in_weight, in_bias, out_weight, wave_table):
    lat_local, chan, nlon = grid_field.shape
    hid = in_weight.shape[1]
    two_waves = wave_table.shape[0]
    full = lambda shape: pl.BlockSpec(shape, lambda j: (0,) * len(shape))
    return pl.pallas_call(
        column_kernel,
        grid=(lat_local,),
        in_specs=[
            pl.BlockSpec(memory_space=pltpu.SMEM),
            pl.BlockSpec((1, chan, nlon), lambda j: (j, 0, 0)),
            full((chan, 1)),
            full((hid, chan)),
            full((hid, 1)),
            full((chan, hid)),
            full((two_waves, nlon)),
        ],
        out_specs=pl.BlockSpec((1, two_waves // 2, 2 * chan), lambda j: (j, 0, 0)),
        out_shape=jax.ShapeDtypeStruct((lat_local, two_waves // 2, 2 * chan), jnp.bfloat16),
        compiler_params=pltpu.CompilerParams(vmem_limit_bytes=48 * 1024 * 1024),
        cost_estimate=pl.CostEstimate(
            flops=2 * lat_local * nlon * (2 * hid * chan + two_waves * chan),
            transcendentals=lat_local * nlon * hid,
            bytes_accessed=two_waves * nlon * 2 + lat_local * (chan * nlon * 2 + two_waves * chan * 2),
        ),
    )(
        lat_w,
        grid_field,
        col_scale[:, None],
        in_weight.T,
        in_bias[:, None],
        out_weight.T,
        wave_table,
    )


def inverse_kernel(wave_ref, basis_ref, north_ref, south_ref, spec_ref, damp_ref, o_ref, *, factor):
    block = basis_ref.shape[0]
    degrees = basis_ref.shape[1]
    n = lax.broadcasted_iota(jnp.int32, (degrees, 1), 0)
    wave_factor = (n * (n + 1)).astype(jnp.float32) / (NN * NN)
    for b in range(block):
        m = wave_ref[pl.program_id(0) * block + b]
        basis = basis_ref[b]
        east = jnp.dot(basis, north_ref[b], preferred_element_type=jnp.float32)
        west = jnp.dot(basis, south_ref[b], preferred_element_type=jnp.float32)
        parity = jnp.where((n + m) % 2 == 0, 1.0, -1.0).astype(jnp.float32)
        legendre = factor * (east + parity * west)
        damped = legendre - damp_ref[...] * wave_factor * spec_ref[b].astype(jnp.float32)
        o_ref[b] = jnp.where(n >= m, damped, 0.0)


def inverse_legendre(wave_own, lat_basis, north, south, spectral, damp_all, factor):
    rows, degrees, half_lat = lat_basis.shape
    width = spectral.shape[2]
    block = 4 if rows % 4 == 0 else 1
    three = lambda shape: pl.BlockSpec(shape, lambda r: (r, 0, 0))
    return pl.pallas_call(
        functools.partial(inverse_kernel, factor=factor),
        grid=(rows // block,),
        in_specs=[
            pl.BlockSpec(memory_space=pltpu.SMEM),
            three((block, degrees, half_lat)),
            three((block, half_lat, width)),
            three((block, half_lat, width)),
            three((block, degrees, width)),
            pl.BlockSpec((1, width), lambda r: (0, 0)),
        ],
        out_specs=three((block, degrees, width)),
        out_shape=jax.ShapeDtypeStruct((rows, degrees, width), jnp.float32),
        cost_estimate=pl.CostEstimate(
            flops=4 * rows * degrees * half_lat * width,
            transcendentals=0,
            bytes_accessed=rows * (degrees * half_lat * 2 + half_lat * width * 4 + degrees * width * 6),
        ),
    )(wave_own, lat_basis, north, south, spectral, damp_all[None, :])


def on_device(spectral, lat_basis, block_order, in_weight, in_bias, out_weight, col_gain, damping):
    devices = lax.axis_size("lat")
    my_index = lax.axis_index("lat")
    row_count = spectral.shape[0]
    degrees = spectral.shape[1]
    chan_width = spectral.shape[2]
    chan_count = chan_width // 2
    half_lat = lat_basis.shape[2]
    lat_total = 2 * half_lat
    half_local = half_lat // devices
    wave_total = row_count * devices
    wave_all = wavenumbers(block_order, wave_total)
    wave_own = lax.dynamic_slice_in_dim(wave_all, my_index * row_count, row_count)
    degree = jnp.arange(degrees, dtype=jnp.int32)
    inside = degree[None, :] >= wave_own[:, None]
    parity = jnp.where((degree[None, :] + wave_own[:, None]) % 2 == 0, 1.0, -1.0).astype(
        jnp.float32
    )
    masked = jnp.where(inside[:, :, None], spectral, jnp.zeros_like(spectral))
    flipped = jnp.where(parity[:, :, None] > 0, masked, -masked)
    wave_table = lon_table(wave_all)

    both = jnp.stack([masked, flipped], axis=0)
    fourier = jnp.einsum(
        "rnj,srnc->sjrc", lat_basis, both, preferred_element_type=jnp.float32
    ).astype(jnp.bfloat16)
    outbound = fourier.reshape(2, devices, half_local, row_count, chan_width).transpose(
        1, 0, 2, 3, 4
    ).reshape(devices, 2 * half_local, row_count, chan_width)
    rows_in = lax.all_to_all(outbound, "lat", split_axis=0, concat_axis=2, tiled=True)[0]
    signed = jnp.concatenate([rows_in[:, :, :chan_count], -rows_in[:, :, chan_count:]], axis=1)
    grid_field = jnp.einsum(
        "jrk,rl->jkl", signed, wave_table, preferred_element_type=jnp.float32
    ).astype(jnp.bfloat16)
    grid_north = grid_field[:half_local]
    grid_south = grid_field[half_local:]
    j_ids = my_index * half_local + jnp.arange(half_local, dtype=jnp.int32)
    weight_north = lat_weights_of(j_ids, lat_total)
    weight_south = lat_weights_of(lat_total - 1 - j_ids, lat_total)

    def sum_squares(grid_field, weight):
        grid_wide = grid_field.astype(jnp.float32)
        return jnp.sum(weight[:, None, None] * grid_wide * grid_wide, axis=(0, 2))

    partial_value = sum_squares(grid_north, weight_north) + sum_squares(grid_south, weight_south)
    gathered = lax.all_to_all(
        jnp.broadcast_to(partial_value[None], (devices, chan_count)), "lat", 0, 0, tiled=True
    )
    global_sum = jnp.sum(gathered, axis=0)
    weight_all = lat_weights_of(jnp.arange(lat_total, dtype=jnp.int32), lat_total)
    variance = global_sum / (NLON * jnp.sum(weight_all))
    col_scale = col_gain * lax.rsqrt(variance + 1e-05)

    def to_spectral(grid_field, weight):
        weighted_local = column_network(
            weight, grid_field, col_scale, in_weight, in_bias, out_weight, wave_table
        )
        returning = weighted_local.reshape(half_local, devices, row_count, chan_width)
        weighted = lax.all_to_all(returning, "lat", split_axis=1, concat_axis=0, tiled=True)
        return weighted.reshape(half_lat, row_count, chan_width).transpose(1, 0, 2)

    north = to_spectral(grid_north, weight_north)
    south = to_spectral(grid_south, weight_south)
    factor = 2.0 * math.sqrt(degrees * wave_total / lat_total)
    damp_all = jnp.concatenate([damping, damping])
    return inverse_legendre(wave_own, lat_basis, north, south, spectral, damp_all, factor)


def solution(mesh):
    in_specs = (
        P(("member", "lat"), None, None),
        P("lat", None, None),
        P(),
        P(),
        P(),
        P(),
        P(),
        P(),
    )
    out_specs = P(("member", "lat"), None, None)
    return jax.shard_map(
        on_device, mesh=mesh, in_specs=in_specs, out_specs=out_specs, check_vma=False
    )
```

```python
import functools
import math

import jax
import jax.numpy as jnp
from jax import lax
from jax.experimental import pallas as pl
from jax.experimental.pallas import tpu as pltpu
from jax.sharding import PartitionSpec as P

NN = 512
NLON = 1536
MB = 4
LON_TILE = 512


def wavenumbers(block_order, slot_count):
    slot_ids = jnp.arange(slot_count, dtype=jnp.int32)
    blocks = block_order.shape[0]
    matches = (slot_ids // MB)[:, None] == jnp.arange(blocks, dtype=jnp.int32)[None, :]
    chosen = jnp.sum(jnp.where(matches, block_order[None, :], 0), axis=1)
    return chosen * MB + slot_ids % MB


def lon_table(wave_all):
    longitude = jnp.arange(NLON, dtype=jnp.int32)
    phase_index = wave_all[:, None] * longitude[None, :] % NLON
    angles = phase_index.astype(jnp.float32) * (2.0 * math.pi / NLON)
    return jnp.concatenate([jnp.cos(angles), jnp.sin(angles)], axis=0).astype(jnp.bfloat16)


def lat_weights_of(latitude_index, lat_total):
    latitude = latitude_index.astype(jnp.float32)
    return jnp.cos(math.pi * ((latitude + 0.5) / lat_total - 0.5))


def grid_kernel(weight_ref, rows_ref, cos_t_ref, sin_t_ref, grid_ref, ssq_ref):
    j = pl.program_id(0)
    chan = grid_ref.shape[2]
    rows = rows_ref[0]
    wide = jnp.dot(cos_t_ref[...], rows[:, :chan], preferred_element_type=jnp.float32)
    wide = wide + jnp.dot(sin_t_ref[...], rows[:, chan:], preferred_element_type=jnp.float32)
    grid = wide.astype(jnp.bfloat16)
    grid_ref[0] = grid
    g = grid.astype(jnp.float32)
    part = weight_ref[j] * jnp.sum(g * g, axis=0, keepdims=True)

    @pl.when(j == 0)
    def _():
        ssq_ref[...] = part

    @pl.when(j > 0)
    def _():
        ssq_ref[...] = ssq_ref[...] + part


def grid_synthesis(lat_w, rows_in, cos_t, neg_sin_t):
    lat_local, waves, width = rows_in.shape
    chan = width // 2
    nlon = cos_t.shape[0]
    return pl.pallas_call(
        grid_kernel,
        grid=(lat_local,),
        in_specs=[
            pl.BlockSpec(memory_space=pltpu.SMEM),
            pl.BlockSpec((1, waves, width), lambda j: (j, 0, 0)),
            pl.BlockSpec((nlon, waves), lambda j: (0, 0)),
            pl.BlockSpec((nlon, waves), lambda j: (0, 0)),
        ],
        out_specs=[
            pl.BlockSpec((1, nlon, chan), lambda j: (j, 0, 0)),
            pl.BlockSpec((1, chan), lambda j: (0, 0)),
        ],
        out_shape=[
            jax.ShapeDtypeStruct((lat_local, nlon, chan), jnp.bfloat16),
            jax.ShapeDtypeStruct((1, chan), jnp.float32),
        ],
        compiler_params=pltpu.CompilerParams(vmem_limit_bytes=48 * 1024 * 1024),
        cost_estimate=pl.CostEstimate(
            flops=2 * lat_local * nlon * waves * width,
            transcendentals=0,
            bytes_accessed=4 * nlon * waves + lat_local * (waves * width * 2 + nlon * chan * 2),
        ),
    )(lat_w, rows_in, cos_t, neg_sin_t)


def column_kernel(weight_ref, grid_ref, scale_ref, in_w_ref, bias_ref, out_w_ref, table_ref, o_ref):
    j = pl.program_id(0)
    chan = grid_ref.shape[2]
    waves = table_ref.shape[0] // 2
    scale = scale_ref[...]
    acc = jnp.zeros((2 * waves, chan), jnp.float32)
    for c in range(NLON // LON_TILE):
        lo = c * LON_TILE
        g = grid_ref[0, lo:lo + LON_TILE, :].astype(jnp.float32)
        normed = (g * scale).astype(jnp.bfloat16)
        pre = jnp.dot(normed, in_w_ref[...], preferred_element_type=jnp.float32) + bias_ref[...]
        hidden = jax.nn.gelu(pre).astype(jnp.bfloat16)
        col = jnp.dot(hidden, out_w_ref[...], preferred_element_type=jnp.float32).astype(
            jnp.bfloat16
        )
        acc = acc + jnp.dot(
            table_ref[:, lo:lo + LON_TILE], col, preferred_element_type=jnp.float32
        )
    inv_root = 1.0 / math.sqrt(NLON)
    w = weight_ref[j]
    cos_part = (acc[:waves] * inv_root).astype(jnp.bfloat16).astype(jnp.float32)
    sin_part = ((-acc[waves:]) * inv_root).astype(jnp.bfloat16).astype(jnp.float32)
    o_ref[0, :, :chan] = (w * cos_part).astype(jnp.bfloat16)
    o_ref[0, :, chan:] = (w * sin_part).astype(jnp.bfloat16)


def column_network(lat_w, grid_t, col_scale, in_weight, in_bias, out_weight, wave_table):
    lat_local, nlon, chan = grid_t.shape
    hid = in_weight.shape[1]
    two_waves = wave_table.shape[0]
    full = lambda shape: pl.BlockSpec(shape, lambda j: (0,) * len(shape))
    return pl.pallas_call(
        column_kernel,
        grid=(lat_local,),
        in_specs=[
            pl.BlockSpec(memory_space=pltpu.SMEM),
            pl.BlockSpec((1, nlon, chan), lambda j: (j, 0, 0)),
            full((1, chan)),
            full((chan, hid)),
            full((1, hid)),
            full((hid, chan)),
            full((two_waves, nlon)),
        ],
        out_specs=pl.BlockSpec((1, two_waves // 2, 2 * chan), lambda j: (j, 0, 0)),
        out_shape=jax.ShapeDtypeStruct((lat_local, two_waves // 2, 2 * chan), jnp.bfloat16),
        compiler_params=pltpu.CompilerParams(vmem_limit_bytes=48 * 1024 * 1024),
        cost_estimate=pl.CostEstimate(
            flops=2 * lat_local * nlon * (2 * hid * chan + two_waves * chan),
            transcendentals=lat_local * nlon * hid,
            bytes_accessed=two_waves * nlon * 2 + lat_local * (chan * nlon * 2 + two_waves * chan * 2),
        ),
    )(
        lat_w,
        grid_t,
        col_scale[None, :],
        in_weight,
        in_bias[None, :],
        out_weight,
        wave_table,
    )


def inverse_kernel(wave_ref, basis_ref, north_ref, south_ref, spec_ref, damp_ref, o_ref, *, factor):
    block = basis_ref.shape[0]
    degrees = basis_ref.shape[1]
    n = lax.broadcasted_iota(jnp.int32, (degrees, 1), 0)
    wave_factor = (n * (n + 1)).astype(jnp.float32) / (NN * NN)
    for b in range(block):
        m = wave_ref[pl.program_id(0) * block + b]
        basis = basis_ref[b]
        east = jnp.dot(basis, north_ref[b], preferred_element_type=jnp.float32)
        west = jnp.dot(basis, south_ref[b], preferred_element_type=jnp.float32)
        parity = jnp.where((n + m) % 2 == 0, 1.0, -1.0).astype(jnp.float32)
        legendre = factor * (east + parity * west)
        damped = legendre - damp_ref[...] * wave_factor * spec_ref[b].astype(jnp.float32)
        o_ref[b] = jnp.where(n >= m, damped, 0.0)


def inverse_legendre(wave_own, lat_basis, north, south, spectral, damp_all, factor):
    rows, degrees, half_lat = lat_basis.shape
    width = spectral.shape[2]
    block = 4 if rows % 4 == 0 else 1
    three = lambda shape: pl.BlockSpec(shape, lambda r: (r, 0, 0))
    return pl.pallas_call(
        functools.partial(inverse_kernel, factor=factor),
        grid=(rows // block,),
        in_specs=[
            pl.BlockSpec(memory_space=pltpu.SMEM),
            three((block, degrees, half_lat)),
            three((block, half_lat, width)),
            three((block, half_lat, width)),
            three((block, degrees, width)),
            pl.BlockSpec((1, width), lambda r: (0, 0)),
        ],
        out_specs=three((block, degrees, width)),
        out_shape=jax.ShapeDtypeStruct((rows, degrees, width), jnp.float32),
        cost_estimate=pl.CostEstimate(
            flops=4 * rows * degrees * half_lat * width,
            transcendentals=0,
            bytes_accessed=rows * (degrees * half_lat * 2 + half_lat * width * 4 + degrees * width * 6),
        ),
    )(wave_own, lat_basis, north, south, spectral, damp_all[None, :])


def on_device(spectral, lat_basis, block_order, in_weight, in_bias, out_weight, col_gain, damping):
    devices = lax.axis_size("lat")
    my_index = lax.axis_index("lat")
    row_count = spectral.shape[0]
    degrees = spectral.shape[1]
    chan_width = spectral.shape[2]
    chan_count = chan_width // 2
    half_lat = lat_basis.shape[2]
    lat_total = 2 * half_lat
    half_local = half_lat // devices
    wave_total = row_count * devices
    wave_all = wavenumbers(block_order, wave_total)
    wave_own = lax.dynamic_slice_in_dim(wave_all, my_index * row_count, row_count)
    degree = jnp.arange(degrees, dtype=jnp.int32)
    inside = degree[None, :] >= wave_own[:, None]
    parity = jnp.where((degree[None, :] + wave_own[:, None]) % 2 == 0, 1.0, -1.0).astype(
        jnp.float32
    )
    masked = jnp.where(inside[:, :, None], spectral, jnp.zeros_like(spectral))
    flipped = jnp.where(parity[:, :, None] > 0, masked, -masked)
    wave_table = lon_table(wave_all)

    both = jnp.stack([masked, flipped], axis=0)
    fourier = jnp.einsum(
        "rnj,srnc->sjrc", lat_basis, both, preferred_element_type=jnp.float32
    ).astype(jnp.bfloat16)
    outbound = fourier.reshape(2, devices, half_local, row_count, chan_width).transpose(
        1, 0, 2, 3, 4
    ).reshape(devices, 2 * half_local, row_count, chan_width)
    rows_in = lax.all_to_all(outbound, "lat", split_axis=0, concat_axis=2, tiled=True)[0]
    j_ids = my_index * half_local + jnp.arange(half_local, dtype=jnp.int32)
    lat_ids = jnp.concatenate([j_ids, lat_total - 1 - j_ids])
    weight_own = lat_weights_of(lat_ids, lat_total)
    cos_t = wave_table[:wave_total].T
    neg_sin_t = -wave_table[wave_total:].T
    grid_t, partial_value = grid_synthesis(weight_own, rows_in, cos_t, neg_sin_t)
    gathered = lax.all_to_all(
        jnp.broadcast_to(partial_value, (devices, chan_count)), "lat", 0, 0, tiled=True
    )
    global_sum = jnp.sum(gathered, axis=0)
    weight_all = lat_weights_of(jnp.arange(lat_total, dtype=jnp.int32), lat_total)
    variance = global_sum / (NLON * jnp.sum(weight_all))
    col_scale = col_gain * lax.rsqrt(variance + 1e-05)
    grid_north = grid_t[:half_local]
    grid_south = grid_t[half_local:]
    weight_north = weight_own[:half_local]
    weight_south = weight_own[half_local:]

    def to_spectral(grid_field, weight):
        weighted_local = column_network(
            weight, grid_field, col_scale, in_weight, in_bias, out_weight, wave_table
        )
        returning = weighted_local.reshape(half_local, devices, row_count, chan_width)
        weighted = lax.all_to_all(returning, "lat", split_axis=1, concat_axis=0, tiled=True)
        return weighted.reshape(half_lat, row_count, chan_width).transpose(1, 0, 2)

    north = to_spectral(grid_north, weight_north)
    south = to_spectral(grid_south, weight_south)
    factor = 2.0 * math.sqrt(degrees * wave_total / lat_total)
    damp_all = jnp.concatenate([damping, damping])
    return inverse_legendre(wave_own, lat_basis, north, south, spectral, damp_all, factor)


def solution(mesh):
    in_specs = (
        P(("member", "lat"), None, None),
        P("lat", None, None),
        P(),
        P(),
        P(),
        P(),
        P(),
        P(),
    )
    out_specs = P(("member", "lat"), None, None)
    return jax.shard_map(
        on_device, mesh=mesh, in_specs=in_specs, out_specs=out_specs, check_vma=False
    )
```

```python
import functools
import math

import jax
import jax.numpy as jnp
from jax import lax
from jax.experimental import pallas as pl
from jax.experimental.pallas import tpu as pltpu
from jax.sharding import PartitionSpec as P

NN = 512
NLON = 1536
MB = 4
LON_TILE = 512


def wavenumbers(block_order, slot_count):
    slot_ids = jnp.arange(slot_count, dtype=jnp.int32)
    blocks = block_order.shape[0]
    matches = (slot_ids // MB)[:, None] == jnp.arange(blocks, dtype=jnp.int32)[None, :]
    chosen = jnp.sum(jnp.where(matches, block_order[None, :], 0), axis=1)
    return chosen * MB + slot_ids % MB


def lon_table(wave_all):
    longitude = jnp.arange(NLON, dtype=jnp.int32)
    phase_index = wave_all[:, None] * longitude[None, :] % NLON
    angles = phase_index.astype(jnp.float32) * (2.0 * math.pi / NLON)
    return jnp.concatenate([jnp.cos(angles), jnp.sin(angles)], axis=0).astype(jnp.bfloat16)


def lat_weights_of(latitude_index, lat_total):
    latitude = latitude_index.astype(jnp.float32)
    return jnp.cos(math.pi * ((latitude + 0.5) / lat_total - 0.5))


def grid_kernel(weight_ref, rows_ref, cos_t_ref, sin_t_ref, grid_ref, ssq_ref):
    j = pl.program_id(0)
    chan = grid_ref.shape[2]
    sources, _, rows_per, width = rows_ref.shape
    rows = rows_ref[:, 0].astype(jnp.float32).reshape(sources * rows_per, width)
    rows = rows.astype(jnp.bfloat16)
    wide = jnp.dot(cos_t_ref[...], rows[:, :chan], preferred_element_type=jnp.float32)
    wide = wide + jnp.dot(sin_t_ref[...], rows[:, chan:], preferred_element_type=jnp.float32)
    grid = wide.astype(jnp.bfloat16)
    grid_ref[0] = grid
    g = grid.astype(jnp.float32)
    part = weight_ref[j] * jnp.sum(g * g, axis=0, keepdims=True)

    @pl.when(j == 0)
    def _():
        ssq_ref[...] = part

    @pl.when(j > 0)
    def _():
        ssq_ref[...] = ssq_ref[...] + part


def grid_synthesis(lat_w, rows_in, cos_t, neg_sin_t):
    sources, lat_local, rows_per, width = rows_in.shape
    waves = sources * rows_per
    chan = width // 2
    nlon = cos_t.shape[0]
    return pl.pallas_call(
        grid_kernel,
        grid=(lat_local,),
        in_specs=[
            pl.BlockSpec(memory_space=pltpu.SMEM),
            pl.BlockSpec((sources, 1, rows_per, width), lambda j: (0, j, 0, 0)),
            pl.BlockSpec((nlon, waves), lambda j: (0, 0)),
            pl.BlockSpec((nlon, waves), lambda j: (0, 0)),
        ],
        out_specs=[
            pl.BlockSpec((1, nlon, chan), lambda j: (j, 0, 0)),
            pl.BlockSpec((1, chan), lambda j: (0, 0)),
        ],
        out_shape=[
            jax.ShapeDtypeStruct((lat_local, nlon, chan), jnp.bfloat16),
            jax.ShapeDtypeStruct((1, chan), jnp.float32),
        ],
        compiler_params=pltpu.CompilerParams(vmem_limit_bytes=48 * 1024 * 1024),
        cost_estimate=pl.CostEstimate(
            flops=2 * lat_local * nlon * waves * width,
            transcendentals=0,
            bytes_accessed=4 * nlon * waves + lat_local * (waves * width * 2 + nlon * chan * 2),
        ),
    )(lat_w, rows_in, cos_t, neg_sin_t)


def column_kernel(
    weight_ref, grid_ref, scale_ref, in_w_ref, bias_ref, out_w_ref, table_ref, o_ref, *, first
):
    j = pl.program_id(0) + first
    chan = grid_ref.shape[2]
    waves = table_ref.shape[0] // 2
    scale = scale_ref[...]
    acc = jnp.zeros((2 * waves, chan), jnp.float32)
    for c in range(NLON // LON_TILE):
        lo = c * LON_TILE
        g = grid_ref[0, lo:lo + LON_TILE, :].astype(jnp.float32)
        normed = (g * scale).astype(jnp.bfloat16)
        pre = jnp.dot(normed, in_w_ref[...], preferred_element_type=jnp.float32) + bias_ref[...]
        hidden = jax.nn.gelu(pre).astype(jnp.bfloat16)
        col = jnp.dot(hidden, out_w_ref[...], preferred_element_type=jnp.float32).astype(
            jnp.bfloat16
        )
        acc = acc + jnp.dot(
            table_ref[:, lo:lo + LON_TILE], col, preferred_element_type=jnp.float32
        )
    inv_root = 1.0 / math.sqrt(NLON)
    w = weight_ref[j]
    cos_part = (acc[:waves] * inv_root).astype(jnp.bfloat16).astype(jnp.float32)
    sin_part = ((-acc[waves:]) * inv_root).astype(jnp.bfloat16).astype(jnp.float32)
    o_ref[0, :, :chan] = (w * cos_part).astype(jnp.bfloat16)
    o_ref[0, :, chan:] = (w * sin_part).astype(jnp.bfloat16)


def column_network(
    lat_w, grid_t, first, lat_local, col_scale, in_weight, in_bias, out_weight, wave_table
):
    nlon, chan = grid_t.shape[1:]
    hid = in_weight.shape[1]
    two_waves = wave_table.shape[0]
    full = lambda shape: pl.BlockSpec(shape, lambda j: (0,) * len(shape))
    return pl.pallas_call(
        functools.partial(column_kernel, first=first),
        grid=(lat_local,),
        in_specs=[
            pl.BlockSpec(memory_space=pltpu.SMEM),
            pl.BlockSpec((1, nlon, chan), lambda j: (j + first, 0, 0)),
            full((1, chan)),
            full((chan, hid)),
            full((1, hid)),
            full((hid, chan)),
            full((two_waves, nlon)),
        ],
        out_specs=pl.BlockSpec((1, two_waves // 2, 2 * chan), lambda j: (j, 0, 0)),
        out_shape=jax.ShapeDtypeStruct((lat_local, two_waves // 2, 2 * chan), jnp.bfloat16),
        compiler_params=pltpu.CompilerParams(vmem_limit_bytes=48 * 1024 * 1024),
        cost_estimate=pl.CostEstimate(
            flops=2 * lat_local * nlon * (2 * hid * chan + two_waves * chan),
            transcendentals=lat_local * nlon * hid,
            bytes_accessed=two_waves * nlon * 2 + lat_local * (chan * nlon * 2 + two_waves * chan * 2),
        ),
    )(
        lat_w,
        grid_t,
        col_scale[None, :],
        in_weight,
        in_bias[None, :],
        out_weight,
        wave_table,
    )


def inverse_kernel(wave_ref, basis_ref, north_ref, south_ref, spec_ref, damp_ref, o_ref, *, factor):
    block = basis_ref.shape[0]
    degrees = basis_ref.shape[1]
    n = lax.broadcasted_iota(jnp.int32, (degrees, 1), 0)
    wave_factor = (n * (n + 1)).astype(jnp.float32) / (NN * NN)
    for b in range(block):
        m = wave_ref[pl.program_id(0) * block + b]
        basis = basis_ref[b]
        east = jnp.dot(basis, north_ref[b], preferred_element_type=jnp.float32)
        west = jnp.dot(basis, south_ref[b], preferred_element_type=jnp.float32)
        parity = jnp.where((n + m) % 2 == 0, 1.0, -1.0).astype(jnp.float32)
        legendre = factor * (east + parity * west)
        damped = legendre - damp_ref[...] * wave_factor * spec_ref[b].astype(jnp.float32)
        o_ref[b] = jnp.where(n >= m, damped, 0.0)


def inverse_legendre(wave_own, lat_basis, north, south, spectral, damp_all, factor):
    rows, degrees, half_lat = lat_basis.shape
    width = spectral.shape[2]
    block = 4 if rows % 4 == 0 else 1
    three = lambda shape: pl.BlockSpec(shape, lambda r: (r, 0, 0))
    return pl.pallas_call(
        functools.partial(inverse_kernel, factor=factor),
        grid=(rows // block,),
        in_specs=[
            pl.BlockSpec(memory_space=pltpu.SMEM),
            three((block, degrees, half_lat)),
            three((block, half_lat, width)),
            three((block, half_lat, width)),
            three((block, degrees, width)),
            pl.BlockSpec((1, width), lambda r: (0, 0)),
        ],
        out_specs=three((block, degrees, width)),
        out_shape=jax.ShapeDtypeStruct((rows, degrees, width), jnp.float32),
        cost_estimate=pl.CostEstimate(
            flops=4 * rows * degrees * half_lat * width,
            transcendentals=0,
            bytes_accessed=rows * (degrees * half_lat * 2 + half_lat * width * 4 + degrees * width * 6),
        ),
    )(wave_own, lat_basis, north, south, spectral, damp_all[None, :])


def on_device(spectral, lat_basis, block_order, in_weight, in_bias, out_weight, col_gain, damping):
    devices = lax.axis_size("lat")
    my_index = lax.axis_index("lat")
    row_count = spectral.shape[0]
    degrees = spectral.shape[1]
    chan_width = spectral.shape[2]
    chan_count = chan_width // 2
    half_lat = lat_basis.shape[2]
    lat_total = 2 * half_lat
    half_local = half_lat // devices
    wave_total = row_count * devices
    wave_all = wavenumbers(block_order, wave_total)
    wave_own = lax.dynamic_slice_in_dim(wave_all, my_index * row_count, row_count)
    degree = jnp.arange(degrees, dtype=jnp.int32)
    inside = degree[None, :] >= wave_own[:, None]
    parity = jnp.where((degree[None, :] + wave_own[:, None]) % 2 == 0, 1.0, -1.0).astype(
        jnp.float32
    )
    masked = jnp.where(inside[:, :, None], spectral, jnp.zeros_like(spectral))
    flipped = jnp.where(parity[:, :, None] > 0, masked, -masked)
    wave_table = lon_table(wave_all)

    both = jnp.stack([masked, flipped], axis=0)
    fourier = jnp.einsum(
        "rnj,srnc->sjrc", lat_basis, both, preferred_element_type=jnp.float32
    ).astype(jnp.bfloat16)
    outbound = fourier.reshape(2, devices, half_local, row_count, chan_width).transpose(
        1, 0, 2, 3, 4
    ).reshape(devices, 2 * half_local, row_count, chan_width)
    rows_in = lax.all_to_all(outbound, "lat", split_axis=0, concat_axis=0, tiled=True)
    j_ids = my_index * half_local + jnp.arange(half_local, dtype=jnp.int32)
    lat_ids = jnp.concatenate([j_ids, lat_total - 1 - j_ids])
    weight_own = lat_weights_of(lat_ids, lat_total)
    cos_t = wave_table[:wave_total].T
    neg_sin_t = -wave_table[wave_total:].T
    grid_t, partial_value = grid_synthesis(weight_own, rows_in, cos_t, neg_sin_t)
    gathered = lax.all_to_all(
        jnp.broadcast_to(partial_value, (devices, chan_count)), "lat", 0, 0, tiled=True
    )
    global_sum = jnp.sum(gathered, axis=0)
    weight_all = lat_weights_of(jnp.arange(lat_total, dtype=jnp.int32), lat_total)
    variance = global_sum / (NLON * jnp.sum(weight_all))
    col_scale = col_gain * lax.rsqrt(variance + 1e-05)
    lat_local = 2 * half_local
    lead = lat_local // 3

    def to_spectral(first, count):
        weighted_local = column_network(
            weight_own, grid_t, first, count, col_scale, in_weight, in_bias, out_weight, wave_table
        )
        returning = weighted_local.reshape(count, devices, row_count, chan_width)
        return lax.all_to_all(returning, "lat", split_axis=1, concat_axis=1, tiled=True)

    weighted = jnp.concatenate([to_spectral(0, lead), to_spectral(lead, lat_local - lead)], axis=0)
    weighted = weighted.reshape(2, half_local, devices, row_count, chan_width)
    north = weighted[0].transpose(2, 1, 0, 3).reshape(row_count, half_lat, chan_width)
    south = weighted[1].transpose(2, 1, 0, 3).reshape(row_count, half_lat, chan_width)
    factor = 2.0 * math.sqrt(degrees * wave_total / lat_total)
    damp_all = jnp.concatenate([damping, damping])
    return inverse_legendre(wave_own, lat_basis, north, south, spectral, damp_all, factor)


def solution(mesh):
    in_specs = (
        P(("member", "lat"), None, None),
        P("lat", None, None),
        P(),
        P(),
        P(),
        P(),
        P(),
        P(),
    )
    out_specs = P(("member", "lat"), None, None)
    return jax.shard_map(
        on_device, mesh=mesh, in_specs=in_specs, out_specs=out_specs, check_vma=False
    )
```

```python
import functools
import math

import jax
import jax.numpy as jnp
from jax import lax
from jax.experimental import pallas as pl
from jax.experimental.pallas import tpu as pltpu
from jax.sharding import PartitionSpec as P

NN = 512
NLON = 1536
MB = 4
LON_TILE = 512


def wavenumbers(block_order, slot_count):
    slot_ids = jnp.arange(slot_count, dtype=jnp.int32)
    blocks = block_order.shape[0]
    matches = (slot_ids // MB)[:, None] == jnp.arange(blocks, dtype=jnp.int32)[None, :]
    chosen = jnp.sum(jnp.where(matches, block_order[None, :], 0), axis=1)
    return chosen * MB + slot_ids % MB


def lon_table(wave_all):
    longitude = jnp.arange(NLON, dtype=jnp.int32)
    phase_index = wave_all[:, None] * longitude[None, :] % NLON
    angles = phase_index.astype(jnp.float32) * (2.0 * math.pi / NLON)
    return jnp.concatenate([jnp.cos(angles), jnp.sin(angles)], axis=0).astype(jnp.bfloat16)


def lat_weights_of(latitude_index, lat_total):
    latitude = latitude_index.astype(jnp.float32)
    return jnp.cos(math.pi * ((latitude + 0.5) / lat_total - 0.5))


def column_kernel(
    weight_ref, rows_ref, scale_ref, in_w_ref, bias_ref, out_w_ref,
    table_ref, o_ref,
):
    j = pl.program_id(0)
    sources, _, rows_per, width = rows_ref.shape
    chan = width // 2
    waves = table_ref.shape[0] // 2
    rows = rows_ref[:, 0].astype(jnp.float32).reshape(sources * rows_per, width)
    rows = rows.astype(jnp.bfloat16)
    real = rows[:, :chan]
    imag = rows[:, chan:]
    scale = scale_ref[...]
    acc = jnp.zeros((2 * waves, chan), jnp.float32)
    for c in range(NLON // LON_TILE):
        lo = c * LON_TILE
        first_dims = (((0,), (0,)), ((), ()))
        wide = lax.dot_general(
            table_ref[:waves, lo:lo + LON_TILE], real, first_dims,
            preferred_element_type=jnp.float32,
        )
        wide = wide - lax.dot_general(
            table_ref[waves:, lo:lo + LON_TILE], imag, first_dims,
            preferred_element_type=jnp.float32,
        )
        g = wide.astype(jnp.bfloat16).astype(jnp.float32)
        normed = (g * scale).astype(jnp.bfloat16)
        pre = jnp.dot(normed, in_w_ref[...], preferred_element_type=jnp.float32) + bias_ref[...]
        hidden = jax.nn.gelu(pre).astype(jnp.bfloat16)
        col = jnp.dot(hidden, out_w_ref[...], preferred_element_type=jnp.float32).astype(
            jnp.bfloat16
        )
        acc = acc + jnp.dot(
            table_ref[:, lo:lo + LON_TILE], col, preferred_element_type=jnp.float32
        )
    inv_root = 1.0 / math.sqrt(NLON)
    w = weight_ref[j]
    cos_part = (acc[:waves] * inv_root).astype(jnp.bfloat16).astype(jnp.float32)
    sin_part = ((-acc[waves:]) * inv_root).astype(jnp.bfloat16).astype(jnp.float32)
    o_ref[0, :, :chan] = (w * cos_part).astype(jnp.bfloat16)
    o_ref[0, :, chan:] = (w * sin_part).astype(jnp.bfloat16)


def column_network(
    lat_w, rows_in, col_scale, in_weight, in_bias, out_weight, wave_table
):
    sources, lat_local, rows_per, width = rows_in.shape
    chan = width // 2
    waves = sources * rows_per
    nlon = wave_table.shape[1]
    hid = in_weight.shape[1]
    two_waves = wave_table.shape[0]
    full = lambda shape: pl.BlockSpec(shape, lambda j: (0,) * len(shape))
    return pl.pallas_call(
        column_kernel,
        grid=(lat_local,),
        in_specs=[
            pl.BlockSpec(memory_space=pltpu.SMEM),
            pl.BlockSpec((sources, 1, rows_per, width), lambda j: (0, j, 0, 0)),
            full((1, chan)),
            full((chan, hid)),
            full((1, hid)),
            full((hid, chan)),
            full((two_waves, nlon)),
        ],
        out_specs=pl.BlockSpec((1, two_waves // 2, 2 * chan), lambda j: (j, 0, 0)),
        out_shape=jax.ShapeDtypeStruct((lat_local, two_waves // 2, 2 * chan), jnp.bfloat16),
        compiler_params=pltpu.CompilerParams(vmem_limit_bytes=48 * 1024 * 1024),
        cost_estimate=pl.CostEstimate(
            flops=2 * lat_local * nlon * (2 * hid * chan + two_waves * chan + waves * width),
            transcendentals=lat_local * nlon * hid,
            bytes_accessed=2 * two_waves * nlon + lat_local * (waves * width * 2 + two_waves * chan * 2),
        ),
    )(
        lat_w,
        rows_in,
        col_scale[None, :],
        in_weight,
        in_bias[None, :],
        out_weight,
        wave_table,
    )


def inverse_kernel(wave_ref, basis_ref, north_ref, south_ref, spec_ref, damp_ref, o_ref, *, factor):
    block = basis_ref.shape[0]
    degrees = basis_ref.shape[1]
    n = lax.broadcasted_iota(jnp.int32, (degrees, 1), 0)
    wave_factor = (n * (n + 1)).astype(jnp.float32) / (NN * NN)
    for b in range(block):
        m = wave_ref[pl.program_id(0) * block + b]
        basis = basis_ref[b]
        east = jnp.dot(basis, north_ref[b], preferred_element_type=jnp.float32)
        west = jnp.dot(basis, south_ref[b], preferred_element_type=jnp.float32)
        parity = jnp.where((n + m) % 2 == 0, 1.0, -1.0).astype(jnp.float32)
        legendre = factor * (east + parity * west)
        damped = legendre - damp_ref[...] * wave_factor * spec_ref[b].astype(jnp.float32)
        o_ref[b] = jnp.where(n >= m, damped, 0.0)


def inverse_legendre(wave_own, lat_basis, north, south, spectral, damp_all, factor):
    rows, degrees, half_lat = lat_basis.shape
    width = spectral.shape[2]
    block = 4 if rows % 4 == 0 else 1
    three = lambda shape: pl.BlockSpec(shape, lambda r: (r, 0, 0))
    return pl.pallas_call(
        functools.partial(inverse_kernel, factor=factor),
        grid=(rows // block,),
        in_specs=[
            pl.BlockSpec(memory_space=pltpu.SMEM),
            three((block, degrees, half_lat)),
            three((block, half_lat, width)),
            three((block, half_lat, width)),
            three((block, degrees, width)),
            pl.BlockSpec((1, width), lambda r: (0, 0)),
        ],
        out_specs=three((block, degrees, width)),
        out_shape=jax.ShapeDtypeStruct((rows, degrees, width), jnp.float32),
        cost_estimate=pl.CostEstimate(
            flops=4 * rows * degrees * half_lat * width,
            transcendentals=0,
            bytes_accessed=rows * (degrees * half_lat * 2 + half_lat * width * 4 + degrees * width * 6),
        ),
    )(wave_own, lat_basis, north, south, spectral, damp_all[None, :])


def on_device(spectral, lat_basis, block_order, in_weight, in_bias, out_weight, col_gain, damping):
    devices = lax.axis_size("lat")
    my_index = lax.axis_index("lat")
    row_count = spectral.shape[0]
    degrees = spectral.shape[1]
    chan_width = spectral.shape[2]
    chan_count = chan_width // 2
    half_lat = lat_basis.shape[2]
    lat_total = 2 * half_lat
    half_local = half_lat // devices
    wave_total = row_count * devices
    wave_all = wavenumbers(block_order, wave_total)
    wave_own = lax.dynamic_slice_in_dim(wave_all, my_index * row_count, row_count)
    degree = jnp.arange(degrees, dtype=jnp.int32)
    inside = degree[None, :] >= wave_own[:, None]
    parity = jnp.where((degree[None, :] + wave_own[:, None]) % 2 == 0, 1.0, -1.0).astype(
        jnp.float32
    )
    masked = jnp.where(inside[:, :, None], spectral, jnp.zeros_like(spectral))
    flipped = jnp.where(parity[:, :, None] > 0, masked, -masked)
    wave_table = lon_table(wave_all)
    j_ids = my_index * half_local + jnp.arange(half_local, dtype=jnp.int32)
    weight_north = lat_weights_of(j_ids, lat_total)
    weight_south = lat_weights_of(lat_total - 1 - j_ids, lat_total)
    j_all = jnp.arange(half_lat, dtype=jnp.int32)
    weight_all = lat_weights_of(jnp.arange(lat_total, dtype=jnp.int32), lat_total)
    real_coef = jnp.where(wave_own == 0, float(NLON), NLON / 2.0)
    imag_coef = jnp.where(wave_own == 0, 0.0, NLON / 2.0)

    def hemisphere(values, lat_weight):
        fourier = jnp.einsum(
            "rnj,rnc->jrc", lat_basis, values, preferred_element_type=jnp.float32
        ).astype(jnp.bfloat16)
        wide = fourier.astype(jnp.float32)
        per_lat = jnp.sum(
            real_coef[None, :, None] * wide[:, :, :chan_count] ** 2
            + imag_coef[None, :, None] * wide[:, :, chan_count:] ** 2,
            axis=1,
        )
        part = jnp.sum(lat_weight[:, None] * per_lat, axis=0)
        return fourier.reshape(devices, half_local, row_count, chan_width), part

    out_north, part_north = hemisphere(masked, lat_weights_of(j_all, lat_total))
    out_south, part_south = hemisphere(flipped, lat_weights_of(lat_total - 1 - j_all, lat_total))
    partial_value = part_north + part_south
    gathered = lax.all_to_all(
        jnp.broadcast_to(partial_value[None], (devices, chan_count)), "lat", 0, 0, tiled=True
    )
    global_sum = jnp.sum(gathered, axis=0)
    variance = global_sum / (NLON * jnp.sum(weight_all))
    col_scale = col_gain * lax.rsqrt(variance + 1e-05)

    def round_trip(outbound, lat_weight):
        rows_in = lax.all_to_all(outbound, "lat", split_axis=0, concat_axis=0, tiled=True)
        weighted_local = column_network(
            lat_weight, rows_in, col_scale, in_weight, in_bias, out_weight, wave_table
        )
        returning = weighted_local.reshape(half_local, devices, row_count, chan_width)
        back = lax.all_to_all(returning, "lat", split_axis=1, concat_axis=1, tiled=True)
        return back.transpose(2, 1, 0, 3).reshape(row_count, half_lat, chan_width)

    north = round_trip(out_north, weight_north)
    south = round_trip(out_south, weight_south)
    factor = 2.0 * math.sqrt(degrees * wave_total / lat_total)
    damp_all = jnp.concatenate([damping, damping])
    return inverse_legendre(wave_own, lat_basis, north, south, spectral, damp_all, factor)


def solution(mesh):
    in_specs = (
        P(("member", "lat"), None, None),
        P("lat", None, None),
        P(),
        P(),
        P(),
        P(),
        P(),
        P(),
    )
    out_specs = P(("member", "lat"), None, None)
    return jax.shard_map(
        on_device, mesh=mesh, in_specs=in_specs, out_specs=out_specs, check_vma=False
    )
```

```python
import functools
import math

import jax
import jax.numpy as jnp
from jax import lax
from jax.experimental import pallas as pl
from jax.experimental.pallas import tpu as pltpu
from jax.sharding import PartitionSpec as P

NN = 512
NLON = 1536
MB = 4
LON_TILE = 512


def wavenumbers(block_order, slot_count):
    slot_ids = jnp.arange(slot_count, dtype=jnp.int32)
    blocks = block_order.shape[0]
    matches = (slot_ids // MB)[:, None] == jnp.arange(blocks, dtype=jnp.int32)[None, :]
    chosen = jnp.sum(jnp.where(matches, block_order[None, :], 0), axis=1)
    return chosen * MB + slot_ids % MB


def lon_table(wave_all):
    longitude = jnp.arange(NLON, dtype=jnp.int32)
    phase_index = wave_all[:, None] * longitude[None, :] % NLON
    angles = phase_index.astype(jnp.float32) * (2.0 * math.pi / NLON)
    return jnp.concatenate([jnp.cos(angles), jnp.sin(angles)], axis=0).astype(jnp.bfloat16)


def lat_weights_of(latitude_index, lat_total):
    latitude = latitude_index.astype(jnp.float32)
    return jnp.cos(math.pi * ((latitude + 0.5) / lat_total - 0.5))


def column_kernel(
    weight_ref, rows_ref, scale_ref, in_w_ref, bias_ref, out_w_ref,
    table_ref, o_ref,
):
    j = pl.program_id(0)
    sources, _, rows_per, width = rows_ref.shape
    chan = width // 2
    waves = table_ref.shape[0] // 2
    rows = rows_ref[:, 0].astype(jnp.float32).reshape(sources * rows_per, width)
    rows = rows.astype(jnp.bfloat16)
    real = rows[:, :chan]
    imag = rows[:, chan:]
    scale = scale_ref[...]
    acc = jnp.zeros((2 * waves, chan), jnp.float32)
    for c in range(NLON // LON_TILE):
        lo = c * LON_TILE
        first_dims = (((0,), (0,)), ((), ()))
        wide = lax.dot_general(
            table_ref[:waves, lo:lo + LON_TILE], real, first_dims,
            preferred_element_type=jnp.float32,
        )
        wide = wide - lax.dot_general(
            table_ref[waves:, lo:lo + LON_TILE], imag, first_dims,
            preferred_element_type=jnp.float32,
        )
        g = wide.astype(jnp.bfloat16).astype(jnp.float32)
        normed = (g * scale).astype(jnp.bfloat16)
        pre = jnp.dot(normed, in_w_ref[...], preferred_element_type=jnp.float32) + bias_ref[...]
        hidden = jax.nn.gelu(pre).astype(jnp.bfloat16)
        col = jnp.dot(hidden, out_w_ref[...], preferred_element_type=jnp.float32).astype(
            jnp.bfloat16
        )
        acc = acc + jnp.dot(
            table_ref[:, lo:lo + LON_TILE], col, preferred_element_type=jnp.float32
        )
    inv_root = 1.0 / math.sqrt(NLON)
    w = weight_ref[j]
    cos_part = (acc[:waves] * inv_root).astype(jnp.bfloat16).astype(jnp.float32)
    sin_part = ((-acc[waves:]) * inv_root).astype(jnp.bfloat16).astype(jnp.float32)
    o_ref[0, :, :chan] = (w * cos_part).astype(jnp.bfloat16)
    o_ref[0, :, chan:] = (w * sin_part).astype(jnp.bfloat16)


def column_network(
    lat_w, rows_in, col_scale, in_weight, in_bias, out_weight, wave_table
):
    sources, lat_local, rows_per, width = rows_in.shape
    chan = width // 2
    waves = sources * rows_per
    nlon = wave_table.shape[1]
    hid = in_weight.shape[1]
    two_waves = wave_table.shape[0]
    full = lambda shape: pl.BlockSpec(shape, lambda j: (0,) * len(shape))
    return pl.pallas_call(
        column_kernel,
        grid=(lat_local,),
        in_specs=[
            pl.BlockSpec(memory_space=pltpu.SMEM),
            pl.BlockSpec((sources, 1, rows_per, width), lambda j: (0, j, 0, 0)),
            full((1, chan)),
            full((chan, hid)),
            full((1, hid)),
            full((hid, chan)),
            full((two_waves, nlon)),
        ],
        out_specs=pl.BlockSpec((1, two_waves // 2, 2 * chan), lambda j: (j, 0, 0)),
        out_shape=jax.ShapeDtypeStruct((lat_local, two_waves // 2, 2 * chan), jnp.bfloat16),
        compiler_params=pltpu.CompilerParams(vmem_limit_bytes=48 * 1024 * 1024),
        cost_estimate=pl.CostEstimate(
            flops=2 * lat_local * nlon * (2 * hid * chan + two_waves * chan + waves * width),
            transcendentals=lat_local * nlon * hid,
            bytes_accessed=2 * two_waves * nlon + lat_local * (waves * width * 2 + two_waves * chan * 2),
        ),
    )(
        lat_w,
        rows_in,
        col_scale[None, :],
        in_weight,
        in_bias[None, :],
        out_weight,
        wave_table,
    )


def inverse_kernel(wave_ref, basis_ref, north_ref, south_ref, spec_ref, damp_ref, o_ref, *, factor):
    block = basis_ref.shape[0]
    degrees = basis_ref.shape[1]
    n = lax.broadcasted_iota(jnp.int32, (degrees, 1), 0)
    wave_factor = (n * (n + 1)).astype(jnp.float32) / (NN * NN)
    for b in range(block):
        m = wave_ref[pl.program_id(0) * block + b]
        basis = basis_ref[b]
        east = jnp.dot(basis, north_ref[b], preferred_element_type=jnp.float32)
        west = jnp.dot(basis, south_ref[b], preferred_element_type=jnp.float32)
        parity = jnp.where((n + m) % 2 == 0, 1.0, -1.0).astype(jnp.float32)
        legendre = factor * (east + parity * west)
        damped = legendre - damp_ref[...] * wave_factor * spec_ref[b].astype(jnp.float32)
        o_ref[b] = jnp.where(n >= m, damped, 0.0)


def inverse_legendre(wave_own, lat_basis, north, south, spectral, damp_all, factor):
    rows, degrees, half_lat = lat_basis.shape
    width = spectral.shape[2]
    block = 4 if rows % 4 == 0 else 1
    three = lambda shape: pl.BlockSpec(shape, lambda r: (r, 0, 0))
    return pl.pallas_call(
        functools.partial(inverse_kernel, factor=factor),
        grid=(rows // block,),
        in_specs=[
            pl.BlockSpec(memory_space=pltpu.SMEM),
            three((block, degrees, half_lat)),
            three((block, half_lat, width)),
            three((block, half_lat, width)),
            three((block, degrees, width)),
            pl.BlockSpec((1, width), lambda r: (0, 0)),
        ],
        out_specs=three((block, degrees, width)),
        out_shape=jax.ShapeDtypeStruct((rows, degrees, width), jnp.float32),
        cost_estimate=pl.CostEstimate(
            flops=4 * rows * degrees * half_lat * width,
            transcendentals=0,
            bytes_accessed=rows * (degrees * half_lat * 2 + half_lat * width * 4 + degrees * width * 6),
        ),
    )(wave_own, lat_basis, north, south, spectral, damp_all[None, :])


def on_device(spectral, lat_basis, block_order, in_weight, in_bias, out_weight, col_gain, damping):
    devices = lax.axis_size("lat")
    my_index = lax.axis_index("lat")
    row_count = spectral.shape[0]
    degrees = spectral.shape[1]
    chan_width = spectral.shape[2]
    chan_count = chan_width // 2
    half_lat = lat_basis.shape[2]
    lat_total = 2 * half_lat
    half_local = half_lat // devices
    wave_total = row_count * devices
    wave_all = wavenumbers(block_order, wave_total)
    wave_own = lax.dynamic_slice_in_dim(wave_all, my_index * row_count, row_count)
    degree = jnp.arange(degrees, dtype=jnp.int32)
    inside = degree[None, :] >= wave_own[:, None]
    parity = jnp.where((degree[None, :] + wave_own[:, None]) % 2 == 0, 1.0, -1.0).astype(
        jnp.float32
    )
    masked = jnp.where(inside[:, :, None], spectral, jnp.zeros_like(spectral))
    flipped = jnp.where(parity[:, :, None] > 0, masked, -masked)
    wave_table = lon_table(wave_all)
    j_ids = my_index * half_local + jnp.arange(half_local, dtype=jnp.int32)
    weight_north = lat_weights_of(j_ids, lat_total)
    weight_south = lat_weights_of(lat_total - 1 - j_ids, lat_total)
    j_all = jnp.arange(half_lat, dtype=jnp.int32)
    weight_all = lat_weights_of(jnp.arange(lat_total, dtype=jnp.int32), lat_total)
    real_coef = jnp.where(wave_own == 0, float(NLON), NLON / 2.0)
    imag_coef = jnp.where(wave_own == 0, 0.0, NLON / 2.0)

    def hemisphere(values, lat_weight):
        fourier = jnp.einsum(
            "rnj,rnc->jrc", lat_basis, values, preferred_element_type=jnp.float32
        ).astype(jnp.bfloat16)
        wide = fourier.astype(jnp.float32)
        per_lat = jnp.sum(
            real_coef[None, :, None] * wide[:, :, :chan_count] ** 2
            + imag_coef[None, :, None] * wide[:, :, chan_count:] ** 2,
            axis=1,
        )
        part = jnp.sum(lat_weight[:, None] * per_lat, axis=0)
        return fourier.reshape(devices, half_local, row_count, chan_width), part

    out_north, part_north = hemisphere(masked, lat_weights_of(j_all, lat_total))
    out_south, part_south = hemisphere(flipped, lat_weights_of(lat_total - 1 - j_all, lat_total))
    partial_value = part_north + part_south
    gathered = lax.all_to_all(
        jnp.broadcast_to(partial_value[None], (devices, chan_count)), "lat", 0, 0, tiled=True
    )
    global_sum = jnp.sum(gathered, axis=0)
    variance = global_sum / (NLON * jnp.sum(weight_all))
    col_scale = col_gain * lax.rsqrt(variance + 1e-05)

    def round_trip(outbound, lat_weight):
        rows_in = lax.all_to_all(outbound, "lat", split_axis=0, concat_axis=0, tiled=True)
        weighted_local = column_network(
            lat_weight, rows_in, col_scale, in_weight, in_bias, out_weight, wave_table
        )
        returning = weighted_local.reshape(half_local, devices, row_count, chan_width)
        back = lax.all_to_all(returning, "lat", split_axis=1, concat_axis=1, tiled=True)
        return back.transpose(2, 1, 0, 3).reshape(row_count, half_lat, chan_width)

    north = round_trip(out_north, weight_north)
    out_south, wave_table = lax.optimization_barrier((out_south, wave_table))
    south = round_trip(out_south, weight_south)
    factor = 2.0 * math.sqrt(degrees * wave_total / lat_total)
    damp_all = jnp.concatenate([damping, damping])
    return inverse_legendre(wave_own, lat_basis, north, south, spectral, damp_all, factor)


def solution(mesh):
    in_specs = (
        P(("member", "lat"), None, None),
        P("lat", None, None),
        P(),
        P(),
        P(),
        P(),
        P(),
        P(),
    )
    out_specs = P(("member", "lat"), None, None)
    return jax.shard_map(
        on_device, mesh=mesh, in_specs=in_specs, out_specs=out_specs, check_vma=False
    )
```

```python
import functools
import math

import jax
import jax.numpy as jnp
from jax import lax
from jax.experimental import pallas as pl
from jax.experimental.pallas import tpu as pltpu
from jax.sharding import PartitionSpec as P

NN = 512
NLON = 1536
MB = 4
LON_TILE = 512


def wavenumbers(block_order, slot_count):
    slot_ids = jnp.arange(slot_count, dtype=jnp.int32)
    blocks = block_order.shape[0]
    matches = (slot_ids // MB)[:, None] == jnp.arange(blocks, dtype=jnp.int32)[None, :]
    chosen = jnp.sum(jnp.where(matches, block_order[None, :], 0), axis=1)
    return chosen * MB + slot_ids % MB


def lon_table(wave_all):
    longitude = jnp.arange(NLON, dtype=jnp.int32)
    phase_index = wave_all[:, None] * longitude[None, :] % NLON
    angles = phase_index.astype(jnp.float32) * (2.0 * math.pi / NLON)
    return jnp.concatenate([jnp.cos(angles), jnp.sin(angles)], axis=0).astype(jnp.bfloat16)


def lat_weights_of(latitude_index, lat_total):
    latitude = latitude_index.astype(jnp.float32)
    return jnp.cos(math.pi * ((latitude + 0.5) / lat_total - 0.5))


def column_kernel(
    weight_ref, rows_ref, scale_ref, in_w_ref, bias_ref, out_w_ref,
    table_ref, o_ref,
):
    j = pl.program_id(0)
    sources, _, rows_per, width = rows_ref.shape
    chan = width // 2
    waves = table_ref.shape[0] // 2
    rows = rows_ref[:, 0].astype(jnp.float32).reshape(sources * rows_per, width)
    rows = rows.astype(jnp.bfloat16)
    real = rows[:, :chan]
    imag = rows[:, chan:]
    scale = scale_ref[...]
    acc = jnp.zeros((2 * waves, chan), jnp.float32)
    for c in range(NLON // LON_TILE):
        lo = c * LON_TILE
        first_dims = (((0,), (0,)), ((), ()))
        wide = lax.dot_general(
            table_ref[:waves, lo:lo + LON_TILE], real, first_dims,
            preferred_element_type=jnp.float32,
        )
        wide = wide - lax.dot_general(
            table_ref[waves:, lo:lo + LON_TILE], imag, first_dims,
            preferred_element_type=jnp.float32,
        )
        g = wide.astype(jnp.bfloat16).astype(jnp.float32)
        normed = (g * scale).astype(jnp.bfloat16)
        pre = jnp.dot(normed, in_w_ref[...], preferred_element_type=jnp.float32) + bias_ref[...]
        hidden = jax.nn.gelu(pre).astype(jnp.bfloat16)
        col = jnp.dot(hidden, out_w_ref[...], preferred_element_type=jnp.float32).astype(
            jnp.bfloat16
        )
        acc = acc + jnp.dot(
            table_ref[:, lo:lo + LON_TILE], col, preferred_element_type=jnp.float32
        )
    inv_root = 1.0 / math.sqrt(NLON)
    w = weight_ref[j]
    cos_part = (acc[:waves] * inv_root).astype(jnp.bfloat16).astype(jnp.float32)
    sin_part = ((-acc[waves:]) * inv_root).astype(jnp.bfloat16).astype(jnp.float32)
    o_ref[0, :, :chan] = (w * cos_part).astype(jnp.bfloat16)
    o_ref[0, :, chan:] = (w * sin_part).astype(jnp.bfloat16)


def column_network(
    lat_w, rows_in, col_scale, in_weight, in_bias, out_weight, wave_table
):
    sources, _, rows_per, width = rows_in.shape
    lat_local = lat_w.shape[0]
    chan = width // 2
    waves = sources * rows_per
    nlon = wave_table.shape[1]
    hid = in_weight.shape[1]
    two_waves = wave_table.shape[0]
    full = lambda shape: pl.BlockSpec(shape, lambda j: (0,) * len(shape))
    return pl.pallas_call(
        column_kernel,
        grid=(lat_local,),
        in_specs=[
            pl.BlockSpec(memory_space=pltpu.SMEM),
            pl.BlockSpec((sources, 1, rows_per, width), lambda j: (0, j, 0, 0)),
            full((1, chan)),
            full((chan, hid)),
            full((1, hid)),
            full((hid, chan)),
            full((two_waves, nlon)),
        ],
        out_specs=pl.BlockSpec((1, two_waves // 2, 2 * chan), lambda j: (j, 0, 0)),
        out_shape=jax.ShapeDtypeStruct((lat_local, two_waves // 2, 2 * chan), jnp.bfloat16),
        compiler_params=pltpu.CompilerParams(vmem_limit_bytes=48 * 1024 * 1024),
        cost_estimate=pl.CostEstimate(
            flops=2 * lat_local * nlon * (2 * hid * chan + two_waves * chan + waves * width),
            transcendentals=lat_local * nlon * hid,
            bytes_accessed=2 * two_waves * nlon + lat_local * (waves * width * 2 + two_waves * chan * 2),
        ),
    )(
        lat_w,
        rows_in,
        col_scale[None, :],
        in_weight,
        in_bias[None, :],
        out_weight,
        wave_table,
    )


def inverse_kernel(wave_ref, basis_ref, north_ref, south_ref, spec_ref, damp_ref, o_ref, *, factor):
    block = basis_ref.shape[0]
    degrees = basis_ref.shape[1]
    n = lax.broadcasted_iota(jnp.int32, (degrees, 1), 0)
    wave_factor = (n * (n + 1)).astype(jnp.float32) / (NN * NN)
    for b in range(block):
        m = wave_ref[pl.program_id(0) * block + b]
        basis = basis_ref[b]
        east = jnp.dot(basis, north_ref[b], preferred_element_type=jnp.float32)
        west = jnp.dot(basis, south_ref[b], preferred_element_type=jnp.float32)
        parity = jnp.where((n + m) % 2 == 0, 1.0, -1.0).astype(jnp.float32)
        legendre = factor * (east + parity * west)
        damped = legendre - damp_ref[...] * wave_factor * spec_ref[b].astype(jnp.float32)
        o_ref[b] = jnp.where(n >= m, damped, 0.0)


def inverse_legendre(wave_own, lat_basis, north, south, spectral, damp_all, factor):
    rows, degrees, half_lat = lat_basis.shape
    width = spectral.shape[2]
    block = 4 if rows % 4 == 0 else 1
    three = lambda shape: pl.BlockSpec(shape, lambda r: (r, 0, 0))
    return pl.pallas_call(
        functools.partial(inverse_kernel, factor=factor),
        grid=(rows // block,),
        in_specs=[
            pl.BlockSpec(memory_space=pltpu.SMEM),
            three((block, degrees, half_lat)),
            three((block, half_lat, width)),
            three((block, half_lat, width)),
            three((block, degrees, width)),
            pl.BlockSpec((1, width), lambda r: (0, 0)),
        ],
        out_specs=three((block, degrees, width)),
        out_shape=jax.ShapeDtypeStruct((rows, degrees, width), jnp.float32),
        cost_estimate=pl.CostEstimate(
            flops=4 * rows * degrees * half_lat * width,
            transcendentals=0,
            bytes_accessed=rows * (degrees * half_lat * 2 + half_lat * width * 4 + degrees * width * 6),
        ),
    )(wave_own, lat_basis, north, south, spectral, damp_all[None, :])


def on_device(spectral, lat_basis, block_order, in_weight, in_bias, out_weight, col_gain, damping):
    devices = lax.axis_size("lat")
    my_index = lax.axis_index("lat")
    row_count = spectral.shape[0]
    degrees = spectral.shape[1]
    chan_width = spectral.shape[2]
    chan_count = chan_width // 2
    half_lat = lat_basis.shape[2]
    lat_total = 2 * half_lat
    half_local = half_lat // devices
    wave_total = row_count * devices
    wave_all = wavenumbers(block_order, wave_total)
    wave_own = lax.dynamic_slice_in_dim(wave_all, my_index * row_count, row_count)
    degree = jnp.arange(degrees, dtype=jnp.int32)
    inside = degree[None, :] >= wave_own[:, None]
    parity = jnp.where((degree[None, :] + wave_own[:, None]) % 2 == 0, 1.0, -1.0).astype(
        jnp.float32
    )
    masked = jnp.where(inside[:, :, None], spectral, jnp.zeros_like(spectral))
    flipped = jnp.where(parity[:, :, None] > 0, masked, -masked)
    wave_table = lon_table(wave_all)
    j_ids = my_index * half_local + jnp.arange(half_local, dtype=jnp.int32)
    weight_north = lat_weights_of(j_ids, lat_total)
    weight_south = lat_weights_of(lat_total - 1 - j_ids, lat_total)
    j_all = jnp.arange(half_lat, dtype=jnp.int32)
    weight_all = lat_weights_of(jnp.arange(lat_total, dtype=jnp.int32), lat_total)
    real_coef = jnp.where(wave_own == 0, float(NLON), NLON / 2.0)
    imag_coef = jnp.where(wave_own == 0, 0.0, NLON / 2.0)

    def hemisphere(values, lat_weight):
        fourier = jnp.einsum(
            "rnj,rnc->jrc", lat_basis, values, preferred_element_type=jnp.float32
        ).astype(jnp.bfloat16)
        wide = fourier.astype(jnp.float32)
        per_lat = jnp.sum(
            real_coef[None, :, None] * wide[:, :, :chan_count] ** 2
            + imag_coef[None, :, None] * wide[:, :, chan_count:] ** 2,
            axis=1,
        )
        part = jnp.sum(lat_weight[:, None] * per_lat, axis=0)
        return fourier.reshape(devices, half_local, row_count, chan_width), part

    out_north, part_north = hemisphere(masked, lat_weights_of(j_all, lat_total))
    out_south, part_south = hemisphere(flipped, lat_weights_of(lat_total - 1 - j_all, lat_total))
    partial_value = part_north + part_south
    hi = partial_value.astype(jnp.bfloat16)
    rest = partial_value - hi.astype(jnp.float32)
    mid = rest.astype(jnp.bfloat16)
    lo = (rest - mid.astype(jnp.float32)).astype(jnp.bfloat16)
    pieces = jnp.zeros((row_count, chan_width), jnp.bfloat16)
    pieces = pieces.at[0, :chan_count].set(hi).at[0, chan_count:].set(mid)
    pieces = pieces.at[1, :chan_count].set(lo)
    slot = jnp.broadcast_to(pieces[None, None], (devices, 1, row_count, chan_width))
    north_in = lax.all_to_all(
        jnp.concatenate([out_north, slot], axis=1), "lat", split_axis=0, concat_axis=0, tiled=True
    )
    got = north_in[:, half_local, :2].astype(jnp.float32)
    global_sum = jnp.sum(got[:, 0, :chan_count] + got[:, 0, chan_count:] + got[:, 1, :chan_count], axis=0)
    variance = global_sum / (NLON * jnp.sum(weight_all))
    col_scale = col_gain * lax.rsqrt(variance + 1e-05)

    def round_trip(rows_in, lat_weight):
        weighted_local = column_network(
            lat_weight, rows_in, col_scale, in_weight, in_bias, out_weight, wave_table
        )
        returning = weighted_local.reshape(half_local, devices, row_count, chan_width)
        back = lax.all_to_all(returning, "lat", split_axis=1, concat_axis=1, tiled=True)
        return back.transpose(2, 1, 0, 3).reshape(row_count, half_lat, chan_width)

    out_south, wave_table, col_scale, north_in = lax.optimization_barrier(
        (out_south, wave_table, col_scale, north_in)
    )
    north = round_trip(north_in, weight_north)
    south_in = lax.all_to_all(out_south, "lat", split_axis=0, concat_axis=0, tiled=True)
    south = round_trip(south_in, weight_south)
    factor = 2.0 * math.sqrt(degrees * wave_total / lat_total)
    damp_all = jnp.concatenate([damping, damping])
    return inverse_legendre(wave_own, lat_basis, north, south, spectral, damp_all, factor)


def solution(mesh):
    in_specs = (
        P(("member", "lat"), None, None),
        P("lat", None, None),
        P(),
        P(),
        P(),
        P(),
        P(),
        P(),
    )
    out_specs = P(("member", "lat"), None, None)
    return jax.shard_map(
        on_device, mesh=mesh, in_specs=in_specs, out_specs=out_specs, check_vma=False
    )
```

```python
import functools
import math

import jax
import jax.numpy as jnp
from jax import lax
from jax.experimental import pallas as pl
from jax.experimental.pallas import tpu as pltpu
from jax.sharding import PartitionSpec as P

NN = 512
NLON = 1536
MB = 4
LON_TILE = 512


def wavenumbers(block_order, slot_count):
    slot_ids = jnp.arange(slot_count, dtype=jnp.int32)
    blocks = block_order.shape[0]
    matches = (slot_ids // MB)[:, None] == jnp.arange(blocks, dtype=jnp.int32)[None, :]
    chosen = jnp.sum(jnp.where(matches, block_order[None, :], 0), axis=1)
    return chosen * MB + slot_ids % MB


def lon_table(wave_all):
    longitude = jnp.arange(NLON, dtype=jnp.int32)
    phase_index = wave_all[:, None] * longitude[None, :] % NLON
    angles = phase_index.astype(jnp.float32) * (2.0 * math.pi / NLON)
    return jnp.concatenate([jnp.cos(angles), jnp.sin(angles)], axis=0).astype(jnp.bfloat16)


def lat_weights_of(latitude_index, lat_total):
    latitude = latitude_index.astype(jnp.float32)
    return jnp.cos(math.pi * ((latitude + 0.5) / lat_total - 0.5))


def column_kernel(
    weight_ref, rows_ref, scale_ref, in_w_ref, bias_ref, out_w_ref,
    table_ref, o_ref,
):
    j = pl.program_id(0)
    sources, _, rows_per, width = rows_ref.shape
    chan = width // 2
    waves = table_ref.shape[0] // 2
    rows = rows_ref[:, 0].astype(jnp.float32).reshape(sources * rows_per, width)
    rows = rows.astype(jnp.bfloat16)
    real = rows[:, :chan]
    imag = rows[:, chan:]
    scale = scale_ref[...]
    acc = jnp.zeros((2 * waves, chan), jnp.float32)
    for c in range(NLON // LON_TILE):
        lo = c * LON_TILE
        first_dims = (((0,), (0,)), ((), ()))
        wide = lax.dot_general(
            table_ref[:waves, lo:lo + LON_TILE], real, first_dims,
            preferred_element_type=jnp.float32,
        )
        wide = wide - lax.dot_general(
            table_ref[waves:, lo:lo + LON_TILE], imag, first_dims,
            preferred_element_type=jnp.float32,
        )
        g = wide.astype(jnp.bfloat16).astype(jnp.float32)
        normed = (g * scale).astype(jnp.bfloat16)
        pre = jnp.dot(normed, in_w_ref[...], preferred_element_type=jnp.float32) + bias_ref[...]
        hidden = jax.nn.gelu(pre).astype(jnp.bfloat16)
        col = jnp.dot(hidden, out_w_ref[...], preferred_element_type=jnp.float32).astype(
            jnp.bfloat16
        )
        acc = acc + jnp.dot(
            table_ref[:, lo:lo + LON_TILE], col, preferred_element_type=jnp.float32
        )
    inv_root = 1.0 / math.sqrt(NLON)
    w = weight_ref[j]
    cos_part = (acc[:waves] * inv_root).astype(jnp.bfloat16).astype(jnp.float32)
    sin_part = ((-acc[waves:]) * inv_root).astype(jnp.bfloat16).astype(jnp.float32)
    o_ref[0, :, :chan] = (w * cos_part).astype(jnp.bfloat16)
    o_ref[0, :, chan:] = (w * sin_part).astype(jnp.bfloat16)


def column_network(
    lat_w, rows_in, col_scale, in_weight, in_bias, out_weight, wave_table
):
    sources, _, rows_per, width = rows_in.shape
    lat_local = lat_w.shape[0]
    chan = width // 2
    waves = sources * rows_per
    nlon = wave_table.shape[1]
    hid = in_weight.shape[1]
    two_waves = wave_table.shape[0]
    full = lambda shape: pl.BlockSpec(shape, lambda j: (0,) * len(shape))
    return pl.pallas_call(
        column_kernel,
        grid=(lat_local,),
        in_specs=[
            pl.BlockSpec(memory_space=pltpu.SMEM),
            pl.BlockSpec((sources, 1, rows_per, width), lambda j: (0, j, 0, 0)),
            full((1, chan)),
            full((chan, hid)),
            full((1, hid)),
            full((hid, chan)),
            full((two_waves, nlon)),
        ],
        out_specs=pl.BlockSpec((1, two_waves // 2, 2 * chan), lambda j: (j, 0, 0)),
        out_shape=jax.ShapeDtypeStruct((lat_local, two_waves // 2, 2 * chan), jnp.bfloat16),
        compiler_params=pltpu.CompilerParams(vmem_limit_bytes=48 * 1024 * 1024),
        cost_estimate=pl.CostEstimate(
            flops=2 * lat_local * nlon * (2 * hid * chan + two_waves * chan + waves * width),
            transcendentals=lat_local * nlon * hid,
            bytes_accessed=2 * two_waves * nlon + lat_local * (waves * width * 2 + two_waves * chan * 2),
        ),
    )(
        lat_w,
        rows_in,
        col_scale[None, :],
        in_weight,
        in_bias[None, :],
        out_weight,
        wave_table,
    )


def inverse_kernel(wave_ref, basis_ref, north_ref, south_ref, spec_ref, damp_ref, o_ref, *, factor):
    block = basis_ref.shape[0]
    degrees = basis_ref.shape[1]
    n = lax.broadcasted_iota(jnp.int32, (degrees, 1), 0)
    wave_factor = (n * (n + 1)).astype(jnp.float32) / (NN * NN)
    for b in range(block):
        m = wave_ref[pl.program_id(0) * block + b]
        basis = basis_ref[b]
        east = jnp.dot(basis, north_ref[b], preferred_element_type=jnp.float32)
        west = jnp.dot(basis, south_ref[b], preferred_element_type=jnp.float32)
        parity = jnp.where((n + m) % 2 == 0, 1.0, -1.0).astype(jnp.float32)
        legendre = factor * (east + parity * west)
        damped = legendre - damp_ref[...] * wave_factor * spec_ref[b].astype(jnp.float32)
        o_ref[b] = jnp.where(n >= m, damped, 0.0)


def inverse_legendre(wave_own, lat_basis, north, south, spectral, damp_all, factor):
    rows, degrees, half_lat = lat_basis.shape
    width = spectral.shape[2]
    block = 4 if rows % 4 == 0 else 1
    three = lambda shape: pl.BlockSpec(shape, lambda r: (r, 0, 0))
    return pl.pallas_call(
        functools.partial(inverse_kernel, factor=factor),
        grid=(rows // block,),
        in_specs=[
            pl.BlockSpec(memory_space=pltpu.SMEM),
            three((block, degrees, half_lat)),
            three((block, half_lat, width)),
            three((block, half_lat, width)),
            three((block, degrees, width)),
            pl.BlockSpec((1, width), lambda r: (0, 0)),
        ],
        out_specs=three((block, degrees, width)),
        out_shape=jax.ShapeDtypeStruct((rows, degrees, width), jnp.float32),
        cost_estimate=pl.CostEstimate(
            flops=4 * rows * degrees * half_lat * width,
            transcendentals=0,
            bytes_accessed=rows * (degrees * half_lat * 2 + half_lat * width * 4 + degrees * width * 6),
        ),
    )(wave_own, lat_basis, north, south, spectral, damp_all[None, :])


def on_device(spectral, lat_basis, block_order, in_weight, in_bias, out_weight, col_gain, damping):
    devices = lax.axis_size("lat")
    my_index = lax.axis_index("lat")
    row_count = spectral.shape[0]
    degrees = spectral.shape[1]
    chan_width = spectral.shape[2]
    chan_count = chan_width // 2
    half_lat = lat_basis.shape[2]
    lat_total = 2 * half_lat
    half_local = half_lat // devices
    wave_total = row_count * devices
    wave_all = wavenumbers(block_order, wave_total)
    wave_own = lax.dynamic_slice_in_dim(wave_all, my_index * row_count, row_count)
    degree = jnp.arange(degrees, dtype=jnp.int32)
    inside = degree[None, :] >= wave_own[:, None]
    parity = jnp.where((degree[None, :] + wave_own[:, None]) % 2 == 0, 1.0, -1.0).astype(
        jnp.float32
    )
    masked = jnp.where(inside[:, :, None], spectral, jnp.zeros_like(spectral))
    flipped = jnp.where(parity[:, :, None] > 0, masked, -masked)
    wave_table = lon_table(wave_all)
    j_ids = my_index * half_local + jnp.arange(half_local, dtype=jnp.int32)
    weight_north = lat_weights_of(j_ids, lat_total)
    weight_south = lat_weights_of(lat_total - 1 - j_ids, lat_total)
    j_all = jnp.arange(half_lat, dtype=jnp.int32)
    weight_all = lat_weights_of(jnp.arange(lat_total, dtype=jnp.int32), lat_total)
    real_coef = jnp.where(wave_own == 0, float(NLON), NLON / 2.0)
    imag_coef = jnp.where(wave_own == 0, 0.0, NLON / 2.0)

    def hemisphere(values, lat_weight):
        fourier = jnp.einsum(
            "rnj,rnc->jrc", lat_basis, values, preferred_element_type=jnp.float32
        ).astype(jnp.bfloat16)
        wide = fourier.astype(jnp.float32)
        per_lat = jnp.sum(
            real_coef[None, :, None] * wide[:, :, :chan_count] ** 2
            + imag_coef[None, :, None] * wide[:, :, chan_count:] ** 2,
            axis=1,
        )
        part = jnp.sum(lat_weight[:, None] * per_lat, axis=0)
        return fourier.reshape(devices, half_local, row_count, chan_width), part

    out_north, part_north = hemisphere(masked, lat_weights_of(j_all, lat_total))
    out_south, part_south = hemisphere(flipped, lat_weights_of(lat_total - 1 - j_all, lat_total))
    partial_value = part_north + part_south
    hi = partial_value.astype(jnp.bfloat16)
    rest = partial_value - hi.astype(jnp.float32)
    mid = rest.astype(jnp.bfloat16)
    lo = (rest - mid.astype(jnp.float32)).astype(jnp.bfloat16)
    pieces = jnp.concatenate(
        [
            jnp.concatenate([hi, mid])[None],
            jnp.concatenate([lo, jnp.zeros_like(lo)])[None],
            jnp.zeros((row_count - 2, chan_width), jnp.bfloat16),
        ]
    )
    slot = jnp.broadcast_to(pieces[None, None], (devices, 1, row_count, chan_width))
    north_in = lax.all_to_all(
        jnp.concatenate([out_north, slot], axis=1), "lat", split_axis=0, concat_axis=0, tiled=True
    )
    got = north_in[:, half_local, :2].astype(jnp.float32)
    global_sum = jnp.sum(got[:, 0, :chan_count] + got[:, 0, chan_count:] + got[:, 1, :chan_count], axis=0)
    variance = global_sum / (NLON * jnp.sum(weight_all))
    col_scale = col_gain * lax.rsqrt(variance + 1e-05)

    def round_trip(rows_in, lat_weight):
        weighted_local = column_network(
            lat_weight, rows_in, col_scale, in_weight, in_bias, out_weight, wave_table
        )
        returning = weighted_local.reshape(half_local, devices, row_count, chan_width)
        back = lax.all_to_all(returning, "lat", split_axis=1, concat_axis=1, tiled=True)
        return back.transpose(2, 1, 0, 3).reshape(row_count, half_lat, chan_width)

    out_south, wave_table, col_scale, north_in = lax.optimization_barrier(
        (out_south, wave_table, col_scale, north_in)
    )
    north = round_trip(north_in, weight_north)
    south_in = lax.all_to_all(out_south, "lat", split_axis=0, concat_axis=0, tiled=True)
    south = round_trip(south_in, weight_south)
    factor = 2.0 * math.sqrt(degrees * wave_total / lat_total)
    damp_all = jnp.concatenate([damping, damping])
    return inverse_legendre(wave_own, lat_basis, north, south, spectral, damp_all, factor)


def solution(mesh):
    in_specs = (
        P(("member", "lat"), None, None),
        P("lat", None, None),
        P(),
        P(),
        P(),
        P(),
        P(),
        P(),
    )
    out_specs = P(("member", "lat"), None, None)
    return jax.shard_map(
        on_device, mesh=mesh, in_specs=in_specs, out_specs=out_specs, check_vma=False
    )
```

```python
import functools
import math

import jax
import jax.numpy as jnp
from jax import lax
from jax.experimental import pallas as pl
from jax.experimental.pallas import tpu as pltpu
from jax.sharding import PartitionSpec as P

NN = 512
NLON = 1536
MB = 4
LON_TILE = 512


def wavenumbers(block_order, slot_count):
    slot_ids = jnp.arange(slot_count, dtype=jnp.int32)
    blocks = block_order.shape[0]
    matches = (slot_ids // MB)[:, None] == jnp.arange(blocks, dtype=jnp.int32)[None, :]
    chosen = jnp.sum(jnp.where(matches, block_order[None, :], 0), axis=1)
    return chosen * MB + slot_ids % MB


def lon_table(wave_all):
    longitude = jnp.arange(NLON, dtype=jnp.int32)
    phase_index = wave_all[:, None] * longitude[None, :] % NLON
    angles = phase_index.astype(jnp.float32) * (2.0 * math.pi / NLON)
    return jnp.concatenate([jnp.cos(angles), jnp.sin(angles)], axis=0).astype(jnp.bfloat16)


def lat_weights_of(latitude_index, lat_total):
    latitude = latitude_index.astype(jnp.float32)
    return jnp.cos(math.pi * ((latitude + 0.5) / lat_total - 0.5))


def column_kernel(
    weight_ref, rows_ref, scale_ref, in_w_ref, bias_ref, out_w_ref,
    table_ref, o_ref,
):
    j = pl.program_id(0)
    sources, _, rows_per, width = rows_ref.shape
    chan = width // 2
    waves = table_ref.shape[0] // 2
    rows = rows_ref[:, 0].astype(jnp.float32).reshape(sources * rows_per, width)
    rows = rows.astype(jnp.bfloat16)
    real = rows[:, :chan]
    imag = rows[:, chan:]
    scale = scale_ref[...]
    acc = jnp.zeros((2 * waves, chan), jnp.float32)
    for c in range(NLON // LON_TILE):
        lo = c * LON_TILE
        first_dims = (((0,), (0,)), ((), ()))
        wide = lax.dot_general(
            table_ref[:waves, lo:lo + LON_TILE], real, first_dims,
            preferred_element_type=jnp.float32,
        )
        wide = wide - lax.dot_general(
            table_ref[waves:, lo:lo + LON_TILE], imag, first_dims,
            preferred_element_type=jnp.float32,
        )
        g = wide.astype(jnp.bfloat16).astype(jnp.float32)
        normed = (g * scale).astype(jnp.bfloat16)
        pre = jnp.dot(normed, in_w_ref[...], preferred_element_type=jnp.float32) + bias_ref[...]
        hidden = jax.nn.gelu(pre).astype(jnp.bfloat16)
        col = jnp.dot(hidden, out_w_ref[...], preferred_element_type=jnp.float32).astype(
            jnp.bfloat16
        )
        acc = acc + jnp.dot(
            table_ref[:, lo:lo + LON_TILE], col, preferred_element_type=jnp.float32
        )
    inv_root = 1.0 / math.sqrt(NLON)
    w = weight_ref[j]
    cos_part = (acc[:waves] * inv_root).astype(jnp.bfloat16).astype(jnp.float32)
    sin_part = ((-acc[waves:]) * inv_root).astype(jnp.bfloat16).astype(jnp.float32)
    o_ref[0, :, :chan] = (w * cos_part).astype(jnp.bfloat16)
    o_ref[0, :, chan:] = (w * sin_part).astype(jnp.bfloat16)


def column_network(
    lat_w, rows_in, col_scale, in_weight, in_bias, out_weight, wave_table
):
    sources, _, rows_per, width = rows_in.shape
    lat_local = lat_w.shape[0]
    chan = width // 2
    waves = sources * rows_per
    nlon = wave_table.shape[1]
    hid = in_weight.shape[1]
    two_waves = wave_table.shape[0]
    full = lambda shape: pl.BlockSpec(shape, lambda j: (0,) * len(shape))
    return pl.pallas_call(
        column_kernel,
        grid=(lat_local,),
        in_specs=[
            pl.BlockSpec(memory_space=pltpu.SMEM),
            pl.BlockSpec((sources, 1, rows_per, width), lambda j: (0, j, 0, 0)),
            full((1, chan)),
            full((chan, hid)),
            full((1, hid)),
            full((hid, chan)),
            full((two_waves, nlon)),
        ],
        out_specs=pl.BlockSpec((1, two_waves // 2, 2 * chan), lambda j: (j, 0, 0)),
        out_shape=jax.ShapeDtypeStruct((lat_local, two_waves // 2, 2 * chan), jnp.bfloat16),
        compiler_params=pltpu.CompilerParams(vmem_limit_bytes=48 * 1024 * 1024),
        cost_estimate=pl.CostEstimate(
            flops=2 * lat_local * nlon * (2 * hid * chan + two_waves * chan + waves * width),
            transcendentals=lat_local * nlon * hid,
            bytes_accessed=2 * two_waves * nlon + lat_local * (waves * width * 2 + two_waves * chan * 2),
        ),
    )(
        lat_w,
        rows_in,
        col_scale[None, :],
        in_weight,
        in_bias[None, :],
        out_weight,
        wave_table,
    )


def inverse_kernel(wave_ref, basis_ref, north_ref, south_ref, spec_ref, damp_ref, o_ref, *, factor):
    block = basis_ref.shape[0]
    degrees = basis_ref.shape[1]
    n = lax.broadcasted_iota(jnp.int32, (degrees, 1), 0)
    wave_factor = (n * (n + 1)).astype(jnp.float32) / (NN * NN)
    for b in range(block):
        m = wave_ref[pl.program_id(0) * block + b]
        basis = basis_ref[b]
        east = jnp.dot(basis, north_ref[b], preferred_element_type=jnp.float32)
        west = jnp.dot(basis, south_ref[b], preferred_element_type=jnp.float32)
        parity = jnp.where((n + m) % 2 == 0, 1.0, -1.0).astype(jnp.float32)
        legendre = factor * (east + parity * west)
        damped = legendre - damp_ref[...] * wave_factor * spec_ref[b].astype(jnp.float32)
        o_ref[b] = jnp.where(n >= m, damped, 0.0)


def inverse_legendre(wave_own, lat_basis, north, south, spectral, damp_all, factor):
    rows, degrees, half_lat = lat_basis.shape
    width = spectral.shape[2]
    block = 4 if rows % 4 == 0 else 1
    three = lambda shape: pl.BlockSpec(shape, lambda r: (r, 0, 0))
    return pl.pallas_call(
        functools.partial(inverse_kernel, factor=factor),
        grid=(rows // block,),
        in_specs=[
            pl.BlockSpec(memory_space=pltpu.SMEM),
            three((block, degrees, half_lat)),
            three((block, half_lat, width)),
            three((block, half_lat, width)),
            three((block, degrees, width)),
            pl.BlockSpec((1, width), lambda r: (0, 0)),
        ],
        out_specs=three((block, degrees, width)),
        out_shape=jax.ShapeDtypeStruct((rows, degrees, width), jnp.float32),
        cost_estimate=pl.CostEstimate(
            flops=4 * rows * degrees * half_lat * width,
            transcendentals=0,
            bytes_accessed=rows * (degrees * half_lat * 2 + half_lat * width * 4 + degrees * width * 6),
        ),
    )(wave_own, lat_basis, north, south, spectral, damp_all[None, :])


def on_device(spectral, lat_basis, block_order, in_weight, in_bias, out_weight, col_gain, damping):
    devices = lax.axis_size("lat")
    my_index = lax.axis_index("lat")
    row_count = spectral.shape[0]
    degrees = spectral.shape[1]
    chan_width = spectral.shape[2]
    chan_count = chan_width // 2
    half_lat = lat_basis.shape[2]
    lat_total = 2 * half_lat
    half_local = half_lat // devices
    wave_total = row_count * devices
    wave_all = wavenumbers(block_order, wave_total)
    wave_own = lax.dynamic_slice_in_dim(wave_all, my_index * row_count, row_count)
    degree = jnp.arange(degrees, dtype=jnp.int32)
    inside = degree[None, :] >= wave_own[:, None]
    parity = jnp.where((degree[None, :] + wave_own[:, None]) % 2 == 0, 1.0, -1.0).astype(
        jnp.float32
    )
    masked = jnp.where(inside[:, :, None], spectral, jnp.zeros_like(spectral))
    flipped = jnp.where(parity[:, :, None] > 0, masked, -masked)
    wave_table = lon_table(wave_all)
    j_ids = my_index * half_local + jnp.arange(half_local, dtype=jnp.int32)
    weight_north = lat_weights_of(j_ids, lat_total)
    weight_south = lat_weights_of(lat_total - 1 - j_ids, lat_total)
    j_all = jnp.arange(half_lat, dtype=jnp.int32)
    weight_all = lat_weights_of(jnp.arange(lat_total, dtype=jnp.int32), lat_total)
    real_coef = jnp.where(wave_own == 0, float(NLON), NLON / 2.0)
    imag_coef = jnp.where(wave_own == 0, 0.0, NLON / 2.0)

    def hemisphere(values, lat_weight):
        fourier = jnp.einsum(
            "rnj,rnc->jrc", lat_basis, values, preferred_element_type=jnp.float32
        ).astype(jnp.bfloat16)
        wide = fourier.astype(jnp.float32)
        per_lat = jnp.sum(
            real_coef[None, :, None] * wide[:, :, :chan_count] ** 2
            + imag_coef[None, :, None] * wide[:, :, chan_count:] ** 2,
            axis=1,
        )
        part = jnp.sum(lat_weight[:, None] * per_lat, axis=0)
        return fourier.reshape(devices, half_local, row_count, chan_width), part

    out_north, part_north = hemisphere(masked, lat_weights_of(j_all, lat_total))
    out_south, part_south = hemisphere(flipped, lat_weights_of(lat_total - 1 - j_all, lat_total))
    partial_value = part_north + part_south
    hi = partial_value.astype(jnp.bfloat16)
    rest = partial_value - hi.astype(jnp.float32)
    mid = rest.astype(jnp.bfloat16)
    lo = (rest - mid.astype(jnp.float32)).astype(jnp.bfloat16)
    pieces = jnp.concatenate([hi, mid, lo])
    flat = half_local * row_count * chan_width
    send = jnp.concatenate(
        [
            out_north.reshape(devices, flat),
            jnp.broadcast_to(pieces[None], (devices, 3 * chan_count)),
        ],
        axis=1,
    )
    got = lax.all_to_all(send, "lat", split_axis=0, concat_axis=0, tiled=True)
    north_in = got[:, :flat].reshape(devices, half_local, row_count, chan_width)
    got = got[:, flat:].astype(jnp.float32)
    global_sum = jnp.sum(
        got[:, :chan_count] + got[:, chan_count:2 * chan_count] + got[:, 2 * chan_count:], axis=0
    )
    variance = global_sum / (NLON * jnp.sum(weight_all))
    col_scale = col_gain * lax.rsqrt(variance + 1e-05)

    def round_trip(rows_in, lat_weight):
        weighted_local = column_network(
            lat_weight, rows_in, col_scale, in_weight, in_bias, out_weight, wave_table
        )
        returning = weighted_local.reshape(half_local, devices, row_count, chan_width)
        back = lax.all_to_all(returning, "lat", split_axis=1, concat_axis=1, tiled=True)
        return back.transpose(2, 1, 0, 3).reshape(row_count, half_lat, chan_width)

    out_south, wave_table, col_scale = lax.optimization_barrier(
        (out_south, wave_table, col_scale)
    )
    north = round_trip(north_in, weight_north)
    south_in = lax.all_to_all(out_south, "lat", split_axis=0, concat_axis=0, tiled=True)
    south = round_trip(south_in, weight_south)
    factor = 2.0 * math.sqrt(degrees * wave_total / lat_total)
    damp_all = jnp.concatenate([damping, damping])
    return inverse_legendre(wave_own, lat_basis, north, south, spectral, damp_all, factor)


def solution(mesh):
    in_specs = (
        P(("member", "lat"), None, None),
        P("lat", None, None),
        P(),
        P(),
        P(),
        P(),
        P(),
        P(),
    )
    out_specs = P(("member", "lat"), None, None)
    return jax.shard_map(
        on_device, mesh=mesh, in_specs=in_specs, out_specs=out_specs, check_vma=False
    )
```

```python
import functools
import math

import jax
import jax.numpy as jnp
from jax import lax
from jax.experimental import pallas as pl
from jax.experimental.pallas import tpu as pltpu
from jax.sharding import PartitionSpec as P

NN = 512
NLON = 1536
MB = 4
LON_TILE = 512


def wavenumbers(block_order, slot_count):
    slot_ids = jnp.arange(slot_count, dtype=jnp.int32)
    blocks = block_order.shape[0]
    matches = (slot_ids // MB)[:, None] == jnp.arange(blocks, dtype=jnp.int32)[None, :]
    chosen = jnp.sum(jnp.where(matches, block_order[None, :], 0), axis=1)
    return chosen * MB + slot_ids % MB


def lon_table(wave_all):
    longitude = jnp.arange(NLON, dtype=jnp.int32)
    phase_index = wave_all[:, None] * longitude[None, :] % NLON
    angles = phase_index.astype(jnp.float32) * (2.0 * math.pi / NLON)
    return jnp.concatenate([jnp.cos(angles), jnp.sin(angles)], axis=0).astype(jnp.bfloat16)


def lat_weights_of(latitude_index, lat_total):
    latitude = latitude_index.astype(jnp.float32)
    return jnp.cos(math.pi * ((latitude + 0.5) / lat_total - 0.5))


def column_kernel(
    weight_ref, rows_ref, scale_ref, in_w_ref, bias_ref, out_w_ref,
    table_ref, o_ref,
):
    j = pl.program_id(0)
    sources, _, rows_per, width = rows_ref.shape
    chan = width // 2
    waves = table_ref.shape[0] // 2
    rows = rows_ref[:, 0].astype(jnp.float32).reshape(sources * rows_per, width)
    rows = rows.astype(jnp.bfloat16)
    real = rows[:, :chan]
    imag = rows[:, chan:]
    scale = scale_ref[...]
    acc = jnp.zeros((2 * waves, chan), jnp.float32)
    for c in range(NLON // LON_TILE):
        lo = c * LON_TILE
        first_dims = (((0,), (0,)), ((), ()))
        wide = lax.dot_general(
            table_ref[:waves, lo:lo + LON_TILE], real, first_dims,
            preferred_element_type=jnp.float32,
        )
        wide = wide - lax.dot_general(
            table_ref[waves:, lo:lo + LON_TILE], imag, first_dims,
            preferred_element_type=jnp.float32,
        )
        g = wide.astype(jnp.bfloat16).astype(jnp.float32)
        normed = (g * scale).astype(jnp.bfloat16)
        pre = jnp.dot(normed, in_w_ref[...], preferred_element_type=jnp.float32) + bias_ref[...]
        hidden = jax.nn.gelu(pre).astype(jnp.bfloat16)
        col = jnp.dot(hidden, out_w_ref[...], preferred_element_type=jnp.float32).astype(
            jnp.bfloat16
        )
        acc = acc + jnp.dot(
            table_ref[:, lo:lo + LON_TILE], col, preferred_element_type=jnp.float32
        )
    inv_root = 1.0 / math.sqrt(NLON)
    w = weight_ref[j]
    cos_part = (acc[:waves] * inv_root).astype(jnp.bfloat16).astype(jnp.float32)
    sin_part = ((-acc[waves:]) * inv_root).astype(jnp.bfloat16).astype(jnp.float32)
    o_ref[0, :, :chan] = (w * cos_part).astype(jnp.bfloat16)
    o_ref[0, :, chan:] = (w * sin_part).astype(jnp.bfloat16)


def column_network(
    lat_w, rows_in, col_scale, in_weight, in_bias, out_weight, wave_table
):
    sources, _, rows_per, width = rows_in.shape
    lat_local = lat_w.shape[0]
    chan = width // 2
    waves = sources * rows_per
    nlon = wave_table.shape[1]
    hid = in_weight.shape[1]
    two_waves = wave_table.shape[0]
    full = lambda shape: pl.BlockSpec(shape, lambda j: (0,) * len(shape))
    return pl.pallas_call(
        column_kernel,
        grid=(lat_local,),
        in_specs=[
            pl.BlockSpec(memory_space=pltpu.SMEM),
            pl.BlockSpec((sources, 1, rows_per, width), lambda j: (0, j, 0, 0)),
            full((1, chan)),
            full((chan, hid)),
            full((1, hid)),
            full((hid, chan)),
            full((two_waves, nlon)),
        ],
        out_specs=pl.BlockSpec((1, two_waves // 2, 2 * chan), lambda j: (j, 0, 0)),
        out_shape=jax.ShapeDtypeStruct((lat_local, two_waves // 2, 2 * chan), jnp.bfloat16),
        compiler_params=pltpu.CompilerParams(vmem_limit_bytes=48 * 1024 * 1024),
        cost_estimate=pl.CostEstimate(
            flops=2 * lat_local * nlon * (2 * hid * chan + two_waves * chan + waves * width),
            transcendentals=lat_local * nlon * hid,
            bytes_accessed=2 * two_waves * nlon + lat_local * (waves * width * 2 + two_waves * chan * 2),
        ),
    )(
        lat_w,
        rows_in,
        col_scale[None, :],
        in_weight,
        in_bias[None, :],
        out_weight,
        wave_table,
    )


def inverse_kernel(wave_ref, basis_ref, north_ref, south_ref, spec_ref, damp_ref, o_ref, *, factor):
    block = basis_ref.shape[0]
    degrees = basis_ref.shape[1]
    n = lax.broadcasted_iota(jnp.int32, (degrees, 1), 0)
    wave_factor = (n * (n + 1)).astype(jnp.float32) / (NN * NN)
    for b in range(block):
        m = wave_ref[pl.program_id(0) * block + b]
        basis = basis_ref[b]
        east = jnp.dot(basis, north_ref[b], preferred_element_type=jnp.float32)
        west = jnp.dot(basis, south_ref[b], preferred_element_type=jnp.float32)
        parity = jnp.where((n + m) % 2 == 0, 1.0, -1.0).astype(jnp.float32)
        legendre = factor * (east + parity * west)
        damped = legendre - damp_ref[...] * wave_factor * spec_ref[b].astype(jnp.float32)
        o_ref[b] = jnp.where(n >= m, damped, 0.0)


def inverse_legendre(wave_own, lat_basis, north, south, spectral, damp_all, factor):
    rows, degrees, half_lat = lat_basis.shape
    width = spectral.shape[2]
    block = 8 if rows % 8 == 0 else 1
    three = lambda shape: pl.BlockSpec(shape, lambda r: (r, 0, 0))
    return pl.pallas_call(
        functools.partial(inverse_kernel, factor=factor),
        grid=(rows // block,),
        in_specs=[
            pl.BlockSpec(memory_space=pltpu.SMEM),
            three((block, degrees, half_lat)),
            three((block, half_lat, width)),
            three((block, half_lat, width)),
            three((block, degrees, width)),
            pl.BlockSpec((1, width), lambda r: (0, 0)),
        ],
        out_specs=three((block, degrees, width)),
        out_shape=jax.ShapeDtypeStruct((rows, degrees, width), jnp.float32),
        cost_estimate=pl.CostEstimate(
            flops=4 * rows * degrees * half_lat * width,
            transcendentals=0,
            bytes_accessed=rows * (degrees * half_lat * 2 + half_lat * width * 4 + degrees * width * 6),
        ),
    )(wave_own, lat_basis, north, south, spectral, damp_all[None, :])


def on_device(spectral, lat_basis, block_order, in_weight, in_bias, out_weight, col_gain, damping):
    devices = lax.axis_size("lat")
    my_index = lax.axis_index("lat")
    row_count = spectral.shape[0]
    degrees = spectral.shape[1]
    chan_width = spectral.shape[2]
    chan_count = chan_width // 2
    half_lat = lat_basis.shape[2]
    lat_total = 2 * half_lat
    half_local = half_lat // devices
    wave_total = row_count * devices
    wave_all = wavenumbers(block_order, wave_total)
    wave_own = lax.dynamic_slice_in_dim(wave_all, my_index * row_count, row_count)
    degree = jnp.arange(degrees, dtype=jnp.int32)
    inside = degree[None, :] >= wave_own[:, None]
    parity = jnp.where((degree[None, :] + wave_own[:, None]) % 2 == 0, 1.0, -1.0).astype(
        jnp.float32
    )
    masked = jnp.where(inside[:, :, None], spectral, jnp.zeros_like(spectral))
    flipped = jnp.where(parity[:, :, None] > 0, masked, -masked)
    wave_table = lon_table(wave_all)
    j_ids = my_index * half_local + jnp.arange(half_local, dtype=jnp.int32)
    weight_north = lat_weights_of(j_ids, lat_total)
    weight_south = lat_weights_of(lat_total - 1 - j_ids, lat_total)
    j_all = jnp.arange(half_lat, dtype=jnp.int32)
    weight_all = lat_weights_of(jnp.arange(lat_total, dtype=jnp.int32), lat_total)
    real_coef = jnp.where(wave_own == 0, float(NLON), NLON / 2.0)
    imag_coef = jnp.where(wave_own == 0, 0.0, NLON / 2.0)

    def hemisphere(values, lat_weight):
        fourier = jnp.einsum(
            "rnj,rnc->jrc", lat_basis, values, preferred_element_type=jnp.float32
        ).astype(jnp.bfloat16)
        wide = fourier.astype(jnp.float32)
        per_lat = jnp.sum(
            real_coef[None, :, None] * wide[:, :, :chan_count] ** 2
            + imag_coef[None, :, None] * wide[:, :, chan_count:] ** 2,
            axis=1,
        )
        part = jnp.sum(lat_weight[:, None] * per_lat, axis=0)
        return fourier.reshape(devices, half_local, row_count, chan_width), part

    out_north, part_north = hemisphere(masked, lat_weights_of(j_all, lat_total))
    out_south, part_south = hemisphere(flipped, lat_weights_of(lat_total - 1 - j_all, lat_total))
    partial_value = part_north + part_south
    hi = partial_value.astype(jnp.bfloat16)
    rest = partial_value - hi.astype(jnp.float32)
    mid = rest.astype(jnp.bfloat16)
    lo = (rest - mid.astype(jnp.float32)).astype(jnp.bfloat16)
    pieces = jnp.concatenate(
        [
            jnp.concatenate([hi, mid])[None],
            jnp.concatenate([lo, jnp.zeros_like(lo)])[None],
            jnp.zeros((row_count - 2, chan_width), jnp.bfloat16),
        ]
    )
    slot = jnp.broadcast_to(pieces[None, None], (devices, 1, row_count, chan_width))
    north_in = lax.all_to_all(
        jnp.concatenate([out_north, slot], axis=1), "lat", split_axis=0, concat_axis=0, tiled=True
    )
    got = north_in[:, half_local, :2].astype(jnp.float32)
    global_sum = jnp.sum(got[:, 0, :chan_count] + got[:, 0, chan_count:] + got[:, 1, :chan_count], axis=0)
    variance = global_sum / (NLON * jnp.sum(weight_all))
    col_scale = col_gain * lax.rsqrt(variance + 1e-05)

    def round_trip(rows_in, lat_weight):
        weighted_local = column_network(
            lat_weight, rows_in, col_scale, in_weight, in_bias, out_weight, wave_table
        )
        returning = weighted_local.reshape(half_local, devices, row_count, chan_width)
        back = lax.all_to_all(returning, "lat", split_axis=1, concat_axis=1, tiled=True)
        return back.transpose(2, 1, 0, 3).reshape(row_count, half_lat, chan_width)

    out_south, wave_table, col_scale, north_in = lax.optimization_barrier(
        (out_south, wave_table, col_scale, north_in)
    )
    north = round_trip(north_in, weight_north)
    south_in = lax.all_to_all(out_south, "lat", split_axis=0, concat_axis=0, tiled=True)
    south = round_trip(south_in, weight_south)
    factor = 2.0 * math.sqrt(degrees * wave_total / lat_total)
    damp_all = jnp.concatenate([damping, damping])
    return inverse_legendre(wave_own, lat_basis, north, south, spectral, damp_all, factor)


def solution(mesh):
    in_specs = (
        P(("member", "lat"), None, None),
        P("lat", None, None),
        P(),
        P(),
        P(),
        P(),
        P(),
        P(),
    )
    out_specs = P(("member", "lat"), None, None)
    return jax.shard_map(
        on_device, mesh=mesh, in_specs=in_specs, out_specs=out_specs, check_vma=False
    )
```

```python
import functools
import math

import jax
import jax.numpy as jnp
from jax import lax
from jax.experimental import pallas as pl
from jax.experimental.pallas import tpu as pltpu
from jax.sharding import PartitionSpec as P

NN = 512
NLON = 1536
MB = 4
LON_TILE = 512


def wavenumbers(block_order, slot_count):
    slot_ids = jnp.arange(slot_count, dtype=jnp.int32)
    blocks = block_order.shape[0]
    matches = (slot_ids // MB)[:, None] == jnp.arange(blocks, dtype=jnp.int32)[None, :]
    chosen = jnp.sum(jnp.where(matches, block_order[None, :], 0), axis=1)
    return chosen * MB + slot_ids % MB


def lon_table(wave_all):
    longitude = jnp.arange(NLON, dtype=jnp.int32)
    phase_index = wave_all[:, None] * longitude[None, :] % NLON
    angles = phase_index.astype(jnp.float32) * (2.0 * math.pi / NLON)
    return jnp.concatenate([jnp.cos(angles), jnp.sin(angles)], axis=0).astype(jnp.bfloat16)


def lat_weights_of(latitude_index, lat_total):
    latitude = latitude_index.astype(jnp.float32)
    return jnp.cos(math.pi * ((latitude + 0.5) / lat_total - 0.5))


def column_kernel(
    weight_ref, rows_ref, scale_ref, in_w_ref, bias_ref, out_w_ref,
    table_ref, o_ref,
):
    j = pl.program_id(0)
    sources, _, rows_per, width = rows_ref.shape
    chan = width // 2
    waves = table_ref.shape[0] // 2
    rows = rows_ref[:, 0].astype(jnp.float32).reshape(sources * rows_per, width)
    rows = rows.astype(jnp.bfloat16)
    real = rows[:, :chan]
    imag = rows[:, chan:]
    scale = scale_ref[...]
    acc = jnp.zeros((2 * waves, chan), jnp.float32)
    for c in range(NLON // LON_TILE):
        lo = c * LON_TILE
        first_dims = (((0,), (0,)), ((), ()))
        wide = lax.dot_general(
            table_ref[:waves, lo:lo + LON_TILE], real, first_dims,
            preferred_element_type=jnp.float32,
        )
        wide = wide - lax.dot_general(
            table_ref[waves:, lo:lo + LON_TILE], imag, first_dims,
            preferred_element_type=jnp.float32,
        )
        g = wide.astype(jnp.bfloat16).astype(jnp.float32)
        normed = (g * scale).astype(jnp.bfloat16)
        pre = jnp.dot(normed, in_w_ref[...], preferred_element_type=jnp.float32) + bias_ref[...]
        hidden = jax.nn.gelu(pre).astype(jnp.bfloat16)
        col = jnp.dot(hidden, out_w_ref[...], preferred_element_type=jnp.float32).astype(
            jnp.bfloat16
        )
        acc = acc + jnp.dot(
            table_ref[:, lo:lo + LON_TILE], col, preferred_element_type=jnp.float32
        )
    inv_root = 1.0 / math.sqrt(NLON)
    w = weight_ref[j]
    cos_part = (acc[:waves] * inv_root).astype(jnp.bfloat16).astype(jnp.float32)
    sin_part = ((-acc[waves:]) * inv_root).astype(jnp.bfloat16).astype(jnp.float32)
    o_ref[0, :, :chan] = (w * cos_part).astype(jnp.bfloat16)
    o_ref[0, :, chan:] = (w * sin_part).astype(jnp.bfloat16)


def column_network(
    lat_w, rows_in, col_scale, in_weight, in_bias, out_weight, wave_table
):
    sources, _, rows_per, width = rows_in.shape
    lat_local = lat_w.shape[0]
    chan = width // 2
    waves = sources * rows_per
    nlon = wave_table.shape[1]
    hid = in_weight.shape[1]
    two_waves = wave_table.shape[0]
    full = lambda shape: pl.BlockSpec(shape, lambda j: (0,) * len(shape))
    return pl.pallas_call(
        column_kernel,
        grid=(lat_local,),
        in_specs=[
            pl.BlockSpec(memory_space=pltpu.SMEM),
            pl.BlockSpec((sources, 1, rows_per, width), lambda j: (0, j, 0, 0)),
            full((1, chan)),
            full((chan, hid)),
            full((1, hid)),
            full((hid, chan)),
            full((two_waves, nlon)),
        ],
        out_specs=pl.BlockSpec((1, two_waves // 2, 2 * chan), lambda j: (j, 0, 0)),
        out_shape=jax.ShapeDtypeStruct((lat_local, two_waves // 2, 2 * chan), jnp.bfloat16),
        compiler_params=pltpu.CompilerParams(vmem_limit_bytes=48 * 1024 * 1024),
        cost_estimate=pl.CostEstimate(
            flops=2 * lat_local * nlon * (2 * hid * chan + two_waves * chan + waves * width),
            transcendentals=lat_local * nlon * hid,
            bytes_accessed=2 * two_waves * nlon + lat_local * (waves * width * 2 + two_waves * chan * 2),
        ),
    )(
        lat_w,
        rows_in,
        col_scale[None, :],
        in_weight,
        in_bias[None, :],
        out_weight,
        wave_table,
    )


def inverse_kernel(wave_ref, basis_ref, north_ref, south_ref, spec_ref, damp_ref, o_ref, *, factor):
    block = basis_ref.shape[0]
    degrees = basis_ref.shape[1]
    n = lax.broadcasted_iota(jnp.int32, (degrees, 1), 0)
    wave_factor = (n * (n + 1)).astype(jnp.float32) / (NN * NN)
    for b in range(block):
        m = wave_ref[pl.program_id(0) * block + b]
        basis = basis_ref[b]
        east = jnp.dot(basis, north_ref[b], preferred_element_type=jnp.float32)
        west = jnp.dot(basis, south_ref[b], preferred_element_type=jnp.float32)
        parity = jnp.where((n + m) % 2 == 0, 1.0, -1.0).astype(jnp.float32)
        legendre = factor * (east + parity * west)
        damped = legendre - damp_ref[...] * wave_factor * spec_ref[b].astype(jnp.float32)
        o_ref[b] = jnp.where(n >= m, damped, 0.0)


def inverse_legendre(wave_own, lat_basis, north, south, spectral, damp_all, factor):
    rows, degrees, half_lat = lat_basis.shape
    width = spectral.shape[2]
    block = 8 if rows % 8 == 0 else 1
    three = lambda shape: pl.BlockSpec(shape, lambda r: (r, 0, 0))
    return pl.pallas_call(
        functools.partial(inverse_kernel, factor=factor),
        grid=(rows // block,),
        in_specs=[
            pl.BlockSpec(memory_space=pltpu.SMEM),
            three((block, degrees, half_lat)),
            three((block, half_lat, width)),
            three((block, half_lat, width)),
            three((block, degrees, width)),
            pl.BlockSpec((1, width), lambda r: (0, 0)),
        ],
        out_specs=three((block, degrees, width)),
        out_shape=jax.ShapeDtypeStruct((rows, degrees, width), jnp.float32),
        cost_estimate=pl.CostEstimate(
            flops=4 * rows * degrees * half_lat * width,
            transcendentals=0,
            bytes_accessed=rows * (degrees * half_lat * 2 + half_lat * width * 4 + degrees * width * 6),
        ),
    )(wave_own, lat_basis, north, south, spectral, damp_all[None, :])


def on_device(spectral, lat_basis, block_order, in_weight, in_bias, out_weight, col_gain, damping):
    devices = lax.axis_size("lat")
    my_index = lax.axis_index("lat")
    row_count = spectral.shape[0]
    degrees = spectral.shape[1]
    chan_width = spectral.shape[2]
    chan_count = chan_width // 2
    half_lat = lat_basis.shape[2]
    lat_total = 2 * half_lat
    half_local = half_lat // devices
    wave_total = row_count * devices
    wave_all = wavenumbers(block_order, wave_total)
    wave_own = lax.dynamic_slice_in_dim(wave_all, my_index * row_count, row_count)
    degree = jnp.arange(degrees, dtype=jnp.int32)
    inside = degree[None, :] >= wave_own[:, None]
    parity = jnp.where((degree[None, :] + wave_own[:, None]) % 2 == 0, 1.0, -1.0).astype(
        jnp.float32
    )
    masked = jnp.where(inside[:, :, None], spectral, jnp.zeros_like(spectral))
    flipped = jnp.where(parity[:, :, None] > 0, masked, -masked)
    wave_table = lon_table(wave_all)
    j_ids = my_index * half_local + jnp.arange(half_local, dtype=jnp.int32)
    weight_north = lat_weights_of(j_ids, lat_total)
    weight_south = lat_weights_of(lat_total - 1 - j_ids, lat_total)
    j_all = jnp.arange(half_lat, dtype=jnp.int32)
    weight_all = lat_weights_of(jnp.arange(lat_total, dtype=jnp.int32), lat_total)
    real_coef = jnp.where(wave_own == 0, float(NLON), NLON / 2.0)
    imag_coef = jnp.where(wave_own == 0, 0.0, NLON / 2.0)

    def hemisphere(values, lat_weight):
        fourier = jnp.einsum(
            "rnj,rnc->jrc", lat_basis, values, preferred_element_type=jnp.float32
        ).astype(jnp.bfloat16)
        fourier = lax.optimization_barrier(fourier)
        wide = fourier.astype(jnp.float32)
        per_lat = jnp.sum(
            real_coef[None, :, None] * wide[:, :, :chan_count] ** 2
            + imag_coef[None, :, None] * wide[:, :, chan_count:] ** 2,
            axis=1,
        )
        part = jnp.sum(lat_weight[:, None] * per_lat, axis=0)
        return fourier.reshape(devices, half_local, row_count, chan_width), part

    out_north, part_north = hemisphere(masked, lat_weights_of(j_all, lat_total))
    out_south, part_south = hemisphere(flipped, lat_weights_of(lat_total - 1 - j_all, lat_total))
    partial_value = part_north + part_south
    hi = partial_value.astype(jnp.bfloat16)
    rest = partial_value - hi.astype(jnp.float32)
    mid = rest.astype(jnp.bfloat16)
    lo = (rest - mid.astype(jnp.float32)).astype(jnp.bfloat16)
    pieces = jnp.concatenate(
        [
            jnp.concatenate([hi, mid])[None],
            jnp.concatenate([lo, jnp.zeros_like(lo)])[None],
            jnp.zeros((row_count - 2, chan_width), jnp.bfloat16),
        ]
    )
    slot = jnp.broadcast_to(pieces[None, None], (devices, 1, row_count, chan_width))
    north_in = lax.all_to_all(
        jnp.concatenate([out_north, slot], axis=1), "lat", split_axis=0, concat_axis=0, tiled=True
    )
    got = north_in[:, half_local, :2].astype(jnp.float32)
    global_sum = jnp.sum(got[:, 0, :chan_count] + got[:, 0, chan_count:] + got[:, 1, :chan_count], axis=0)
    variance = global_sum / (NLON * jnp.sum(weight_all))
    col_scale = col_gain * lax.rsqrt(variance + 1e-05)

    def round_trip(rows_in, lat_weight):
        weighted_local = column_network(
            lat_weight, rows_in, col_scale, in_weight, in_bias, out_weight, wave_table
        )
        returning = weighted_local.reshape(half_local, devices, row_count, chan_width)
        back = lax.all_to_all(returning, "lat", split_axis=1, concat_axis=1, tiled=True)
        return back.transpose(2, 1, 0, 3).reshape(row_count, half_lat, chan_width)

    out_south, wave_table, col_scale, north_in = lax.optimization_barrier(
        (out_south, wave_table, col_scale, north_in)
    )
    north = round_trip(north_in, weight_north)
    south_in = lax.all_to_all(out_south, "lat", split_axis=0, concat_axis=0, tiled=True)
    south = round_trip(south_in, weight_south)
    factor = 2.0 * math.sqrt(degrees * wave_total / lat_total)
    damp_all = jnp.concatenate([damping, damping])
    return inverse_legendre(wave_own, lat_basis, north, south, spectral, damp_all, factor)


def solution(mesh):
    in_specs = (
        P(("member", "lat"), None, None),
        P("lat", None, None),
        P(),
        P(),
        P(),
        P(),
        P(),
        P(),
    )
    out_specs = P(("member", "lat"), None, None)
    return jax.shard_map(
        on_device, mesh=mesh, in_specs=in_specs, out_specs=out_specs, check_vma=False
    )
```

```python
import functools
import math

import jax
import jax.numpy as jnp
from jax import lax
from jax.experimental import pallas as pl
from jax.experimental.pallas import tpu as pltpu
from jax.sharding import PartitionSpec as P

NN = 512
NLON = 1536
MB = 4
LON_TILE = 512


def wavenumbers(block_order, slot_count):
    slot_ids = jnp.arange(slot_count, dtype=jnp.int32)
    blocks = block_order.shape[0]
    matches = (slot_ids // MB)[:, None] == jnp.arange(blocks, dtype=jnp.int32)[None, :]
    chosen = jnp.sum(jnp.where(matches, block_order[None, :], 0), axis=1)
    return chosen * MB + slot_ids % MB


def lon_table(wave_all):
    longitude = jnp.arange(NLON, dtype=jnp.int32)
    phase_index = wave_all[:, None] * longitude[None, :] % NLON
    angles = phase_index.astype(jnp.float32) * (2.0 * math.pi / NLON)
    return jnp.concatenate([jnp.cos(angles), jnp.sin(angles)], axis=0).astype(jnp.bfloat16)


def lat_weights_of(latitude_index, lat_total):
    latitude = latitude_index.astype(jnp.float32)
    return jnp.cos(math.pi * ((latitude + 0.5) / lat_total - 0.5))


def column_kernel(
    weight_ref, rows_ref, scale_ref, in_w_ref, bias_ref, out_w_ref,
    table_ref, o_ref,
):
    j = pl.program_id(0)
    sources, _, rows_per, width = rows_ref.shape
    chan = width // 2
    waves = table_ref.shape[0] // 2
    rows = rows_ref[:, 0].astype(jnp.float32).reshape(sources * rows_per, width)
    rows = rows.astype(jnp.bfloat16)
    real = rows[:, :chan]
    imag = rows[:, chan:]
    scale = scale_ref[...]
    acc = jnp.zeros((2 * waves, chan), jnp.float32)
    for c in range(NLON // LON_TILE):
        lo = c * LON_TILE
        first_dims = (((0,), (0,)), ((), ()))
        wide = lax.dot_general(
            table_ref[:waves, lo:lo + LON_TILE], real, first_dims,
            preferred_element_type=jnp.float32,
        )
        wide = wide - lax.dot_general(
            table_ref[waves:, lo:lo + LON_TILE], imag, first_dims,
            preferred_element_type=jnp.float32,
        )
        g = wide.astype(jnp.bfloat16).astype(jnp.float32)
        normed = (g * scale).astype(jnp.bfloat16)
        pre = jnp.dot(normed, in_w_ref[...], preferred_element_type=jnp.float32) + bias_ref[...]
        hidden = jax.nn.gelu(pre).astype(jnp.bfloat16)
        col = jnp.dot(hidden, out_w_ref[...], preferred_element_type=jnp.float32).astype(
            jnp.bfloat16
        )
        acc = acc + jnp.dot(
            table_ref[:, lo:lo + LON_TILE], col, preferred_element_type=jnp.float32
        )
    inv_root = 1.0 / math.sqrt(NLON)
    w = weight_ref[j]
    cos_part = (acc[:waves] * inv_root).astype(jnp.bfloat16).astype(jnp.float32)
    sin_part = ((-acc[waves:]) * inv_root).astype(jnp.bfloat16).astype(jnp.float32)
    o_ref[0, :, :chan] = (w * cos_part).astype(jnp.bfloat16)
    o_ref[0, :, chan:] = (w * sin_part).astype(jnp.bfloat16)


def column_network(
    lat_w, rows_in, col_scale, in_weight, in_bias, out_weight, wave_table
):
    sources, _, rows_per, width = rows_in.shape
    lat_local = lat_w.shape[0]
    chan = width // 2
    waves = sources * rows_per
    nlon = wave_table.shape[1]
    hid = in_weight.shape[1]
    two_waves = wave_table.shape[0]
    full = lambda shape: pl.BlockSpec(shape, lambda j: (0,) * len(shape))
    return pl.pallas_call(
        column_kernel,
        grid=(lat_local,),
        in_specs=[
            pl.BlockSpec(memory_space=pltpu.SMEM),
            pl.BlockSpec((sources, 1, rows_per, width), lambda j: (0, j, 0, 0)),
            full((1, chan)),
            full((chan, hid)),
            full((1, hid)),
            full((hid, chan)),
            full((two_waves, nlon)),
        ],
        out_specs=pl.BlockSpec((1, two_waves // 2, 2 * chan), lambda j: (j, 0, 0)),
        out_shape=jax.ShapeDtypeStruct((lat_local, two_waves // 2, 2 * chan), jnp.bfloat16),
        compiler_params=pltpu.CompilerParams(vmem_limit_bytes=48 * 1024 * 1024),
        cost_estimate=pl.CostEstimate(
            flops=2 * lat_local * nlon * (2 * hid * chan + two_waves * chan + waves * width),
            transcendentals=lat_local * nlon * hid,
            bytes_accessed=2 * two_waves * nlon + lat_local * (waves * width * 2 + two_waves * chan * 2),
        ),
    )(
        lat_w,
        rows_in,
        col_scale[None, :],
        in_weight,
        in_bias[None, :],
        out_weight,
        wave_table,
    )


def inverse_kernel(wave_ref, basis_ref, north_ref, south_ref, spec_ref, damp_ref, o_ref, *, factor):
    block = basis_ref.shape[0]
    degrees = basis_ref.shape[1]
    n = lax.broadcasted_iota(jnp.int32, (degrees, 1), 0)
    wave_factor = (n * (n + 1)).astype(jnp.float32) / (NN * NN)
    for b in range(block):
        m = wave_ref[pl.program_id(0) * block + b]
        basis = basis_ref[b]
        east = jnp.dot(basis, north_ref[b], preferred_element_type=jnp.float32)
        west = jnp.dot(basis, south_ref[b], preferred_element_type=jnp.float32)
        parity = jnp.where((n + m) % 2 == 0, 1.0, -1.0).astype(jnp.float32)
        legendre = factor * (east + parity * west)
        damped = legendre - damp_ref[...] * wave_factor * spec_ref[b].astype(jnp.float32)
        o_ref[b] = jnp.where(n >= m, damped, 0.0)


def inverse_legendre(wave_own, lat_basis, north, south, spectral, damp_all, factor):
    rows, degrees, half_lat = lat_basis.shape
    width = spectral.shape[2]
    block = 8 if rows % 8 == 0 else 1
    three = lambda shape: pl.BlockSpec(shape, lambda r: (r, 0, 0))
    return pl.pallas_call(
        functools.partial(inverse_kernel, factor=factor),
        grid=(rows // block,),
        in_specs=[
            pl.BlockSpec(memory_space=pltpu.SMEM),
            three((block, degrees, half_lat)),
            three((block, half_lat, width)),
            three((block, half_lat, width)),
            three((block, degrees, width)),
            pl.BlockSpec((1, width), lambda r: (0, 0)),
        ],
        out_specs=three((block, degrees, width)),
        out_shape=jax.ShapeDtypeStruct((rows, degrees, width), jnp.float32),
        cost_estimate=pl.CostEstimate(
            flops=4 * rows * degrees * half_lat * width,
            transcendentals=0,
            bytes_accessed=rows * (degrees * half_lat * 2 + half_lat * width * 4 + degrees * width * 6),
        ),
    )(wave_own, lat_basis, north, south, spectral, damp_all[None, :])


def on_device(spectral, lat_basis, block_order, in_weight, in_bias, out_weight, col_gain, damping):
    devices = lax.axis_size("lat")
    my_index = lax.axis_index("lat")
    row_count = spectral.shape[0]
    degrees = spectral.shape[1]
    chan_width = spectral.shape[2]
    chan_count = chan_width // 2
    half_lat = lat_basis.shape[2]
    lat_total = 2 * half_lat
    half_local = half_lat // devices
    wave_total = row_count * devices
    wave_all = wavenumbers(block_order, wave_total)
    wave_own = lax.dynamic_slice_in_dim(wave_all, my_index * row_count, row_count)
    degree = jnp.arange(degrees, dtype=jnp.int32)
    inside = degree[None, :] >= wave_own[:, None]
    parity = jnp.where((degree[None, :] + wave_own[:, None]) % 2 == 0, 1.0, -1.0).astype(
        jnp.float32
    )
    masked = jnp.where(inside[:, :, None], spectral, jnp.zeros_like(spectral))
    flipped = jnp.where(parity[:, :, None] > 0, masked, -masked)
    wave_table = lon_table(wave_all)
    j_ids = my_index * half_local + jnp.arange(half_local, dtype=jnp.int32)
    weight_north = lat_weights_of(j_ids, lat_total)
    weight_south = lat_weights_of(lat_total - 1 - j_ids, lat_total)
    j_all = jnp.arange(half_lat, dtype=jnp.int32)
    weight_all = lat_weights_of(jnp.arange(lat_total, dtype=jnp.int32), lat_total)
    real_coef = jnp.where(wave_own == 0, float(NLON), NLON / 2.0)
    imag_coef = jnp.where(wave_own == 0, 0.0, NLON / 2.0)

    def hemisphere(values, lat_weight):
        fourier = jnp.einsum(
            "rnj,rnc->jrc", lat_basis, values, preferred_element_type=jnp.float32
        ).astype(jnp.bfloat16)
        wide = fourier.astype(jnp.float32)
        per_lat = jnp.sum(
            real_coef[None, :, None] * wide[:, :, :chan_count] ** 2
            + imag_coef[None, :, None] * wide[:, :, chan_count:] ** 2,
            axis=1,
        )
        part = jnp.sum(lat_weight[:, None] * per_lat, axis=0)
        return fourier.reshape(devices, half_local, row_count, chan_width), part

    out_north, part_north = hemisphere(masked, lat_weights_of(j_all, lat_total))
    north_in = lax.all_to_all(out_north, "lat", split_axis=0, concat_axis=0, tiled=True)
    out_south, part_south = hemisphere(flipped, lat_weights_of(lat_total - 1 - j_all, lat_total))
    partial_value, north_in = lax.optimization_barrier((part_north + part_south, north_in))
    gathered = lax.all_to_all(
        jnp.broadcast_to(partial_value[None], (devices, chan_count)), "lat", 0, 0, tiled=True
    )
    global_sum = jnp.sum(gathered, axis=0)
    variance = global_sum / (NLON * jnp.sum(weight_all))
    col_scale = col_gain * lax.rsqrt(variance + 1e-05)

    def round_trip(rows_in, lat_weight):
        weighted_local = column_network(
            lat_weight, rows_in, col_scale, in_weight, in_bias, out_weight, wave_table
        )
        returning = weighted_local.reshape(half_local, devices, row_count, chan_width)
        back = lax.all_to_all(returning, "lat", split_axis=1, concat_axis=1, tiled=True)
        return back.transpose(2, 1, 0, 3).reshape(row_count, half_lat, chan_width)

    out_south, wave_table, col_scale, north_in = lax.optimization_barrier(
        (out_south, wave_table, col_scale, north_in)
    )
    north = round_trip(north_in, weight_north)
    south_in = lax.all_to_all(out_south, "lat", split_axis=0, concat_axis=0, tiled=True)
    south = round_trip(south_in, weight_south)
    factor = 2.0 * math.sqrt(degrees * wave_total / lat_total)
    damp_all = jnp.concatenate([damping, damping])
    return inverse_legendre(wave_own, lat_basis, north, south, spectral, damp_all, factor)


def solution(mesh):
    in_specs = (
        P(("member", "lat"), None, None),
        P("lat", None, None),
        P(),
        P(),
        P(),
        P(),
        P(),
        P(),
    )
    out_specs = P(("member", "lat"), None, None)
    return jax.shard_map(
        on_device, mesh=mesh, in_specs=in_specs, out_specs=out_specs, check_vma=False
    )
```

```python
import functools
import math

import jax
import jax.numpy as jnp
from jax import lax
from jax.experimental import pallas as pl
from jax.experimental.pallas import tpu as pltpu
from jax.sharding import PartitionSpec as P

NN = 512
NLON = 1536
MB = 4
LON_TILE = 512


def wavenumbers(block_order, slot_count):
    slot_ids = jnp.arange(slot_count, dtype=jnp.int32)
    blocks = block_order.shape[0]
    matches = (slot_ids // MB)[:, None] == jnp.arange(blocks, dtype=jnp.int32)[None, :]
    chosen = jnp.sum(jnp.where(matches, block_order[None, :], 0), axis=1)
    return chosen * MB + slot_ids % MB


def lon_table(wave_all):
    longitude = jnp.arange(NLON, dtype=jnp.int32)
    phase_index = wave_all[:, None] * longitude[None, :] % NLON
    angles = phase_index.astype(jnp.float32) * (2.0 * math.pi / NLON)
    return jnp.concatenate([jnp.cos(angles), jnp.sin(angles)], axis=0).astype(jnp.bfloat16)


def lat_weights_of(latitude_index, lat_total):
    latitude = latitude_index.astype(jnp.float32)
    return jnp.cos(math.pi * ((latitude + 0.5) / lat_total - 0.5))


def column_kernel(
    weight_ref, rows_ref, scale_ref, in_w_ref, bias_ref, out_w_ref,
    table_ref, o_ref,
):
    j = pl.program_id(0)
    sources, _, rows_per, width = rows_ref.shape
    chan = width // 2
    waves = table_ref.shape[0] // 2
    rows = rows_ref[:, 0].astype(jnp.float32).reshape(sources * rows_per, width)
    rows = rows.astype(jnp.bfloat16)
    real = rows[:, :chan]
    imag = rows[:, chan:]
    scale = scale_ref[...]
    acc = jnp.zeros((2 * waves, chan), jnp.float32)
    for c in range(NLON // LON_TILE):
        lo = c * LON_TILE
        first_dims = (((0,), (0,)), ((), ()))
        wide = lax.dot_general(
            table_ref[:waves, lo:lo + LON_TILE], real, first_dims,
            preferred_element_type=jnp.float32,
        )
        wide = wide - lax.dot_general(
            table_ref[waves:, lo:lo + LON_TILE], imag, first_dims,
            preferred_element_type=jnp.float32,
        )
        g = wide.astype(jnp.bfloat16).astype(jnp.float32)
        normed = (g * scale).astype(jnp.bfloat16)
        pre = jnp.dot(normed, in_w_ref[...], preferred_element_type=jnp.float32) + bias_ref[...]
        hidden = jax.nn.gelu(pre).astype(jnp.bfloat16)
        col = jnp.dot(hidden, out_w_ref[...], preferred_element_type=jnp.float32).astype(
            jnp.bfloat16
        )
        acc = acc + jnp.dot(
            table_ref[:, lo:lo + LON_TILE], col, preferred_element_type=jnp.float32
        )
    inv_root = 1.0 / math.sqrt(NLON)
    w = weight_ref[j]
    cos_part = (acc[:waves] * inv_root).astype(jnp.bfloat16).astype(jnp.float32)
    sin_part = ((-acc[waves:]) * inv_root).astype(jnp.bfloat16).astype(jnp.float32)
    o_ref[0, :, :chan] = (w * cos_part).astype(jnp.bfloat16)
    o_ref[0, :, chan:] = (w * sin_part).astype(jnp.bfloat16)


def column_network(
    lat_w, rows_in, col_scale, in_weight, in_bias, out_weight, wave_table
):
    sources, _, rows_per, width = rows_in.shape
    lat_local = lat_w.shape[0]
    chan = width // 2
    waves = sources * rows_per
    nlon = wave_table.shape[1]
    hid = in_weight.shape[1]
    two_waves = wave_table.shape[0]
    full = lambda shape: pl.BlockSpec(shape, lambda j: (0,) * len(shape))
    return pl.pallas_call(
        column_kernel,
        grid=(lat_local,),
        in_specs=[
            pl.BlockSpec(memory_space=pltpu.SMEM),
            pl.BlockSpec((sources, 1, rows_per, width), lambda j: (0, j, 0, 0)),
            full((1, chan)),
            full((chan, hid)),
            full((1, hid)),
            full((hid, chan)),
            full((two_waves, nlon)),
        ],
        out_specs=pl.BlockSpec((1, two_waves // 2, 2 * chan), lambda j: (j, 0, 0)),
        out_shape=jax.ShapeDtypeStruct((lat_local, two_waves // 2, 2 * chan), jnp.bfloat16),
        compiler_params=pltpu.CompilerParams(vmem_limit_bytes=48 * 1024 * 1024),
        cost_estimate=pl.CostEstimate(
            flops=2 * lat_local * nlon * (2 * hid * chan + two_waves * chan + waves * width),
            transcendentals=lat_local * nlon * hid,
            bytes_accessed=2 * two_waves * nlon + lat_local * (waves * width * 2 + two_waves * chan * 2),
        ),
    )(
        lat_w,
        rows_in,
        col_scale[None, :],
        in_weight,
        in_bias[None, :],
        out_weight,
        wave_table,
    )


def inverse_kernel(wave_ref, basis_ref, north_ref, south_ref, spec_ref, damp_ref, o_ref, *, factor):
    block = basis_ref.shape[0]
    degrees = basis_ref.shape[1]
    n = lax.broadcasted_iota(jnp.int32, (degrees, 1), 0)
    wave_factor = (n * (n + 1)).astype(jnp.float32) / (NN * NN)
    for b in range(block):
        m = wave_ref[pl.program_id(0) * block + b]
        basis = basis_ref[b]
        east = jnp.dot(basis, north_ref[b], preferred_element_type=jnp.float32)
        west = jnp.dot(basis, south_ref[b], preferred_element_type=jnp.float32)
        parity = jnp.where((n + m) % 2 == 0, 1.0, -1.0).astype(jnp.float32)
        legendre = factor * (east + parity * west)
        damped = legendre - damp_ref[...] * wave_factor * spec_ref[b].astype(jnp.float32)
        o_ref[b] = jnp.where(n >= m, damped, 0.0)


def inverse_legendre(wave_own, lat_basis, north, south, spectral, damp_all, factor):
    rows, degrees, half_lat = lat_basis.shape
    width = spectral.shape[2]
    block = 8 if rows % 8 == 0 else 1
    three = lambda shape: pl.BlockSpec(shape, lambda r: (r, 0, 0))
    return pl.pallas_call(
        functools.partial(inverse_kernel, factor=factor),
        grid=(rows // block,),
        in_specs=[
            pl.BlockSpec(memory_space=pltpu.SMEM),
            three((block, degrees, half_lat)),
            three((block, half_lat, width)),
            three((block, half_lat, width)),
            three((block, degrees, width)),
            pl.BlockSpec((1, width), lambda r: (0, 0)),
        ],
        out_specs=three((block, degrees, width)),
        out_shape=jax.ShapeDtypeStruct((rows, degrees, width), jnp.float32),
        cost_estimate=pl.CostEstimate(
            flops=4 * rows * degrees * half_lat * width,
            transcendentals=0,
            bytes_accessed=rows * (degrees * half_lat * 2 + half_lat * width * 4 + degrees * width * 6),
        ),
    )(wave_own, lat_basis, north, south, spectral, damp_all[None, :])


def on_device(spectral, lat_basis, block_order, in_weight, in_bias, out_weight, col_gain, damping):
    devices = lax.axis_size("lat")
    my_index = lax.axis_index("lat")
    row_count = spectral.shape[0]
    degrees = spectral.shape[1]
    chan_width = spectral.shape[2]
    chan_count = chan_width // 2
    half_lat = lat_basis.shape[2]
    lat_total = 2 * half_lat
    half_local = half_lat // devices
    wave_total = row_count * devices
    wave_all = wavenumbers(block_order, wave_total)
    wave_own = lax.dynamic_slice_in_dim(wave_all, my_index * row_count, row_count)
    degree = jnp.arange(degrees, dtype=jnp.int32)
    inside = degree[None, :] >= wave_own[:, None]
    parity = jnp.where((degree[None, :] + wave_own[:, None]) % 2 == 0, 1.0, -1.0).astype(
        jnp.float32
    )
    masked = jnp.where(inside[:, :, None], spectral, jnp.zeros_like(spectral))
    flipped = jnp.where(parity[:, :, None] > 0, masked, -masked)
    wave_table = lon_table(wave_all)
    j_ids = my_index * half_local + jnp.arange(half_local, dtype=jnp.int32)
    weight_north = lat_weights_of(j_ids, lat_total)
    weight_south = lat_weights_of(lat_total - 1 - j_ids, lat_total)
    j_all = jnp.arange(half_lat, dtype=jnp.int32)
    weight_all = lat_weights_of(jnp.arange(lat_total, dtype=jnp.int32), lat_total)
    real_coef = jnp.where(wave_own == 0, float(NLON), NLON / 2.0)
    imag_coef = jnp.where(wave_own == 0, 0.0, NLON / 2.0)

    def squares(fourier, lat_weight):
        wide = fourier.astype(jnp.float32)
        per_lat = jnp.sum(
            real_coef[None, :, None] * wide[:, :, :chan_count] ** 2
            + imag_coef[None, :, None] * wide[:, :, chan_count:] ** 2,
            axis=1,
        )
        return jnp.sum(lat_weight[:, None] * per_lat, axis=0)

    both = jnp.stack([masked, flipped], axis=0)
    fourier = jnp.einsum(
        "rnj,srnc->sjrc", lat_basis, both, preferred_element_type=jnp.float32
    ).astype(jnp.bfloat16)
    part_north = squares(fourier[0], lat_weights_of(j_all, lat_total))
    part_south = squares(fourier[1], lat_weights_of(lat_total - 1 - j_all, lat_total))
    out_north = fourier[0].reshape(devices, half_local, row_count, chan_width)
    out_south = fourier[1].reshape(devices, half_local, row_count, chan_width)
    partial_value = part_north + part_south
    hi = partial_value.astype(jnp.bfloat16)
    rest = partial_value - hi.astype(jnp.float32)
    mid = rest.astype(jnp.bfloat16)
    lo = (rest - mid.astype(jnp.float32)).astype(jnp.bfloat16)
    pieces = jnp.concatenate(
        [
            jnp.concatenate([hi, mid])[None],
            jnp.concatenate([lo, jnp.zeros_like(lo)])[None],
            jnp.zeros((row_count - 2, chan_width), jnp.bfloat16),
        ]
    )
    slot = jnp.broadcast_to(pieces[None, None], (devices, 1, row_count, chan_width))
    north_in = lax.all_to_all(
        jnp.concatenate([out_north, slot], axis=1), "lat", split_axis=0, concat_axis=0, tiled=True
    )
    got = north_in[:, half_local, :2].astype(jnp.float32)
    global_sum = jnp.sum(got[:, 0, :chan_count] + got[:, 0, chan_count:] + got[:, 1, :chan_count], axis=0)
    variance = global_sum / (NLON * jnp.sum(weight_all))
    col_scale = col_gain * lax.rsqrt(variance + 1e-05)

    def round_trip(rows_in, lat_weight):
        weighted_local = column_network(
            lat_weight, rows_in, col_scale, in_weight, in_bias, out_weight, wave_table
        )
        returning = weighted_local.reshape(half_local, devices, row_count, chan_width)
        back = lax.all_to_all(returning, "lat", split_axis=1, concat_axis=1, tiled=True)
        return back.transpose(2, 1, 0, 3).reshape(row_count, half_lat, chan_width)

    out_south, wave_table, col_scale, north_in = lax.optimization_barrier(
        (out_south, wave_table, col_scale, north_in)
    )
    north = round_trip(north_in, weight_north)
    south_in = lax.all_to_all(out_south, "lat", split_axis=0, concat_axis=0, tiled=True)
    south = round_trip(south_in, weight_south)
    factor = 2.0 * math.sqrt(degrees * wave_total / lat_total)
    damp_all = jnp.concatenate([damping, damping])
    return inverse_legendre(wave_own, lat_basis, north, south, spectral, damp_all, factor)


def solution(mesh):
    in_specs = (
        P(("member", "lat"), None, None),
        P("lat", None, None),
        P(),
        P(),
        P(),
        P(),
        P(),
        P(),
    )
    out_specs = P(("member", "lat"), None, None)
    return jax.shard_map(
        on_device, mesh=mesh, in_specs=in_specs, out_specs=out_specs, check_vma=False
    )
```

```python
import functools
import math

import jax
import jax.numpy as jnp
from jax import lax
from jax.experimental import pallas as pl
from jax.experimental.pallas import tpu as pltpu
from jax.sharding import PartitionSpec as P

NN = 512
NLON = 1536
MB = 4
LON_TILE = 512


def wavenumbers(block_order, slot_count):
    slot_ids = jnp.arange(slot_count, dtype=jnp.int32)
    blocks = block_order.shape[0]
    matches = (slot_ids // MB)[:, None] == jnp.arange(blocks, dtype=jnp.int32)[None, :]
    chosen = jnp.sum(jnp.where(matches, block_order[None, :], 0), axis=1)
    return chosen * MB + slot_ids % MB


def lon_table(wave_all):
    longitude = jnp.arange(NLON, dtype=jnp.int32)
    phase_index = wave_all[:, None] * longitude[None, :] % NLON
    angles = phase_index.astype(jnp.float32) * (2.0 * math.pi / NLON)
    return jnp.concatenate([jnp.cos(angles), jnp.sin(angles)], axis=0).astype(jnp.bfloat16)


def lat_weights_of(latitude_index, lat_total):
    latitude = latitude_index.astype(jnp.float32)
    return jnp.cos(math.pi * ((latitude + 0.5) / lat_total - 0.5))


def column_kernel(
    weight_ref, rows_ref, scale_ref, in_w_ref, bias_ref, out_w_ref,
    table_ref, o_ref,
):
    j = pl.program_id(0)
    sources, _, rows_per, width = rows_ref.shape
    chan = width // 2
    waves = table_ref.shape[0] // 2
    rows = rows_ref[:, 0].astype(jnp.float32).reshape(sources * rows_per, width)
    rows = rows.astype(jnp.bfloat16)
    real = rows[:, :chan]
    imag = rows[:, chan:]
    scale = scale_ref[...]
    acc = jnp.zeros((2 * waves, chan), jnp.float32)
    for c in range(NLON // LON_TILE):
        lo = c * LON_TILE
        first_dims = (((0,), (0,)), ((), ()))
        wide = lax.dot_general(
            table_ref[:waves, lo:lo + LON_TILE], real, first_dims,
            preferred_element_type=jnp.float32,
        )
        wide = wide - lax.dot_general(
            table_ref[waves:, lo:lo + LON_TILE], imag, first_dims,
            preferred_element_type=jnp.float32,
        )
        g = wide.astype(jnp.bfloat16).astype(jnp.float32)
        normed = (g * scale).astype(jnp.bfloat16)
        pre = jnp.dot(normed, in_w_ref[...], preferred_element_type=jnp.float32) + bias_ref[...]
        hidden = jax.nn.gelu(pre).astype(jnp.bfloat16)
        col = jnp.dot(hidden, out_w_ref[...], preferred_element_type=jnp.float32).astype(
            jnp.bfloat16
        )
        acc = acc + jnp.dot(
            table_ref[:, lo:lo + LON_TILE], col, preferred_element_type=jnp.float32
        )
    inv_root = 1.0 / math.sqrt(NLON)
    w = weight_ref[j]
    cos_part = (acc[:waves] * inv_root).astype(jnp.bfloat16).astype(jnp.float32)
    sin_part = ((-acc[waves:]) * inv_root).astype(jnp.bfloat16).astype(jnp.float32)
    o_ref[0, :, :chan] = (w * cos_part).astype(jnp.bfloat16)
    o_ref[0, :, chan:] = (w * sin_part).astype(jnp.bfloat16)


def column_network(
    lat_w, rows_in, col_scale, in_weight, in_bias, out_weight, wave_table
):
    sources, _, rows_per, width = rows_in.shape
    lat_local = lat_w.shape[0]
    chan = width // 2
    waves = sources * rows_per
    nlon = wave_table.shape[1]
    hid = in_weight.shape[1]
    two_waves = wave_table.shape[0]
    full = lambda shape: pl.BlockSpec(shape, lambda j: (0,) * len(shape))
    return pl.pallas_call(
        column_kernel,
        grid=(lat_local,),
        in_specs=[
            pl.BlockSpec(memory_space=pltpu.SMEM),
            pl.BlockSpec((sources, 1, rows_per, width), lambda j: (0, j, 0, 0)),
            full((1, chan)),
            full((chan, hid)),
            full((1, hid)),
            full((hid, chan)),
            full((two_waves, nlon)),
        ],
        out_specs=pl.BlockSpec((1, two_waves // 2, 2 * chan), lambda j: (j, 0, 0)),
        out_shape=jax.ShapeDtypeStruct((lat_local, two_waves // 2, 2 * chan), jnp.bfloat16),
        compiler_params=pltpu.CompilerParams(vmem_limit_bytes=48 * 1024 * 1024),
        cost_estimate=pl.CostEstimate(
            flops=2 * lat_local * nlon * (2 * hid * chan + two_waves * chan + waves * width),
            transcendentals=lat_local * nlon * hid,
            bytes_accessed=2 * two_waves * nlon + lat_local * (waves * width * 2 + two_waves * chan * 2),
        ),
    )(
        lat_w,
        rows_in,
        col_scale[None, :],
        in_weight,
        in_bias[None, :],
        out_weight,
        wave_table,
    )


def inverse_kernel(wave_ref, basis_ref, north_ref, south_ref, spec_ref, damp_ref, o_ref, *, factor):
    block, degrees, half_lat = basis_ref.shape
    width = spec_ref.shape[2]
    n = lax.broadcasted_iota(jnp.int32, (degrees, 1), 0)
    wave_factor = (n * (n + 1)).astype(jnp.float32) / (NN * NN)
    north_all = north_ref[...].astype(jnp.float32)
    south_all = south_ref[...].astype(jnp.float32)
    for b in range(block):
        m = wave_ref[pl.program_id(0) * block + b]
        basis = basis_ref[b]
        north = north_all[:, :, b, :].reshape(half_lat, width).astype(jnp.bfloat16)
        south = south_all[:, :, b, :].reshape(half_lat, width).astype(jnp.bfloat16)
        east = jnp.dot(basis, north, preferred_element_type=jnp.float32)
        west = jnp.dot(basis, south, preferred_element_type=jnp.float32)
        parity = jnp.where((n + m) % 2 == 0, 1.0, -1.0).astype(jnp.float32)
        legendre = factor * (east + parity * west)
        damped = legendre - damp_ref[...] * wave_factor * spec_ref[b].astype(jnp.float32)
        o_ref[b] = jnp.where(n >= m, damped, 0.0)


def inverse_legendre(wave_own, lat_basis, north, south, spectral, damp_all, factor):
    rows, degrees, half_lat = lat_basis.shape
    width = spectral.shape[2]
    block = 8 if rows % 8 == 0 else 1
    three = lambda shape: pl.BlockSpec(shape, lambda r: (r, 0, 0))
    return pl.pallas_call(
        functools.partial(inverse_kernel, factor=factor),
        grid=(rows // block,),
        in_specs=[
            pl.BlockSpec(memory_space=pltpu.SMEM),
            three((block, degrees, half_lat)),
            pl.BlockSpec(north.shape[:2] + (block, width), lambda r: (0, 0, r, 0)),
            pl.BlockSpec(south.shape[:2] + (block, width), lambda r: (0, 0, r, 0)),
            three((block, degrees, width)),
            pl.BlockSpec((1, width), lambda r: (0, 0)),
        ],
        out_specs=three((block, degrees, width)),
        out_shape=jax.ShapeDtypeStruct((rows, degrees, width), jnp.float32),
        cost_estimate=pl.CostEstimate(
            flops=4 * rows * degrees * half_lat * width,
            transcendentals=0,
            bytes_accessed=rows * (degrees * half_lat * 2 + half_lat * width * 4 + degrees * width * 6),
        ),
    )(wave_own, lat_basis, north, south, spectral, damp_all[None, :])


def on_device(spectral, lat_basis, block_order, in_weight, in_bias, out_weight, col_gain, damping):
    devices = lax.axis_size("lat")
    my_index = lax.axis_index("lat")
    row_count = spectral.shape[0]
    degrees = spectral.shape[1]
    chan_width = spectral.shape[2]
    chan_count = chan_width // 2
    half_lat = lat_basis.shape[2]
    lat_total = 2 * half_lat
    half_local = half_lat // devices
    wave_total = row_count * devices
    wave_all = wavenumbers(block_order, wave_total)
    wave_own = lax.dynamic_slice_in_dim(wave_all, my_index * row_count, row_count)
    degree = jnp.arange(degrees, dtype=jnp.int32)
    inside = degree[None, :] >= wave_own[:, None]
    parity = jnp.where((degree[None, :] + wave_own[:, None]) % 2 == 0, 1.0, -1.0).astype(
        jnp.float32
    )
    masked = jnp.where(inside[:, :, None], spectral, jnp.zeros_like(spectral))
    flipped = jnp.where(parity[:, :, None] > 0, masked, -masked)
    wave_table = lon_table(wave_all)
    j_ids = my_index * half_local + jnp.arange(half_local, dtype=jnp.int32)
    weight_north = lat_weights_of(j_ids, lat_total)
    weight_south = lat_weights_of(lat_total - 1 - j_ids, lat_total)
    j_all = jnp.arange(half_lat, dtype=jnp.int32)
    weight_all = lat_weights_of(jnp.arange(lat_total, dtype=jnp.int32), lat_total)
    real_coef = jnp.where(wave_own == 0, float(NLON), NLON / 2.0)
    imag_coef = jnp.where(wave_own == 0, 0.0, NLON / 2.0)

    def squares(fourier, lat_weight):
        wide = fourier.astype(jnp.float32)
        per_lat = jnp.sum(
            real_coef[None, :, None] * wide[:, :, :chan_count] ** 2
            + imag_coef[None, :, None] * wide[:, :, chan_count:] ** 2,
            axis=1,
        )
        return jnp.sum(lat_weight[:, None] * per_lat, axis=0)

    both = jnp.stack([masked, flipped], axis=0)
    fourier = jnp.einsum(
        "rnj,srnc->sjrc", lat_basis, both, preferred_element_type=jnp.float32
    ).astype(jnp.bfloat16)
    part_north = squares(fourier[0], lat_weights_of(j_all, lat_total))
    part_south = squares(fourier[1], lat_weights_of(lat_total - 1 - j_all, lat_total))
    out_north = fourier[0].reshape(devices, half_local, row_count, chan_width)
    out_south = fourier[1].reshape(devices, half_local, row_count, chan_width)
    partial_value = part_north + part_south
    hi = partial_value.astype(jnp.bfloat16)
    rest = partial_value - hi.astype(jnp.float32)
    mid = rest.astype(jnp.bfloat16)
    lo = (rest - mid.astype(jnp.float32)).astype(jnp.bfloat16)
    pieces = jnp.concatenate(
        [
            jnp.concatenate([hi, mid])[None],
            jnp.concatenate([lo, jnp.zeros_like(lo)])[None],
            jnp.zeros((row_count - 2, chan_width), jnp.bfloat16),
        ]
    )
    slot = jnp.broadcast_to(pieces[None, None], (devices, 1, row_count, chan_width))
    north_in = lax.all_to_all(
        jnp.concatenate([out_north, slot], axis=1), "lat", split_axis=0, concat_axis=0, tiled=True
    )
    got = north_in[:, half_local, :2].astype(jnp.float32)
    global_sum = jnp.sum(got[:, 0, :chan_count] + got[:, 0, chan_count:] + got[:, 1, :chan_count], axis=0)
    variance = global_sum / (NLON * jnp.sum(weight_all))
    col_scale = col_gain * lax.rsqrt(variance + 1e-05)

    def round_trip(rows_in, lat_weight):
        weighted_local = column_network(
            lat_weight, rows_in, col_scale, in_weight, in_bias, out_weight, wave_table
        )
        returning = weighted_local.reshape(half_local, devices, row_count, chan_width)
        back = lax.all_to_all(returning, "lat", split_axis=1, concat_axis=1, tiled=True)
        return back

    out_south, wave_table, col_scale, north_in = lax.optimization_barrier(
        (out_south, wave_table, col_scale, north_in)
    )
    north = round_trip(north_in, weight_north)
    south_in = lax.all_to_all(out_south, "lat", split_axis=0, concat_axis=0, tiled=True)
    south = round_trip(south_in, weight_south)
    factor = 2.0 * math.sqrt(degrees * wave_total / lat_total)
    damp_all = jnp.concatenate([damping, damping])
    basis_perm = lat_basis.reshape(row_count, degrees, devices, half_local).transpose(0, 1, 3, 2)
    basis_perm = basis_perm.reshape(row_count, degrees, half_lat)
    return inverse_legendre(wave_own, basis_perm, north, south, spectral, damp_all, factor)


def solution(mesh):
    in_specs = (
        P(("member", "lat"), None, None),
        P("lat", None, None),
        P(),
        P(),
        P(),
        P(),
        P(),
        P(),
    )
    out_specs = P(("member", "lat"), None, None)
    return jax.shard_map(
        on_device, mesh=mesh, in_specs=in_specs, out_specs=out_specs, check_vma=False
    )
```

```python
import functools
import math

import jax
import jax.numpy as jnp
from jax import lax
from jax.experimental import pallas as pl
from jax.experimental.pallas import tpu as pltpu
from jax.sharding import PartitionSpec as P

NN = 512
NLON = 1536
MB = 4
LON_TILE = 512


def wavenumbers(block_order, slot_count):
    slot_ids = jnp.arange(slot_count, dtype=jnp.int32)
    blocks = block_order.shape[0]
    if slot_count == blocks * MB:
        return jnp.repeat(block_order, MB) * MB + slot_ids % MB
    matches = (slot_ids // MB)[:, None] == jnp.arange(blocks, dtype=jnp.int32)[None, :]
    chosen = jnp.sum(jnp.where(matches, block_order[None, :], 0), axis=1)
    return chosen * MB + slot_ids % MB


def lon_table(wave_all):
    longitude = jnp.arange(NLON, dtype=jnp.int32)
    phase_index = wave_all[:, None] * longitude[None, :] % NLON
    angles = phase_index.astype(jnp.float32) * (2.0 * math.pi / NLON)
    return jnp.concatenate([jnp.cos(angles), jnp.sin(angles)], axis=0).astype(jnp.bfloat16)


def lat_weights_of(latitude_index, lat_total):
    latitude = latitude_index.astype(jnp.float32)
    return jnp.cos(math.pi * ((latitude + 0.5) / lat_total - 0.5))


def column_kernel(
    weight_ref, rows_ref, scale_ref, in_w_ref, bias_ref, out_w_ref,
    table_ref, o_ref,
):
    j = pl.program_id(0)
    sources, _, rows_per, width = rows_ref.shape
    chan = width // 2
    waves = table_ref.shape[0] // 2
    rows = rows_ref[:, 0].astype(jnp.float32).reshape(sources * rows_per, width)
    rows = rows.astype(jnp.bfloat16)
    real = rows[:, :chan]
    imag = rows[:, chan:]
    scale = scale_ref[...]
    acc = jnp.zeros((2 * waves, chan), jnp.float32)
    for c in range(NLON // LON_TILE):
        lo = c * LON_TILE
        first_dims = (((0,), (0,)), ((), ()))
        wide = lax.dot_general(
            table_ref[:waves, lo:lo + LON_TILE], real, first_dims,
            preferred_element_type=jnp.float32,
        )
        wide = wide - lax.dot_general(
            table_ref[waves:, lo:lo + LON_TILE], imag, first_dims,
            preferred_element_type=jnp.float32,
        )
        g = wide.astype(jnp.bfloat16).astype(jnp.float32)
        normed = (g * scale).astype(jnp.bfloat16)
        pre = jnp.dot(normed, in_w_ref[...], preferred_element_type=jnp.float32) + bias_ref[...]
        hidden = jax.nn.gelu(pre).astype(jnp.bfloat16)
        col = jnp.dot(hidden, out_w_ref[...], preferred_element_type=jnp.float32).astype(
            jnp.bfloat16
        )
        acc = acc + jnp.dot(
            table_ref[:, lo:lo + LON_TILE], col, preferred_element_type=jnp.float32
        )
    inv_root = 1.0 / math.sqrt(NLON)
    w = weight_ref[j]
    cos_part = (acc[:waves] * inv_root).astype(jnp.bfloat16).astype(jnp.float32)
    sin_part = ((-acc[waves:]) * inv_root).astype(jnp.bfloat16).astype(jnp.float32)
    o_ref[0, :, :chan] = (w * cos_part).astype(jnp.bfloat16)
    o_ref[0, :, chan:] = (w * sin_part).astype(jnp.bfloat16)


def column_network(
    lat_w, rows_in, col_scale, in_weight, in_bias, out_weight, wave_table
):
    sources, _, rows_per, width = rows_in.shape
    lat_local = lat_w.shape[0]
    chan = width // 2
    waves = sources * rows_per
    nlon = wave_table.shape[1]
    hid = in_weight.shape[1]
    two_waves = wave_table.shape[0]
    full = lambda shape: pl.BlockSpec(shape, lambda j: (0,) * len(shape))
    return pl.pallas_call(
        column_kernel,
        grid=(lat_local,),
        in_specs=[
            pl.BlockSpec(memory_space=pltpu.SMEM),
            pl.BlockSpec((sources, 1, rows_per, width), lambda j: (0, j, 0, 0)),
            full((1, chan)),
            full((chan, hid)),
            full((1, hid)),
            full((hid, chan)),
            full((two_waves, nlon)),
        ],
        out_specs=pl.BlockSpec((1, two_waves // 2, 2 * chan), lambda j: (j, 0, 0)),
        out_shape=jax.ShapeDtypeStruct((lat_local, two_waves // 2, 2 * chan), jnp.bfloat16),
        compiler_params=pltpu.CompilerParams(vmem_limit_bytes=48 * 1024 * 1024),
        cost_estimate=pl.CostEstimate(
            flops=2 * lat_local * nlon * (2 * hid * chan + two_waves * chan + waves * width),
            transcendentals=lat_local * nlon * hid,
            bytes_accessed=2 * two_waves * nlon + lat_local * (waves * width * 2 + two_waves * chan * 2),
        ),
    )(
        lat_w,
        rows_in,
        col_scale[None, :],
        in_weight,
        in_bias[None, :],
        out_weight,
        wave_table,
    )


def inverse_kernel(wave_ref, basis_ref, north_ref, south_ref, spec_ref, damp_ref, o_ref, *, factor):
    block = basis_ref.shape[0]
    degrees = basis_ref.shape[1]
    n = lax.broadcasted_iota(jnp.int32, (degrees, 1), 0)
    wave_factor = (n * (n + 1)).astype(jnp.float32) / (NN * NN)
    for b in range(block):
        m = wave_ref[pl.program_id(0) * block + b]
        basis = basis_ref[b]
        east = jnp.dot(basis, north_ref[b], preferred_element_type=jnp.float32)
        west = jnp.dot(basis, south_ref[b], preferred_element_type=jnp.float32)
        parity = jnp.where((n + m) % 2 == 0, 1.0, -1.0).astype(jnp.float32)
        legendre = factor * (east + parity * west)
        damped = legendre - damp_ref[...] * wave_factor * spec_ref[b].astype(jnp.float32)
        o_ref[b] = jnp.where(n >= m, damped, 0.0)


def inverse_legendre(wave_own, lat_basis, north, south, spectral, damp_all, factor):
    rows, degrees, half_lat = lat_basis.shape
    width = spectral.shape[2]
    block = 8 if rows % 8 == 0 else 1
    three = lambda shape: pl.BlockSpec(shape, lambda r: (r, 0, 0))
    return pl.pallas_call(
        functools.partial(inverse_kernel, factor=factor),
        grid=(rows // block,),
        in_specs=[
            pl.BlockSpec(memory_space=pltpu.SMEM),
            three((block, degrees, half_lat)),
            three((block, half_lat, width)),
            three((block, half_lat, width)),
            three((block, degrees, width)),
            pl.BlockSpec((1, width), lambda r: (0, 0)),
        ],
        out_specs=three((block, degrees, width)),
        out_shape=jax.ShapeDtypeStruct((rows, degrees, width), jnp.float32),
        cost_estimate=pl.CostEstimate(
            flops=4 * rows * degrees * half_lat * width,
            transcendentals=0,
            bytes_accessed=rows * (degrees * half_lat * 2 + half_lat * width * 4 + degrees * width * 6),
        ),
    )(wave_own, lat_basis, north, south, spectral, damp_all[None, :])


def on_device(spectral, lat_basis, block_order, in_weight, in_bias, out_weight, col_gain, damping):
    devices = lax.axis_size("lat")
    my_index = lax.axis_index("lat")
    row_count = spectral.shape[0]
    degrees = spectral.shape[1]
    chan_width = spectral.shape[2]
    chan_count = chan_width // 2
    half_lat = lat_basis.shape[2]
    lat_total = 2 * half_lat
    half_local = half_lat // devices
    wave_total = row_count * devices
    wave_all = wavenumbers(block_order, wave_total)
    wave_own = lax.dynamic_slice_in_dim(wave_all, my_index * row_count, row_count)
    degree = jnp.arange(degrees, dtype=jnp.int32)
    inside = degree[None, :] >= wave_own[:, None]
    parity = jnp.where((degree[None, :] + wave_own[:, None]) % 2 == 0, 1.0, -1.0).astype(
        jnp.float32
    )
    masked = jnp.where(inside[:, :, None], spectral, jnp.zeros_like(spectral))
    flipped = jnp.where(parity[:, :, None] > 0, masked, -masked)
    wave_table = lon_table(wave_all)
    j_ids = my_index * half_local + jnp.arange(half_local, dtype=jnp.int32)
    weight_north = lat_weights_of(j_ids, lat_total)
    weight_south = lat_weights_of(lat_total - 1 - j_ids, lat_total)
    j_all = jnp.arange(half_lat, dtype=jnp.int32)
    weight_all = lat_weights_of(jnp.arange(lat_total, dtype=jnp.int32), lat_total)
    real_coef = jnp.where(wave_own == 0, float(NLON), NLON / 2.0)
    imag_coef = jnp.where(wave_own == 0, 0.0, NLON / 2.0)

    def squares(fourier, lat_weight):
        wide = fourier.astype(jnp.float32)
        per_lat = jnp.sum(
            real_coef[None, :, None] * wide[:, :, :chan_count] ** 2
            + imag_coef[None, :, None] * wide[:, :, chan_count:] ** 2,
            axis=1,
        )
        return jnp.sum(lat_weight[:, None] * per_lat, axis=0)

    both = jnp.stack([masked, flipped], axis=0)
    fourier = jnp.einsum(
        "rnj,srnc->sjrc", lat_basis, both, preferred_element_type=jnp.float32
    ).astype(jnp.bfloat16)
    part_north = squares(fourier[0], lat_weights_of(j_all, lat_total))
    part_south = squares(fourier[1], lat_weights_of(lat_total - 1 - j_all, lat_total))
    out_north = fourier[0].reshape(devices, half_local, row_count, chan_width)
    out_south = fourier[1].reshape(devices, half_local, row_count, chan_width)
    partial_value = part_north + part_south
    hi = partial_value.astype(jnp.bfloat16)
    rest = partial_value - hi.astype(jnp.float32)
    mid = rest.astype(jnp.bfloat16)
    lo = (rest - mid.astype(jnp.float32)).astype(jnp.bfloat16)
    pieces = jnp.concatenate(
        [
            jnp.concatenate([hi, mid])[None],
            jnp.concatenate([lo, jnp.zeros_like(lo)])[None],
            jnp.zeros((row_count - 2, chan_width), jnp.bfloat16),
        ]
    )
    slot = jnp.broadcast_to(pieces[None, None], (devices, 1, row_count, chan_width))
    north_in = lax.all_to_all(
        jnp.concatenate([out_north, slot], axis=1), "lat", split_axis=0, concat_axis=0, tiled=True
    )
    got = north_in[:, half_local, :2].astype(jnp.float32)
    global_sum = jnp.sum(got[:, 0, :chan_count] + got[:, 0, chan_count:] + got[:, 1, :chan_count], axis=0)
    variance = global_sum / (NLON * jnp.sum(weight_all))
    col_scale = col_gain * lax.rsqrt(variance + 1e-05)

    def round_trip(rows_in, lat_weight):
        weighted_local = column_network(
            lat_weight, rows_in, col_scale, in_weight, in_bias, out_weight, wave_table
        )
        returning = weighted_local.reshape(half_local, devices, row_count, chan_width)
        back = lax.all_to_all(returning, "lat", split_axis=1, concat_axis=1, tiled=True)
        return back.transpose(2, 1, 0, 3).reshape(row_count, half_lat, chan_width)

    out_south, wave_table, col_scale, north_in = lax.optimization_barrier(
        (out_south, wave_table, col_scale, north_in)
    )
    north = round_trip(north_in, weight_north)
    south_in = lax.all_to_all(out_south, "lat", split_axis=0, concat_axis=0, tiled=True)
    south = round_trip(south_in, weight_south)
    factor = 2.0 * math.sqrt(degrees * wave_total / lat_total)
    damp_all = jnp.concatenate([damping, damping])
    return inverse_legendre(wave_own, lat_basis, north, south, spectral, damp_all, factor)


def solution(mesh):
    in_specs = (
        P(("member", "lat"), None, None),
        P("lat", None, None),
        P(),
        P(),
        P(),
        P(),
        P(),
        P(),
    )
    out_specs = P(("member", "lat"), None, None)
    return jax.shard_map(
        on_device, mesh=mesh, in_specs=in_specs, out_specs=out_specs, check_vma=False
    )
```
